32 devices in a mesh: section: 4 (over y, core), site: 8 (over z, x).
Axes of the slice: x: 2, y: 2, z: 4, core: 2. Of those that a mesh axis runs over, the one named last changes fastest.
Arguments:
- acts: bfloat16 [4, 8, 4096], P('section', 'site'), may hold values from -36 to 36
- patches: bfloat16 [4, 2048, 1024], P('section', 'site'), may hold values from -36 to 36
- site_tiles: int32 [8, 256], replicated, may hold values from 0 to 2047, as said below
- site_count: int32 [8], replicated, may hold values from 128 to 256, as said below
- q_weight: bfloat16 [4, 2048, 4096], P('section', 'site'), may hold values from -0.09375 to 0.09375
- q_gain: float32 [4, 128], P('section'), may hold values from 1 to 2.5
- k_gain: float32 [4, 128], P('section'), may hold values from 1 to 2.5
- tile_in: bfloat16 [4, 1024, 512], P('section', 'site'), may hold values from -0.1875 to 0.1875
- tile_out: bfloat16 [4, 512, 4096], P('section', 'site'), may hold values from -0.25 to 0.25
- out_weight: bfloat16 [4, 2048, 4096], P('section', 'site'), may hold values from -0.125 to 0.125
- ffn_gain: float32 [4, 4096], P('section'), may hold values from 0.25 to 1.75
- gate_weight: bfloat16 [4, 7168, 4096], P('section', 'site'), may hold values from -0.09375 to 0.09375
- up_weight: bfloat16 [4, 7168, 4096], P('section', 'site'), may hold values from -0.09375 to 0.09375
- down_weight: bfloat16 [4, 7168, 4096], P('section', 'site'), may hold values from -0.0625 to 0.0625
Outputs:
- passed: bfloat16 [4, 8, 4096], P('section', 'site')
The draws below stay inside these ranges and needn't reach their ends.
Inputs may be any that keep to these rules, and one draw needn't show every extreme that they name: `site_tiles`: shard k owns tiles k * 256 to (k + 1) * 256 - 1. Of the live entries (l < site_count[n]) of the one site held by a device, at most 40 name tiles of one shard, and in every device exactly 40 name tiles of some shard. All entries of one device's sites are different tiles. `site_count`: sites n with n % 1 == 0, except site 8 - 1, have all 256 entries live; site 8 - 1 has exactly 128.
All inputs are finite; a program needn't handle non-finite values.
Results may differ from the reference program's by a relative error of at most 0.0055.
Values may be sent and summed in bfloat16 or wider, within the bound.
No kernel may reach another device: no remote copies, remote signals or barrier semaphores. Data moves between devices by JAX's collectives and lax.ppermute only.
A program may use at most 128 MiB of HBM per device.

```python
import math
import jax
import jax.numpy as jnp
from jax import lax

D = 4096
HEADS = 16
HD = 128
FF = 7168
PF = 1024
TH = 512
LIST = 256
SITE_DEV = 1
INNER = 2048
TILE_DEV = 256
CAP = 40
NS = 8
NT = 2048
SECTIONS = 4
N_SECTION = 4


def scaled_field(key, leading, columns):
    first_key, row_key, column_key = jax.random.split(key, 3)
    shape = (SECTIONS, leading, columns)
    row_scale = jnp.exp(jax.random.uniform(row_key, (SECTIONS, leading, 1), jnp.float32, math.log(0.3), math.log(3.0)))
    column_scale = jnp.exp(jax.random.uniform(column_key, (SECTIONS, 1, columns), jnp.float32, math.log(0.3), math.log(3.0)))
    base = jnp.clip(jax.random.normal(first_key, shape, jnp.float32), -4.0, 4.0)
    return base * row_scale * column_scale


def draw_acts(key, part):
    return scaled_field(key, NS, D).astype(jnp.bfloat16)


def draw_patches(key, part):
    return scaled_field(key, NT, PF).astype(jnp.bfloat16)


def draw_site_tiles(key, part):
    device_count = NS // SITE_DEV
    pair_total = SITE_DEV * LIST
    half_list = LIST // 2
    rest_len = LIST - half_list
    guaranteed = jnp.arange(SITE_DEV * half_list, dtype=jnp.int32) // half_list * LIST + jnp.arange(SITE_DEV * half_list, dtype=jnp.int32) % half_list
    remainder = jnp.arange(SITE_DEV * rest_len, dtype=jnp.int32) // rest_len * LIST + half_list + jnp.arange(SITE_DEV * rest_len, dtype=jnp.int32) % rest_len

    def one_device(device_key):
        busy_key, grid_key, first_key, second_key, local_key = jax.random.split(device_key, 5)
        busy_owner = jax.random.randint(busy_key, (), 0, device_count, dtype=jnp.int32)
        grid_slots = jax.random.permutation(grid_key, (device_count - 1) * CAP)[:pair_total - CAP].astype(jnp.int32)
        other_owners = (busy_owner + 1 + grid_slots // CAP) % device_count
        owner_list = jnp.concatenate([jnp.full((CAP,), busy_owner, jnp.int32), other_owners])
        slot_order = jnp.concatenate([jax.random.permutation(first_key, guaranteed), jax.random.permutation(second_key, remainder)])
        owner_at = jnp.zeros((pair_total,), jnp.int32).at[slot_order].set(owner_list)
        local_ids = jax.random.permutation(local_key, TILE_DEV)[:pair_total].astype(jnp.int32)
        return (owner_at * TILE_DEV + local_ids).reshape(SITE_DEV, LIST)
    device_keys = jax.random.split(key, device_count)
    return jax.vmap(one_device)(device_keys).reshape(NS, LIST).astype(jnp.int32)


def draw_site_count(key, part):
    drawn = jax.random.randint(key, (NS,), LIST // 2, LIST + 1, dtype=jnp.int32)
    position = jnp.arange(NS, dtype=jnp.int32)
    counted = jnp.where(position % SITE_DEV == 0, LIST, drawn)
    return jnp.where(position == NS - 1, LIST // 2, counted).astype(jnp.int32)


def block_scale(rng, extent, cuts, smallest, high):
    level, own = 1.0, jax.random.fold_in(rng, 6)
    for dim, blocks in cuts:
        draws = jnp.exp(jax.random.uniform(jax.random.fold_in(own, dim), (blocks,), jnp.float32, smallest / len(cuts), high / len(cuts)))
        level = level * jnp.repeat(draws, extent[dim] // blocks).reshape([-1 if axis == dim else 1 for axis in range(len(extent))])
    return level


def scatter_about(rng, extent, width, bound, cuts=(), held_as=jnp.bfloat16):
    values = jax.random.normal(rng, extent, jnp.float32) * width
    if len(cuts) > 0:
        values = block_scale(rng, extent, cuts, -0.22, 0.18) * values
    return jnp.clip(values, min=-bound, max=bound).astype(held_as)


def setup_inputs(seed: int = 0) -> dict:
    splits = jax.random.split(jax.random.key(seed), 15)
    acts = draw_acts(jax.random.fold_in(splits[14], 71), 0)
    patches = draw_patches(jax.random.fold_in(splits[14], 71), 0)
    site_tiles = draw_site_tiles(jax.random.fold_in(splits[14], 71), 0)
    site_count = draw_site_count(jax.random.fold_in(splits[14], 71), 0)
    q_weight = scatter_about(splits[4], (SECTIONS, INNER, D), D ** -0.5, 0.09375, ((0, 4), (1, 8)))
    q_gain = jnp.clip(jnp.exp(math.log(2.5) - 0.916290732 * jax.random.uniform(splits[5], (SECTIONS, HD), jnp.float32) ** block_scale(splits[5], (SECTIONS, HD), ((0, 4),), -0.2, 0.2)), 1.0, 2.5)
    k_gain = jnp.clip(jnp.exp(math.log(2.5) - 0.916290732 * jax.random.uniform(splits[6], (SECTIONS, HD), jnp.float32) ** block_scale(splits[6], (SECTIONS, HD), ((0, 4),), -0.2, 0.2)), 1.0, 2.5)
    tile_in = scatter_about(splits[7], (SECTIONS, PF, TH), PF ** -0.5, 0.1875, ((0, 4), (1, 8)))
    tile_out = scatter_about(splits[8], (SECTIONS, TH, 2 * INNER), TH ** -0.5, 0.25, ((0, 4), (1, 8)))
    out_weight = scatter_about(splits[9], (SECTIONS, INNER, D), INNER ** -0.5, 0.125, ((0, 4), (1, 8)))
    ffn_gain = jnp.clip(1.0 + 0.15 * jax.random.normal(splits[10], (SECTIONS, D), jnp.float32), 0.25, 1.75)
    gate_weight = scatter_about(splits[11], (SECTIONS, FF, D), D ** -0.5, 0.09375, ((0, 4), (1, 8)))
    up_weight = scatter_about(splits[12], (SECTIONS, FF, D), D ** -0.5, 0.09375, ((0, 4), (1, 8)))
    down_weight = scatter_about(splits[13], (SECTIONS, FF, D), FF ** -0.5, 0.0625, ((0, 4), (1, 8)))
    return {"acts": acts, "patches": patches, "site_tiles": site_tiles, "site_count": site_count, "q_weight": q_weight, "q_gain": q_gain, "k_gain": k_gain, "tile_in": tile_in, "tile_out": tile_out, "out_weight": out_weight, "ffn_gain": ffn_gain, "gate_weight": gate_weight, "up_weight": up_weight, "down_weight": down_weight}


epsilon = 1e-05

def rounded(values):
    return lax.optimization_barrier(values.astype(jnp.bfloat16))

def by_rows(left, weight_rows):
    return lax.dot_general(left, weight_rows, (((1,), (1,)), ((), ())), preferred_element_type=jnp.float32)

def head_norm(values, gain_row):
    shaped = values.astype(jnp.float32).reshape(values.shape[0], -1, gain_row.shape[0])
    scaled = shaped * lax.rsqrt(lax.optimization_barrier(jnp.mean(shaped * shaped, axis=-1, keepdims=True)) + epsilon) * gain_row
    return scaled.reshape(values.shape[0], -1)

def rms_norm(values, gain_row):
    return values * lax.rsqrt(lax.optimization_barrier(jnp.mean(values * values, axis=-1, keepdims=True)) + epsilon) * gain_row

def encode(tile_rows, weight_in, weight_out, key_gain):
    hidden = jax.nn.gelu(jnp.dot(tile_rows, weight_in, preferred_element_type=jnp.float32), approximate=True).astype(jnp.bfloat16)
    keyval = jnp.dot(hidden, weight_out, preferred_element_type=jnp.float32)
    half_width = keyval.shape[1] // 2
    normed_keys = head_norm(keyval[:, :half_width], key_gain)
    return jnp.concatenate([normed_keys, keyval[:, half_width:]], axis=1).astype(jnp.bfloat16)

def reference(acts, patches, site_tiles, site_count, q_weight, q_gain, k_gain, tile_in, tile_out, out_weight, ffn_gain, gate_weight, up_weight, down_weight):
    slot_index = jnp.arange(LIST, dtype=jnp.int32)
    live_mask = (slot_index[None, :] < site_count[:, None]).astype(jnp.float32)
    outputs = []
    for section_index in range(N_SECTION):
        current = acts[section_index]
        q_raw = by_rows(current, q_weight[section_index]).astype(jnp.bfloat16)
        queries = rounded(head_norm(q_raw, q_gain[section_index]))
        patch_table = patches[section_index]
        weight_in = tile_in[section_index]
        weight_out = tile_out[section_index]
        key_gain = k_gain[section_index]

        def attend(inputs):
            query_block, tile_block, mask_block = inputs
            rows_here = patch_table[tile_block.reshape(-1)]
            pair_kv = rounded(encode(rows_here, weight_in, weight_out, key_gain)).astype(jnp.float32)
            pair_kv = pair_kv.reshape(SITE_DEV, LIST, 2, HEADS, HD)
            query_heads = query_block.astype(jnp.float32).reshape(SITE_DEV, HEADS, HD)
            scores = jnp.einsum('nhd,nlhd->nhl', query_heads, pair_kv[:, :, 0]) / math.sqrt(HD)
            exponents = jnp.exp(scores) * mask_block[:, None, :]
            weights = rounded(exponents / lax.optimization_barrier(jnp.sum(exponents, axis=-1, keepdims=True))).astype(jnp.float32)
            combined = jnp.einsum('nhl,nlhd->nhd', weights, pair_kv[:, :, 1])
            return combined.reshape(SITE_DEV, HEADS * HD).astype(jnp.bfloat16)
        attended = lax.map(attend, (queries.reshape(-1, SITE_DEV, INNER), site_tiles.reshape(-1, SITE_DEV, LIST), live_mask.reshape(-1, SITE_DEV, LIST)))
        attended = attended.reshape(NS, INNER)
        residual = current.astype(jnp.float32) + jnp.dot(attended, out_weight[section_index], preferred_element_type=jnp.float32)
        normed = rms_norm(residual, ffn_gain[section_index]).astype(jnp.bfloat16)
        gate_sum = by_rows(normed, gate_weight[section_index])
        up_sum = by_rows(normed, up_weight[section_index])
        hidden = (jax.nn.silu(gate_sum) * up_sum).astype(jnp.bfloat16)
        outputs.append((residual + jnp.dot(hidden, down_weight[section_index], preferred_element_type=jnp.float32)).astype(jnp.bfloat16))
    return jnp.stack([outputs[(position - 1) % N_SECTION] for position in range(N_SECTION)])
```

```python
import math

import jax
import jax.numpy as jnp
from jax import lax
from jax.sharding import PartitionSpec as P

HEADS = 16


epsilon = 1e-05

DIRECT_LIMIT = 8


def shift_pairs(count, steps):
    return [(source, (source + steps) % count) for source in range(count)]


def by_rows(left, weight_rows):
    return lax.dot_general(
        left, weight_rows, (((1,), (1,)), ((), ())), preferred_element_type=jnp.float32
    )


def head_norm(values, gain_row):
    shaped = values.astype(jnp.float32).reshape(values.shape[0], -1, gain_row.shape[0])
    scaled = (
        shaped * lax.rsqrt(jnp.mean(shaped * shaped, axis=-1, keepdims=True) + epsilon) * gain_row
    )
    return scaled.reshape(values.shape[0], -1)


def rms_norm(values, gain_row):
    return (
        values * lax.rsqrt(jnp.mean(values * values, axis=-1, keepdims=True) + epsilon) * gain_row
    )


def encode(tile_rows, weight_in, weight_out, key_gain):
    hidden = jax.nn.gelu(
        jnp.dot(tile_rows, weight_in, preferred_element_type=jnp.float32), approximate=True
    ).astype(jnp.bfloat16)
    keyval = jnp.dot(hidden, weight_out, preferred_element_type=jnp.float32)
    half_width = keyval.shape[1] // 2
    normed_keys = head_norm(keyval[:, :half_width], key_gain)
    return jnp.concatenate([normed_keys, keyval[:, half_width:]], axis=1).astype(jnp.bfloat16)


def to_source_order(slots, count, me):
    return jnp.take(slots, (me - jnp.arange(count, dtype=jnp.int32)) % count, axis=0)


def site_gather(value, count, me):
    if count > DIRECT_LIMIT:
        return lax.all_gather(value, "site", axis=0, tiled=False)
    slots = [value] + [
        lax.ppermute(value, "site", shift_pairs(count, steps)) for steps in range(1, count)
    ]
    return to_source_order(jnp.stack(slots), count, me)


def site_exchange(by_target, count, me):
    if count > DIRECT_LIMIT:
        return lax.all_to_all(by_target, "site", split_axis=0, concat_axis=0, tiled=True)
    slots = [lax.dynamic_index_in_dim(by_target, me, 0, keepdims=False)]
    for steps in range(1, count):
        piece = lax.dynamic_index_in_dim(by_target, (me + steps) % count, 0, keepdims=False)
        slots.append(lax.ppermute(piece, "site", shift_pairs(count, steps)))
    return to_source_order(jnp.stack(slots), count, me)


def ring_gather(values, count, me):
    if count > DIRECT_LIMIT:
        return [lax.all_gather(value, "site", axis=0, tiled=False) for value in values]
    order = list(range(0, count, 2)) + [i for i in range(count - 1, -1, -1) if i % 2 == 1]
    place = [0] * count
    for position, device in enumerate(order):
        place[device] = position
    forward = [(order[p], order[(p + 1) % count]) for p in range(count)]
    backward = [(order[p], order[(p - 1) % count]) for p in range(count)]
    order_arr = jnp.array(order, dtype=jnp.int32)
    my_place = jnp.array(place, dtype=jnp.int32)[me]
    forward_steps = count // 2
    backward_steps = count - 1 - forward_steps
    slot_source = [me]
    slots = [[value] for value in values]
    moving = list(values)
    for steps in range(1, forward_steps + 1):
        moving = [lax.ppermute(value, "site", forward) for value in moving]
        for slot, value in zip(slots, moving):
            slot.append(value)
        slot_source.append(order_arr[(my_place - steps) % count])
    moving = list(values)
    for steps in range(1, backward_steps + 1):
        moving = [lax.ppermute(value, "site", backward) for value in moving]
        for slot, value in zip(slots, moving):
            slot.append(value)
        slot_source.append(order_arr[(my_place + steps) % count])
    source_of_slot = jnp.stack(slot_source)
    slot_of_source = jnp.zeros((count,), jnp.int32).at[source_of_slot].set(
        jnp.arange(count, dtype=jnp.int32)
    )
    return [jnp.take(jnp.stack(slot), slot_of_source, axis=0) for slot in slots]


def shards(
    acts,
    patches,
    site_tiles,
    site_count,
    q_weight,
    q_gain,
    k_gain,
    tile_in,
    tile_out,
    out_weight,
    ffn_gain,
    gate_weight,
    up_weight,
    down_weight,
):
    group_size = lax.axis_size("site")
    section_count = lax.axis_size("section")
    my_index = lax.axis_index("site")
    sites_here = acts.shape[1]
    list_width = site_tiles.shape[1]
    tiles_here = patches.shape[1]
    head_size = q_gain.shape[1]
    capacity = max(2, 5 * sites_here * list_width // (4 * group_size))
    entries = sites_here * list_width
    current = acts[0]

    gathered_in, gathered_out = ring_gather([tile_in[0], tile_out[0]], group_size, my_index)
    weight_in = gathered_in.reshape(-1, gathered_in.shape[-1])
    weight_out = gathered_out.reshape(-1, gathered_out.shape[-1])

    slot_index = jnp.arange(list_width, dtype=jnp.int32)
    live_all = (slot_index[None, :] < site_count[:, None]).reshape(group_size, entries)
    owner_all = (site_tiles // tiles_here).reshape(group_size, entries)
    local_all = (site_tiles % tiles_here).reshape(group_size, entries)
    mine_mask = jnp.logical_and(live_all, owner_all == my_index)
    slot_rank = jnp.cumsum(mine_mask.astype(jnp.int32), axis=1) - 1
    picks = jnp.logical_and(
        mine_mask[:, :, None],
        slot_rank[:, :, None] == jnp.arange(capacity, dtype=jnp.int32)[None, None, :],
    )
    send_index = jnp.sum(jnp.where(picks, local_all[:, :, None], 0), axis=1)
    send_rows = patches[0][send_index.reshape(-1)].reshape(group_size, capacity, -1)
    arrived = site_exchange(send_rows, group_size, my_index)

    my_tiles = lax.dynamic_slice_in_dim(site_tiles, my_index * sites_here, sites_here, 0)
    my_count = lax.dynamic_slice_in_dim(site_count, my_index * sites_here, sites_here, 0)
    my_live = slot_index[None, :] < my_count[:, None]
    my_owner = (my_tiles // tiles_here).reshape(-1)
    one_hot = jnp.logical_and(
        my_owner[:, None] == jnp.arange(group_size, dtype=jnp.int32)[None, :],
        my_live.reshape(-1)[:, None],
    ).astype(jnp.int32)
    my_rank = jnp.sum(jnp.cumsum(one_hot, axis=0) * one_hot, axis=1) - 1
    fetch_index = jnp.where(my_live.reshape(-1), my_owner * capacity + my_rank, 0)
    pair_rows = arrived.reshape(group_size * capacity, -1)[fetch_index]
    pair_kv = encode(pair_rows, weight_in, weight_out, k_gain[0])
    pair_kv = pair_kv.reshape(sites_here, list_width, 2, HEADS, head_size)

    everyone = site_gather(current, group_size, my_index).reshape(-1, current.shape[-1])
    q_part = by_rows(everyone, q_weight[0]).astype(jnp.bfloat16)
    q_blocks = site_exchange(
        q_part.reshape(group_size, sites_here, -1), group_size, my_index
    )
    my_queries = jnp.moveaxis(q_blocks, 0, 1).reshape(sites_here, -1)
    queries = head_norm(my_queries, q_gain[0]).astype(jnp.bfloat16)
    query_heads = queries.reshape(sites_here, HEADS, head_size)
    scores = jnp.einsum(
        "nhd,nlhd->nhl", query_heads, pair_kv[:, :, 0], preferred_element_type=jnp.float32
    ) / math.sqrt(head_size)
    exponents = jnp.exp(scores) * my_live.astype(jnp.float32)[:, None, :]
    weights = (exponents / jnp.sum(exponents, axis=-1, keepdims=True)).astype(jnp.bfloat16)
    combined = jnp.einsum(
        "nhl,nlhd->nhd", weights, pair_kv[:, :, 1], preferred_element_type=jnp.float32
    )
    combined = combined.reshape(sites_here, -1).astype(jnp.bfloat16)
    column_blocks = jnp.moveaxis(combined.reshape(sites_here, group_size, -1), 1, 0)
    columns = site_exchange(column_blocks, group_size, my_index).reshape(
        group_size * sites_here, -1
    )
    attn_part = jnp.dot(columns, out_weight[0], preferred_element_type=jnp.float32)
    attn_sum = jnp.sum(
        site_exchange(attn_part.reshape(group_size, sites_here, -1), group_size, my_index),
        axis=0,
    )
    residual = current.astype(jnp.float32) + attn_sum
    normed = rms_norm(residual, ffn_gain[0]).astype(jnp.bfloat16)
    normed_rows = site_gather(normed, group_size, my_index).reshape(-1, normed.shape[-1])
    gate_sum = by_rows(normed_rows, gate_weight[0])
    up_sum = by_rows(normed_rows, up_weight[0])
    hidden = (jax.nn.silu(gate_sum) * up_sum).astype(jnp.bfloat16)
    down_part = jnp.dot(hidden, down_weight[0], preferred_element_type=jnp.float32)
    down_part = down_part.reshape(group_size, sites_here, -1)
    if group_size > DIRECT_LIMIT:
        down_sum = lax.psum_scatter(down_part, "site", scatter_dimension=0, tiled=True)[0]
        output_rows = (residual + down_sum).astype(jnp.bfloat16)
        pairs = shift_pairs(section_count, 1)
        return lax.ppermute(output_rows[None], "section", pairs)
    contributions = []
    for steps in range(group_size):
        piece = lax.dynamic_index_in_dim(
            down_part, (my_index + steps) % group_size, 0, keepdims=False
        )
        if steps == 0:
            piece = piece + residual
        pairs = [
            (
                section * group_size + site,
                ((section + 1) % section_count) * group_size + (site + steps) % group_size,
            )
            for section in range(section_count)
            for site in range(group_size)
        ]
        contributions.append(lax.ppermute(piece, ("section", "site"), pairs))
    output_rows = sum(contributions[1:], contributions[0]).astype(jnp.bfloat16)
    return output_rows[None]


def solution(mesh):
    return jax.shard_map(
        shards,
        mesh=mesh,
        in_specs=(
            P("section", "site", None),
            P("section", "site", None),
            P(),
            P(),
            P("section", "site", None),
            P("section", None),
            P("section", None),
            P("section", "site", None),
            P("section", "site", None),
            P("section", "site", None),
            P("section", None),
            P("section", "site", None),
            P("section", "site", None),
            P("section", "site", None),
        ),
        out_specs=P("section", "site", None),
        check_vma=False,
    )
```

```python
import math

import jax
import jax.numpy as jnp
from jax import lax
from jax.sharding import PartitionSpec as P

HEADS = 16


epsilon = 1e-05

DIRECT_LIMIT = 8


def shift_pairs(count, steps):
    return [(source, (source + steps) % count) for source in range(count)]


def by_rows(left, weight_rows):
    return lax.dot_general(
        left, weight_rows, (((1,), (1,)), ((), ())), preferred_element_type=jnp.float32
    )


def head_norm(values, gain_row):
    shaped = values.astype(jnp.float32).reshape(values.shape[0], -1, gain_row.shape[0])
    scaled = (
        shaped * lax.rsqrt(jnp.mean(shaped * shaped, axis=-1, keepdims=True) + epsilon) * gain_row
    )
    return scaled.reshape(values.shape[0], -1)


def rms_norm(values, gain_row):
    return (
        values * lax.rsqrt(jnp.mean(values * values, axis=-1, keepdims=True) + epsilon) * gain_row
    )


def to_source_order(slots, count, me):
    return jnp.take(slots, (me - jnp.arange(count, dtype=jnp.int32)) % count, axis=0)


def xor_pairs(count, bit):
    return [(source, source ^ (1 << bit)) for source in range(count)]


def direct_ok(count):
    return count <= DIRECT_LIMIT and count & (count - 1) == 0


def site_exchange(by_target, count, me):
    if not direct_ok(count):
        return lax.all_to_all(by_target, "site", split_axis=0, concat_axis=0, tiled=True)
    slots = [lax.dynamic_index_in_dim(by_target, me, 0, keepdims=False)]
    for steps in range(1, count):
        piece = lax.dynamic_index_in_dim(by_target, (me + steps) % count, 0, keepdims=False)
        slots.append(lax.ppermute(piece, "site", shift_pairs(count, steps)))
    return to_source_order(jnp.stack(slots), count, me)


def halving_exchange(by_target, count, me):
    if not direct_ok(count):
        return lax.all_to_all(by_target, "site", split_axis=0, concat_axis=0, tiled=True)
    bits = count.bit_length() - 1
    rest = by_target.shape[1:]
    state = by_target.reshape((2,) * bits + rest)
    for bit in range(bits):
        axis = bits - 1 - bit
        mine = (me >> bit) & 1
        keep = lax.dynamic_index_in_dim(state, mine, axis, keepdims=True)
        send = lax.dynamic_index_in_dim(state, 1 - mine, axis, keepdims=True)
        recv = lax.ppermute(send, "site", xor_pairs(count, bit))
        state = jnp.where(
            mine == 0,
            jnp.concatenate([keep, recv], axis),
            jnp.concatenate([recv, keep], axis),
        )
    return state.reshape((count,) + rest)


def doubling_gather(value, count, me):
    if not direct_ok(count):
        return lax.all_gather(value, "site", axis=0, tiled=False)
    bits = count.bit_length() - 1
    state = value[None]
    for bit in range(bits):
        recv = lax.ppermute(state, "site", xor_pairs(count, bit))
        mine = (me >> bit) & 1
        state = jnp.where(
            mine == 0, jnp.concatenate([state, recv], 0), jnp.concatenate([recv, state], 0)
        )
    return state


def halving_sum(parts, count, me):
    if not direct_ok(count):
        return lax.psum_scatter(parts, "site", scatter_dimension=0, tiled=True)[0]
    bits = count.bit_length() - 1
    rest = parts.shape[1:]
    state = parts.reshape((2,) * bits + rest)
    for bit in range(bits):
        axis = bits - 1 - bit
        mine = (me >> bit) & 1
        keep = lax.dynamic_index_in_dim(state, mine, axis, keepdims=True)
        send = lax.dynamic_index_in_dim(state, 1 - mine, axis, keepdims=True)
        state = keep + lax.ppermute(send, "site", xor_pairs(count, bit))
    return state.reshape(rest)


def ring_gather(value, count, me):
    if not direct_ok(count):
        return lax.all_gather(value, "site", axis=0, tiled=False), jnp.arange(count, dtype=jnp.int32)
    order = list(range(0, count, 2)) + [i for i in range(count - 1, -1, -1) if i % 2 == 1]
    place = [0] * count
    for position, device in enumerate(order):
        place[device] = position
    forward = [(order[p], order[(p + 1) % count]) for p in range(count)]
    backward = [(order[p], order[(p - 1) % count]) for p in range(count)]
    forward_steps = count // 2
    backward_steps = count - 1 - forward_steps
    slots = [value]
    moving = value
    for _ in range(forward_steps):
        moving = lax.ppermute(moving, "site", forward)
        slots.append(moving)
    moving = value
    for _ in range(backward_steps):
        moving = lax.ppermute(moving, "site", backward)
        slots.append(moving)
    offsets = [0] + [-s for s in range(1, forward_steps + 1)] + list(range(1, backward_steps + 1))
    my_place = jnp.array(place, dtype=jnp.int32)[me]
    source_of_slot = jnp.array(order, dtype=jnp.int32)[
        (my_place + jnp.array(offsets, dtype=jnp.int32)) % count
    ]
    return jnp.stack(slots), source_of_slot


def shards(
    acts,
    patches,
    site_tiles,
    site_count,
    q_weight,
    q_gain,
    k_gain,
    tile_in,
    tile_out,
    out_weight,
    ffn_gain,
    gate_weight,
    up_weight,
    down_weight,
):
    group_size = lax.axis_size("site")
    section_count = lax.axis_size("section")
    my_index = lax.axis_index("site")
    sites_here = acts.shape[1]
    list_width = site_tiles.shape[1]
    tiles_here = patches.shape[1]
    head_size = q_gain.shape[1]
    capacity = max(2, 5 * sites_here * list_width // (4 * group_size))
    entries = sites_here * list_width
    current = acts[0]
    model_width = current.shape[-1]
    row_width = patches.shape[-1]

    width_in = tile_in.shape[-1]
    in_rows = tile_in.shape[1] * width_in // tile_out.shape[-1]
    packed_weights = jnp.concatenate(
        [tile_in[0].reshape(in_rows, tile_out.shape[-1]), tile_out[0]], axis=0
    )
    weight_slots, source_of_slot = ring_gather(packed_weights, group_size, my_index)
    weight_in = weight_slots[:, :in_rows].reshape(-1, width_in)
    weight_out = weight_slots[:, in_rows:].reshape(-1, weight_slots.shape[-1])

    slot_index = jnp.arange(list_width, dtype=jnp.int32)
    live_all = (slot_index[None, :] < site_count[:, None]).reshape(group_size, entries)
    owner_all = (site_tiles // tiles_here).reshape(group_size, entries)
    local_all = (site_tiles % tiles_here).reshape(group_size, entries)
    mine_mask = jnp.logical_and(live_all, owner_all == my_index)
    slot_rank = jnp.cumsum(mine_mask.astype(jnp.int32), axis=1) - 1
    picks = jnp.logical_and(
        mine_mask[:, :, None],
        slot_rank[:, :, None] == jnp.arange(capacity, dtype=jnp.int32)[None, None, :],
    )
    send_index = jnp.sum(jnp.where(picks, local_all[:, :, None], 0), axis=1)
    send_rows = patches[0][send_index.reshape(-1)].reshape(group_size, capacity, row_width)
    act_rows = sites_here * model_width // row_width
    packed = model_width % row_width == 0
    if packed:
        act_block = jnp.broadcast_to(
            current.reshape(1, act_rows, row_width), (group_size, act_rows, row_width)
        )
        arrived = site_exchange(
            jnp.concatenate([send_rows, act_block], axis=1), group_size, my_index
        )
        everyone = arrived[:, capacity:].reshape(-1, model_width)
        arrived = arrived[:, :capacity]
    else:
        arrived = site_exchange(send_rows, group_size, my_index)
        everyone = doubling_gather(current, group_size, my_index).reshape(-1, model_width)

    my_tiles = lax.dynamic_slice_in_dim(site_tiles, my_index * sites_here, sites_here, 0)
    my_count = lax.dynamic_slice_in_dim(site_count, my_index * sites_here, sites_here, 0)
    my_live = slot_index[None, :] < my_count[:, None]
    my_owner = (my_tiles // tiles_here).reshape(-1)
    one_hot = jnp.logical_and(
        my_owner[:, None] == jnp.arange(group_size, dtype=jnp.int32)[None, :],
        my_live.reshape(-1)[:, None],
    ).astype(jnp.int32)
    my_rank = jnp.sum(jnp.cumsum(one_hot, axis=0) * one_hot, axis=1) - 1
    fetch_index = jnp.where(my_live.reshape(-1), my_owner * capacity + my_rank, 0)
    pair_rows = arrived.reshape(group_size * capacity, row_width)[fetch_index]

    rows_in = pair_rows.reshape(entries, group_size, -1)
    rows_in = jnp.take(rows_in, source_of_slot, axis=1).reshape(entries, -1)
    hidden = jax.nn.gelu(
        jnp.dot(rows_in, weight_in, preferred_element_type=jnp.float32), approximate=True
    ).astype(jnp.bfloat16)
    hidden = jnp.take(hidden.reshape(entries, group_size, -1), source_of_slot, axis=1)
    keyval = jnp.dot(hidden.reshape(entries, -1), weight_out, preferred_element_type=jnp.float32)
    half_width = keyval.shape[1] // 2
    normed_keys = head_norm(keyval[:, :half_width], k_gain[0])
    pair_kv = jnp.concatenate([normed_keys, keyval[:, half_width:]], axis=1).astype(jnp.bfloat16)
    pair_kv = pair_kv.reshape(sites_here, list_width, 2, HEADS, head_size)

    q_part = by_rows(everyone, q_weight[0]).astype(jnp.bfloat16)
    q_blocks = halving_exchange(
        q_part.reshape(group_size, sites_here, -1), group_size, my_index
    )
    my_queries = jnp.moveaxis(q_blocks, 0, 1).reshape(sites_here, -1)
    queries = head_norm(my_queries, q_gain[0]).astype(jnp.bfloat16)
    query_heads = queries.reshape(sites_here, HEADS, head_size)
    scores = jnp.einsum(
        "nhd,nlhd->nhl", query_heads, pair_kv[:, :, 0], preferred_element_type=jnp.float32
    ) / math.sqrt(head_size)
    exponents = jnp.exp(scores) * my_live.astype(jnp.float32)[:, None, :]
    weights = (exponents / jnp.sum(exponents, axis=-1, keepdims=True)).astype(jnp.bfloat16)
    combined = jnp.einsum(
        "nhl,nlhd->nhd", weights, pair_kv[:, :, 1], preferred_element_type=jnp.float32
    )
    combined = combined.reshape(sites_here, -1).astype(jnp.bfloat16)
    column_blocks = jnp.moveaxis(combined.reshape(sites_here, group_size, -1), 1, 0)
    columns = halving_exchange(column_blocks, group_size, my_index).reshape(
        group_size * sites_here, -1
    )
    attn_part = jnp.dot(columns, out_weight[0], preferred_element_type=jnp.float32)
    attn_sum = halving_sum(attn_part.reshape(group_size, sites_here, -1), group_size, my_index)
    residual = current.astype(jnp.float32) + attn_sum
    normed = rms_norm(residual, ffn_gain[0]).astype(jnp.bfloat16)
    normed_rows = doubling_gather(normed, group_size, my_index).reshape(-1, model_width)
    gate_sum = by_rows(normed_rows, gate_weight[0])
    up_sum = by_rows(normed_rows, up_weight[0])
    hidden_ffn = (jax.nn.silu(gate_sum) * up_sum).astype(jnp.bfloat16)
    down_part = jnp.dot(hidden_ffn, down_weight[0], preferred_element_type=jnp.float32)
    down_sum = halving_sum(down_part.reshape(group_size, sites_here, -1), group_size, my_index)
    output_rows = (residual + down_sum).astype(jnp.bfloat16)
    return lax.ppermute(output_rows[None], "section", shift_pairs(section_count, 1))


def solution(mesh):
    return jax.shard_map(
        shards,
        mesh=mesh,
        in_specs=(
            P("section", "site", None),
            P("section", "site", None),
            P(),
            P(),
            P("section", "site", None),
            P("section", None),
            P("section", None),
            P("section", "site", None),
            P("section", "site", None),
            P("section", "site", None),
            P("section", None),
            P("section", "site", None),
            P("section", "site", None),
            P("section", "site", None),
        ),
        out_specs=P("section", "site", None),
        check_vma=False,
    )
```

```python
import math

import jax
import jax.numpy as jnp
from jax import lax
from jax.sharding import PartitionSpec as P

HEADS = 16


epsilon = 1e-05

DIRECT_LIMIT = 8


def shift_pairs(count, steps):
    return [(source, (source + steps) % count) for source in range(count)]


def by_rows(left, weight_rows):
    return lax.dot_general(
        left, weight_rows, (((1,), (1,)), ((), ())), preferred_element_type=jnp.float32
    )


def head_norm(values, gain_row):
    shaped = values.astype(jnp.float32).reshape(values.shape[0], -1, gain_row.shape[0])
    scaled = (
        shaped * lax.rsqrt(jnp.mean(shaped * shaped, axis=-1, keepdims=True) + epsilon) * gain_row
    )
    return scaled.reshape(values.shape[0], -1)


def rms_norm(values, gain_row):
    return (
        values * lax.rsqrt(jnp.mean(values * values, axis=-1, keepdims=True) + epsilon) * gain_row
    )


def to_source_order(slots, count, me):
    return jnp.take(slots, (me - jnp.arange(count, dtype=jnp.int32)) % count, axis=0)


def xor_pairs(count, bit):
    return [(source, source ^ (1 << bit)) for source in range(count)]


def direct_ok(count):
    return count <= DIRECT_LIMIT and count & (count - 1) == 0


def site_exchange(by_target, count, me):
    if not direct_ok(count):
        return lax.all_to_all(by_target, "site", split_axis=0, concat_axis=0, tiled=True)
    slots = [lax.dynamic_index_in_dim(by_target, me, 0, keepdims=False)]
    for steps in range(1, count):
        piece = lax.dynamic_index_in_dim(by_target, (me + steps) % count, 0, keepdims=False)
        slots.append(lax.ppermute(piece, "site", shift_pairs(count, steps)))
    return to_source_order(jnp.stack(slots), count, me)


def halving_exchange(by_target, count, me):
    if not direct_ok(count):
        return lax.all_to_all(by_target, "site", split_axis=0, concat_axis=0, tiled=True)
    bits = count.bit_length() - 1
    rest = by_target.shape[1:]
    state = by_target.reshape((2,) * bits + rest)
    for bit in range(bits):
        axis = bits - 1 - bit
        mine = (me >> bit) & 1
        keep = lax.dynamic_index_in_dim(state, mine, axis, keepdims=True)
        send = lax.dynamic_index_in_dim(state, 1 - mine, axis, keepdims=True)
        recv = lax.ppermute(send, "site", xor_pairs(count, bit))
        state = jnp.where(
            mine == 0,
            jnp.concatenate([keep, recv], axis),
            jnp.concatenate([recv, keep], axis),
        )
    return state.reshape((count,) + rest)


def doubling_gather(value, count, me):
    if not direct_ok(count):
        return lax.all_gather(value, "site", axis=0, tiled=False)
    bits = count.bit_length() - 1
    state = value[None]
    for bit in range(bits):
        recv = lax.ppermute(state, "site", xor_pairs(count, bit))
        mine = (me >> bit) & 1
        state = jnp.where(
            mine == 0, jnp.concatenate([state, recv], 0), jnp.concatenate([recv, state], 0)
        )
    return state


def halving_sum(parts, count, me):
    if not direct_ok(count):
        return lax.psum_scatter(parts, "site", scatter_dimension=0, tiled=True)[0]
    bits = count.bit_length() - 1
    rest = parts.shape[1:]
    state = parts.reshape((2,) * bits + rest)
    for bit in range(bits):
        axis = bits - 1 - bit
        mine = (me >> bit) & 1
        keep = lax.dynamic_index_in_dim(state, mine, axis, keepdims=True)
        send = lax.dynamic_index_in_dim(state, 1 - mine, axis, keepdims=True)
        state = keep + lax.ppermute(send, "site", xor_pairs(count, bit))
    return state.reshape(rest)


def doubling_sum(parts, count):
    state = parts
    for bit in range(count.bit_length() - 1):
        state = state + lax.ppermute(state, "site", xor_pairs(count, bit))
    return state


class RingGather:
    def __init__(self, value, count, me):
        self.count = count
        self.direct = direct_ok(count)
        if not self.direct:
            self.slots = lax.all_gather(value, "site", axis=0, tiled=False)
            self.sources = jnp.arange(count, dtype=jnp.int32)
            return
        order = list(range(0, count, 2)) + [i for i in range(count - 1, -1, -1) if i % 2 == 1]
        place = [0] * count
        for position, device in enumerate(order):
            place[device] = position
        self.forward = [(order[p], order[(p + 1) % count]) for p in range(count)]
        self.backward = [(order[p], order[(p - 1) % count]) for p in range(count)]
        self.forward_left = count // 2
        self.backward_left = count - 1 - self.forward_left
        offsets = [0] + [-s for s in range(1, self.forward_left + 1)]
        offsets += list(range(1, self.backward_left + 1))
        my_place = jnp.array(place, dtype=jnp.int32)[me]
        self.sources = jnp.array(order, dtype=jnp.int32)[
            (my_place + jnp.array(offsets, dtype=jnp.int32)) % count
        ]
        self.forward_slots = []
        self.backward_slots = []
        self.ahead = value
        self.behind = value
        self.value = value
        self._issue()

    def _issue(self):
        if self.forward_left > 0:
            self.ahead = lax.ppermute(self.ahead, "site", self.forward)
            self.forward_slots.append(self.ahead)
            self.forward_left -= 1
        if self.backward_left > 0:
            self.behind = lax.ppermute(self.behind, "site", self.backward)
            self.backward_slots.append(self.behind)
            self.backward_left -= 1

    def step(self, tied):
        if not self.direct or (self.forward_left == 0 and self.backward_left == 0):
            return tied
        self.ahead, self.behind, tied = lax.optimization_barrier((self.ahead, self.behind, tied))
        self.forward_slots[-1] = self.ahead
        if self.backward_slots:
            self.backward_slots[-1] = self.behind
        self._issue()
        return tied

    def finish(self):
        if not self.direct:
            return self.slots, self.sources
        while self.forward_left > 0 or self.backward_left > 0:
            self._issue()
        slots = [self.value] + self.forward_slots + self.backward_slots
        return jnp.stack(slots), self.sources


def shards(
    acts,
    patches,
    site_tiles,
    site_count,
    q_weight,
    q_gain,
    k_gain,
    tile_in,
    tile_out,
    out_weight,
    ffn_gain,
    gate_weight,
    up_weight,
    down_weight,
):
    group_size = lax.axis_size("site")
    section_count = lax.axis_size("section")
    my_index = lax.axis_index("site")
    sites_here = acts.shape[1]
    list_width = site_tiles.shape[1]
    tiles_here = patches.shape[1]
    head_size = q_gain.shape[1]
    capacity = max(2, 5 * sites_here * list_width // (4 * group_size))
    entries = sites_here * list_width
    current = acts[0]
    model_width = current.shape[-1]
    row_width = patches.shape[-1]

    width_in = tile_in.shape[-1]
    in_rows = tile_in.shape[1] * width_in // tile_out.shape[-1]
    packed_weights = jnp.concatenate(
        [tile_in[0].reshape(in_rows, tile_out.shape[-1]), tile_out[0]], axis=0
    )
    ring = RingGather(packed_weights, group_size, my_index)

    slot_index = jnp.arange(list_width, dtype=jnp.int32)
    live_all = (slot_index[None, :] < site_count[:, None]).reshape(group_size, entries)
    owner_all = (site_tiles // tiles_here).reshape(group_size, entries)
    local_all = (site_tiles % tiles_here).reshape(group_size, entries)
    mine_mask = jnp.logical_and(live_all, owner_all == my_index)
    slot_rank = jnp.cumsum(mine_mask.astype(jnp.int32), axis=1) - 1
    picks = jnp.logical_and(
        mine_mask[:, :, None],
        slot_rank[:, :, None] == jnp.arange(capacity, dtype=jnp.int32)[None, None, :],
    )
    send_index = jnp.sum(jnp.where(picks, local_all[:, :, None], 0), axis=1)
    send_rows = patches[0][send_index.reshape(-1)].reshape(group_size, capacity, row_width)
    act_rows = sites_here * model_width // row_width
    packed = model_width % row_width == 0
    if packed:
        act_block = jnp.broadcast_to(
            current.reshape(1, act_rows, row_width), (group_size, act_rows, row_width)
        )
        send_rows = jnp.concatenate([send_rows, act_block], axis=1)
    send_rows = ring.step(send_rows)
    arrived = lax.all_to_all(send_rows, "site", split_axis=0, concat_axis=0, tiled=True)
    if packed:
        everyone = arrived[:, capacity:].reshape(-1, model_width)
        arrived = arrived[:, :capacity]
    else:
        everyone = doubling_gather(current, group_size, my_index).reshape(-1, model_width)
    q_part = by_rows(everyone, q_weight[0]).astype(jnp.bfloat16)
    q_part = ring.step(q_part)
    q_blocks = halving_exchange(
        q_part.reshape(group_size, sites_here, -1), group_size, my_index
    )
    q_blocks = ring.step(q_blocks)
    weight_slots, source_of_slot = ring.finish()
    weight_in = weight_slots[:, :in_rows].reshape(-1, width_in)
    weight_out = weight_slots[:, in_rows:].reshape(-1, weight_slots.shape[-1])

    my_tiles = lax.dynamic_slice_in_dim(site_tiles, my_index * sites_here, sites_here, 0)
    my_count = lax.dynamic_slice_in_dim(site_count, my_index * sites_here, sites_here, 0)
    my_live = slot_index[None, :] < my_count[:, None]
    my_owner = (my_tiles // tiles_here).reshape(-1)
    one_hot = jnp.logical_and(
        my_owner[:, None] == jnp.arange(group_size, dtype=jnp.int32)[None, :],
        my_live.reshape(-1)[:, None],
    ).astype(jnp.int32)
    my_rank = jnp.sum(jnp.cumsum(one_hot, axis=0) * one_hot, axis=1) - 1
    fetch_index = jnp.where(my_live.reshape(-1), my_owner * capacity + my_rank, 0)
    pair_rows = arrived.reshape(group_size * capacity, row_width)[fetch_index]

    rows_in = pair_rows.reshape(entries, group_size, -1)
    rows_in = jnp.take(rows_in, source_of_slot, axis=1).reshape(entries, -1)
    hidden = jax.nn.gelu(
        jnp.dot(rows_in, weight_in, preferred_element_type=jnp.float32), approximate=True
    ).astype(jnp.bfloat16)
    hidden = jnp.take(hidden.reshape(entries, group_size, -1), source_of_slot, axis=1)
    keyval = jnp.dot(hidden.reshape(entries, -1), weight_out, preferred_element_type=jnp.float32)
    half_width = keyval.shape[1] // 2
    normed_keys = head_norm(keyval[:, :half_width], k_gain[0])
    pair_kv = jnp.concatenate([normed_keys, keyval[:, half_width:]], axis=1).astype(jnp.bfloat16)
    pair_kv = pair_kv.reshape(sites_here, list_width, 2, HEADS, head_size)

    my_queries = jnp.moveaxis(q_blocks, 0, 1).reshape(sites_here, -1)
    queries = head_norm(my_queries, q_gain[0]).astype(jnp.bfloat16)
    query_heads = queries.reshape(sites_here, HEADS, head_size)
    scores = jnp.einsum(
        "nhd,nlhd->nhl", query_heads, pair_kv[:, :, 0], preferred_element_type=jnp.float32
    ) / math.sqrt(head_size)
    exponents = jnp.exp(scores) * my_live.astype(jnp.float32)[:, None, :]
    weights = (exponents / jnp.sum(exponents, axis=-1, keepdims=True)).astype(jnp.bfloat16)
    combined = jnp.einsum(
        "nhl,nlhd->nhd", weights, pair_kv[:, :, 1], preferred_element_type=jnp.float32
    )
    combined = combined.reshape(sites_here, -1).astype(jnp.bfloat16)
    column_blocks = jnp.moveaxis(combined.reshape(sites_here, group_size, -1), 1, 0)
    columns = halving_exchange(column_blocks, group_size, my_index).reshape(
        group_size * sites_here, -1
    )
    attn_part = jnp.dot(columns, out_weight[0], preferred_element_type=jnp.float32)
    attn_part = attn_part.reshape(group_size, sites_here, -1)
    if direct_ok(group_size):
        attn_all = doubling_sum(attn_part, group_size)
        residual_all = everyone.reshape(group_size, sites_here, -1).astype(jnp.float32) + attn_all
        residual = lax.dynamic_index_in_dim(residual_all, my_index, 0, keepdims=False)
        normed_rows = rms_norm(residual_all, ffn_gain[0]).astype(jnp.bfloat16)
        normed_rows = normed_rows.reshape(-1, model_width)
    else:
        attn_sum = halving_sum(attn_part, group_size, my_index)
        residual = current.astype(jnp.float32) + attn_sum
        normed = rms_norm(residual, ffn_gain[0]).astype(jnp.bfloat16)
        normed_rows = doubling_gather(normed, group_size, my_index).reshape(-1, model_width)
    gate_sum = by_rows(normed_rows, gate_weight[0])
    up_sum = by_rows(normed_rows, up_weight[0])
    hidden_ffn = (jax.nn.silu(gate_sum) * up_sum).astype(jnp.bfloat16)
    down_part = jnp.dot(hidden_ffn, down_weight[0], preferred_element_type=jnp.float32)
    down_part = down_part.reshape(group_size, sites_here, -1)
    if not direct_ok(group_size) or group_size == 1:
        down_sum = halving_sum(down_part, group_size, my_index)
        output_rows = (residual + down_sum).astype(jnp.bfloat16)
        return lax.ppermute(output_rows[None], "section", shift_pairs(section_count, 1))
    bits = group_size.bit_length() - 1
    rest = down_part.shape[1:]
    state = down_part.reshape((2,) * bits + rest)
    for bit in range(bits):
        axis = bits - 1 - bit
        mine = (my_index >> bit) & 1
        keep = lax.dynamic_index_in_dim(state, mine, axis, keepdims=True)
        send = lax.dynamic_index_in_dim(state, 1 - mine, axis, keepdims=True)
        if bit < bits - 1:
            state = keep + lax.ppermute(send, "site", xor_pairs(group_size, bit))
            continue
        own = keep.reshape(rest) + residual
        forward = [
            (section * group_size + site, ((section + 1) % section_count) * group_size + site)
            for section in range(section_count)
            for site in range(group_size)
        ]
        across = [
            (
                section * group_size + site,
                ((section + 1) % section_count) * group_size + (site ^ (1 << bit)),
            )
            for section in range(section_count)
            for site in range(group_size)
        ]
        mine_part = lax.ppermute(own, ("section", "site"), forward)
        other_part = lax.ppermute(send.reshape(rest), ("section", "site"), across)
        output_rows = (mine_part + other_part).astype(jnp.bfloat16)
    return output_rows[None]


def solution(mesh):
    return jax.shard_map(
        shards,
        mesh=mesh,
        in_specs=(
            P("section", "site", None),
            P("section", "site", None),
            P(),
            P(),
            P("section", "site", None),
            P("section", None),
            P("section", None),
            P("section", "site", None),
            P("section", "site", None),
            P("section", "site", None),
            P("section", None),
            P("section", "site", None),
            P("section", "site", None),
            P("section", "site", None),
        ),
        out_specs=P("section", "site", None),
        check_vma=False,
    )
```

```python
import math

import jax
import jax.numpy as jnp
from jax import lax
from jax.sharding import PartitionSpec as P

HEADS = 16


epsilon = 1e-05

DIRECT_LIMIT = 8


def shift_pairs(count, steps):
    return [(source, (source + steps) % count) for source in range(count)]


def by_rows(left, weight_rows):
    return lax.dot_general(
        left, weight_rows, (((1,), (1,)), ((), ())), preferred_element_type=jnp.float32
    )


def head_norm(values, gain_row):
    shaped = values.astype(jnp.float32).reshape(values.shape[0], -1, gain_row.shape[0])
    scaled = (
        shaped * lax.rsqrt(jnp.mean(shaped * shaped, axis=-1, keepdims=True) + epsilon) * gain_row
    )
    return scaled.reshape(values.shape[0], -1)


def rms_norm(values, gain_row):
    return (
        values * lax.rsqrt(jnp.mean(values * values, axis=-1, keepdims=True) + epsilon) * gain_row
    )


def to_source_order(slots, count, me):
    return jnp.take(slots, (me - jnp.arange(count, dtype=jnp.int32)) % count, axis=0)


def xor_pairs(count, bit):
    return [(source, source ^ (1 << bit)) for source in range(count)]


def direct_ok(count):
    return count <= DIRECT_LIMIT and count & (count - 1) == 0


def site_exchange(by_target, count, me):
    if not direct_ok(count):
        return lax.all_to_all(by_target, "site", split_axis=0, concat_axis=0, tiled=True)
    slots = [lax.dynamic_index_in_dim(by_target, me, 0, keepdims=False)]
    for steps in range(1, count):
        piece = lax.dynamic_index_in_dim(by_target, (me + steps) % count, 0, keepdims=False)
        slots.append(lax.ppermute(piece, "site", shift_pairs(count, steps)))
    return to_source_order(jnp.stack(slots), count, me)


def halving_exchange(by_target, count, me):
    if not direct_ok(count):
        return lax.all_to_all(by_target, "site", split_axis=0, concat_axis=0, tiled=True)
    bits = count.bit_length() - 1
    rest = by_target.shape[1:]
    state = by_target.reshape((2,) * bits + rest)
    for bit in range(bits):
        axis = bits - 1 - bit
        mine = (me >> bit) & 1
        keep = lax.dynamic_index_in_dim(state, mine, axis, keepdims=True)
        send = lax.dynamic_index_in_dim(state, 1 - mine, axis, keepdims=True)
        recv = lax.ppermute(send, "site", xor_pairs(count, bit))
        state = jnp.where(
            mine == 0,
            jnp.concatenate([keep, recv], axis),
            jnp.concatenate([recv, keep], axis),
        )
    return state.reshape((count,) + rest)


def doubling_gather(value, count, me):
    if not direct_ok(count):
        return lax.all_gather(value, "site", axis=0, tiled=False)
    bits = count.bit_length() - 1
    state = value[None]
    for bit in range(bits):
        recv = lax.ppermute(state, "site", xor_pairs(count, bit))
        mine = (me >> bit) & 1
        state = jnp.where(
            mine == 0, jnp.concatenate([state, recv], 0), jnp.concatenate([recv, state], 0)
        )
    return state


def halving_sum(parts, count, me):
    if not direct_ok(count):
        return lax.psum_scatter(parts, "site", scatter_dimension=0, tiled=True)[0]
    bits = count.bit_length() - 1
    rest = parts.shape[1:]
    state = parts.reshape((2,) * bits + rest)
    for bit in range(bits):
        axis = bits - 1 - bit
        mine = (me >> bit) & 1
        keep = lax.dynamic_index_in_dim(state, mine, axis, keepdims=True)
        send = lax.dynamic_index_in_dim(state, 1 - mine, axis, keepdims=True)
        state = keep + lax.ppermute(send, "site", xor_pairs(count, bit))
    return state.reshape(rest)


def doubling_sum(parts, count):
    state = parts
    for bit in range(count.bit_length() - 1):
        state = state + lax.ppermute(state, "site", xor_pairs(count, bit))
    return state


class RingGather:
    def __init__(self, value, count, me):
        self.count = count
        self.direct = direct_ok(count)
        if not self.direct:
            self.slots = lax.all_gather(value, "site", axis=0, tiled=False)
            self.sources = jnp.arange(count, dtype=jnp.int32)
            return
        order = list(range(0, count, 2)) + [i for i in range(count - 1, -1, -1) if i % 2 == 1]
        place = [0] * count
        for position, device in enumerate(order):
            place[device] = position
        self.forward = [(order[p], order[(p + 1) % count]) for p in range(count)]
        self.backward = [(order[p], order[(p - 1) % count]) for p in range(count)]
        self.forward_left = count // 2
        self.backward_left = count - 1 - self.forward_left
        offsets = [0] + [-s for s in range(1, self.forward_left + 1)]
        offsets += list(range(1, self.backward_left + 1))
        my_place = jnp.array(place, dtype=jnp.int32)[me]
        self.sources = jnp.array(order, dtype=jnp.int32)[
            (my_place + jnp.array(offsets, dtype=jnp.int32)) % count
        ]
        self.forward_slots = []
        self.backward_slots = []
        self.ahead = value
        self.behind = value
        self.value = value
        self._issue()

    def _issue(self):
        if self.forward_left > 0:
            self.ahead = lax.ppermute(self.ahead, "site", self.forward)
            self.forward_slots.append(self.ahead)
            self.forward_left -= 1
        if self.backward_left > 0:
            self.behind = lax.ppermute(self.behind, "site", self.backward)
            self.backward_slots.append(self.behind)
            self.backward_left -= 1

    def step(self, tied):
        if not self.direct or (self.forward_left == 0 and self.backward_left == 0):
            return tied
        self.ahead, self.behind, tied = lax.optimization_barrier((self.ahead, self.behind, tied))
        self.forward_slots[-1] = self.ahead
        if self.backward_slots:
            self.backward_slots[-1] = self.behind
        self._issue()
        return tied

    def slots_in_arrival(self):
        if not self.direct:
            return [self.slots[i] for i in range(self.count)], [self.sources[i] for i in range(self.count)]
        while self.forward_left > 0 or self.backward_left > 0:
            self._issue()
        slots = [self.value]
        positions = [0]
        forward_count = len(self.forward_slots)
        for step in range(max(forward_count, len(self.backward_slots))):
            if step < forward_count:
                slots.append(self.forward_slots[step])
                positions.append(1 + step)
            if step < len(self.backward_slots):
                slots.append(self.backward_slots[step])
                positions.append(1 + forward_count + step)
        return slots, [self.sources[p] for p in positions]

    def finish(self):
        if not self.direct:
            return self.slots, self.sources
        while self.forward_left > 0 or self.backward_left > 0:
            self._issue()
        slots = [self.value] + self.forward_slots + self.backward_slots
        return jnp.stack(slots), self.sources


def shards(
    acts,
    patches,
    site_tiles,
    site_count,
    q_weight,
    q_gain,
    k_gain,
    tile_in,
    tile_out,
    out_weight,
    ffn_gain,
    gate_weight,
    up_weight,
    down_weight,
):
    group_size = lax.axis_size("site")
    section_count = lax.axis_size("section")
    my_index = lax.axis_index("site")
    sites_here = acts.shape[1]
    list_width = site_tiles.shape[1]
    tiles_here = patches.shape[1]
    head_size = q_gain.shape[1]
    capacity = max(2, 5 * sites_here * list_width // (4 * group_size))
    entries = sites_here * list_width
    current = acts[0]
    model_width = current.shape[-1]
    row_width = patches.shape[-1]

    ring_in = RingGather(tile_in[0], group_size, my_index)
    in_slots, in_sources = ring_in.finish()
    ring_out = RingGather(tile_out[0], group_size, my_index)
    weight_in = in_slots.reshape(-1, in_slots.shape[-1])
    own_rows = jnp.take(patches[0].reshape(tiles_here, group_size, -1), in_sources, axis=1)
    tile_hidden = jax.nn.gelu(
        jnp.dot(own_rows.reshape(tiles_here, -1), weight_in, preferred_element_type=jnp.float32),
        approximate=True,
    ).astype(jnp.bfloat16)
    hidden_width = tile_hidden.shape[-1]

    slot_index = jnp.arange(list_width, dtype=jnp.int32)
    live_all = (slot_index[None, :] < site_count[:, None]).reshape(group_size, entries)
    owner_all = (site_tiles // tiles_here).reshape(group_size, entries)
    local_all = (site_tiles % tiles_here).reshape(group_size, entries)
    mine_mask = jnp.logical_and(live_all, owner_all == my_index)
    slot_rank = jnp.cumsum(mine_mask.astype(jnp.int32), axis=1) - 1
    picks = jnp.logical_and(
        mine_mask[:, :, None],
        slot_rank[:, :, None] == jnp.arange(capacity, dtype=jnp.int32)[None, None, :],
    )
    send_index = jnp.sum(jnp.where(picks, local_all[:, :, None], 0), axis=1)
    send_rows = tile_hidden[send_index.reshape(-1)].reshape(group_size, capacity, hidden_width)
    act_rows = sites_here * model_width // hidden_width
    packed = model_width % hidden_width == 0
    if packed:
        act_block = jnp.broadcast_to(
            current.reshape(1, act_rows, hidden_width), (group_size, act_rows, hidden_width)
        )
        send_rows = jnp.concatenate([send_rows, act_block], axis=1)
    send_rows = ring_out.step(send_rows)
    arrived = lax.all_to_all(send_rows, "site", split_axis=0, concat_axis=0, tiled=True)
    if packed:
        everyone = arrived[:, capacity:].reshape(-1, model_width)
        arrived = arrived[:, :capacity]
    else:
        everyone = doubling_gather(current, group_size, my_index).reshape(-1, model_width)
    q_part = by_rows(everyone, q_weight[0]).astype(jnp.bfloat16)
    q_part = ring_out.step(q_part)
    q_blocks = halving_exchange(
        q_part.reshape(group_size, sites_here, -1), group_size, my_index
    )
    q_blocks = ring_out.step(q_blocks)

    my_tiles = lax.dynamic_slice_in_dim(site_tiles, my_index * sites_here, sites_here, 0)
    my_count = lax.dynamic_slice_in_dim(site_count, my_index * sites_here, sites_here, 0)
    my_live = slot_index[None, :] < my_count[:, None]
    my_owner = (my_tiles // tiles_here).reshape(-1)
    one_hot = jnp.logical_and(
        my_owner[:, None] == jnp.arange(group_size, dtype=jnp.int32)[None, :],
        my_live.reshape(-1)[:, None],
    ).astype(jnp.int32)
    my_rank = jnp.sum(jnp.cumsum(one_hot, axis=0) * one_hot, axis=1) - 1
    fetch_index = jnp.where(my_live.reshape(-1), my_owner * capacity + my_rank, 0)
    pair_hidden = arrived.reshape(group_size * capacity, hidden_width)[fetch_index]

    shard_rows = tile_out.shape[1]
    keyval = None
    if not ring_out.direct:
        out_slots, out_sources = [ring_out.slots.reshape(-1, ring_out.slots.shape[-1])], [0]
        shard_rows = hidden_width
    else:
        out_slots, out_sources = ring_out.slots_in_arrival()
    for slot, source in zip(out_slots, out_sources):
        columns_here = lax.dynamic_slice_in_dim(pair_hidden, source * shard_rows, shard_rows, 1)
        term = jnp.dot(columns_here, slot, preferred_element_type=jnp.float32)
        keyval = term if keyval is None else keyval + term
    half_width = keyval.shape[1] // 2
    normed_keys = head_norm(keyval[:, :half_width], k_gain[0])
    pair_kv = jnp.concatenate([normed_keys, keyval[:, half_width:]], axis=1).astype(jnp.bfloat16)
    pair_kv = pair_kv.reshape(sites_here, list_width, 2, HEADS, head_size)

    my_queries = jnp.moveaxis(q_blocks, 0, 1).reshape(sites_here, -1)
    queries = head_norm(my_queries, q_gain[0]).astype(jnp.bfloat16)
    query_heads = queries.reshape(sites_here, HEADS, head_size)
    scores = jnp.einsum(
        "nhd,nlhd->nhl", query_heads, pair_kv[:, :, 0], preferred_element_type=jnp.float32
    ) / math.sqrt(head_size)
    exponents = jnp.exp(scores) * my_live.astype(jnp.float32)[:, None, :]
    weights = (exponents / jnp.sum(exponents, axis=-1, keepdims=True)).astype(jnp.bfloat16)
    combined = jnp.einsum(
        "nhl,nlhd->nhd", weights, pair_kv[:, :, 1], preferred_element_type=jnp.float32
    )
    combined = combined.reshape(sites_here, -1).astype(jnp.bfloat16)
    column_blocks = jnp.moveaxis(combined.reshape(sites_here, group_size, -1), 1, 0)
    columns = halving_exchange(column_blocks, group_size, my_index).reshape(
        group_size * sites_here, -1
    )
    attn_part = jnp.dot(columns, out_weight[0], preferred_element_type=jnp.float32)
    attn_part = attn_part.reshape(group_size, sites_here, -1)
    if direct_ok(group_size):
        attn_all = doubling_sum(attn_part, group_size)
        residual_all = everyone.reshape(group_size, sites_here, -1).astype(jnp.float32) + attn_all
        residual = lax.dynamic_index_in_dim(residual_all, my_index, 0, keepdims=False)
        normed_rows = rms_norm(residual_all, ffn_gain[0]).astype(jnp.bfloat16)
        normed_rows = normed_rows.reshape(-1, model_width)
    else:
        attn_sum = halving_sum(attn_part, group_size, my_index)
        residual = current.astype(jnp.float32) + attn_sum
        normed = rms_norm(residual, ffn_gain[0]).astype(jnp.bfloat16)
        normed_rows = doubling_gather(normed, group_size, my_index).reshape(-1, model_width)
    gate_sum = by_rows(normed_rows, gate_weight[0])
    up_sum = by_rows(normed_rows, up_weight[0])
    hidden_ffn = (jax.nn.silu(gate_sum) * up_sum).astype(jnp.bfloat16)
    down_part = jnp.dot(hidden_ffn, down_weight[0], preferred_element_type=jnp.float32)
    down_part = down_part.reshape(group_size, sites_here, -1)
    if not direct_ok(group_size) or group_size == 1:
        down_sum = halving_sum(down_part, group_size, my_index)
        output_rows = (residual + down_sum).astype(jnp.bfloat16)
        return lax.ppermute(output_rows[None], "section", shift_pairs(section_count, 1))
    bits = group_size.bit_length() - 1
    rest = down_part.shape[1:]
    state = down_part.reshape((2,) * bits + rest)
    for bit in range(bits):
        axis = bits - 1 - bit
        mine = (my_index >> bit) & 1
        keep = lax.dynamic_index_in_dim(state, mine, axis, keepdims=True)
        send = lax.dynamic_index_in_dim(state, 1 - mine, axis, keepdims=True)
        if bit < bits - 1:
            state = keep + lax.ppermute(send, "site", xor_pairs(group_size, bit))
            continue
        own = keep.reshape(rest) + residual
        forward = [
            (section * group_size + site, ((section + 1) % section_count) * group_size + site)
            for section in range(section_count)
            for site in range(group_size)
        ]
        across = [
            (
                section * group_size + site,
                ((section + 1) % section_count) * group_size + (site ^ (1 << bit)),
            )
            for section in range(section_count)
            for site in range(group_size)
        ]
        mine_part = lax.ppermute(own, ("section", "site"), forward)
        other_part = lax.ppermute(send.reshape(rest), ("section", "site"), across)
        output_rows = (mine_part + other_part).astype(jnp.bfloat16)
    return output_rows[None]


def solution(mesh):
    return jax.shard_map(
        shards,
        mesh=mesh,
        in_specs=(
            P("section", "site", None),
            P("section", "site", None),
            P(),
            P(),
            P("section", "site", None),
            P("section", None),
            P("section", None),
            P("section", "site", None),
            P("section", "site", None),
            P("section", "site", None),
            P("section", None),
            P("section", "site", None),
            P("section", "site", None),
            P("section", "site", None),
        ),
        out_specs=P("section", "site", None),
        check_vma=False,
    )
```

```python
import math

import jax
import jax.numpy as jnp
from jax import lax
from jax.sharding import PartitionSpec as P

HEADS = 16


epsilon = 1e-05

DIRECT_LIMIT = 8


def shift_pairs(count, steps):
    return [(source, (source + steps) % count) for source in range(count)]


def by_rows(left, weight_rows):
    return lax.dot_general(
        left, weight_rows, (((1,), (1,)), ((), ())), preferred_element_type=jnp.float32
    )


def head_norm(values, gain_row):
    shaped = values.astype(jnp.float32).reshape(values.shape[0], -1, gain_row.shape[0])
    scaled = (
        shaped * lax.rsqrt(jnp.mean(shaped * shaped, axis=-1, keepdims=True) + epsilon) * gain_row
    )
    return scaled.reshape(values.shape[0], -1)


def rms_norm(values, gain_row):
    return (
        values * lax.rsqrt(jnp.mean(values * values, axis=-1, keepdims=True) + epsilon) * gain_row
    )


def to_source_order(slots, count, me):
    return jnp.take(slots, (me - jnp.arange(count, dtype=jnp.int32)) % count, axis=0)


def xor_pairs(count, bit):
    return [(source, source ^ (1 << bit)) for source in range(count)]


def direct_ok(count):
    return count <= DIRECT_LIMIT and count & (count - 1) == 0


def site_exchange(by_target, count, me):
    if not direct_ok(count):
        return lax.all_to_all(by_target, "site", split_axis=0, concat_axis=0, tiled=True)
    slots = [lax.dynamic_index_in_dim(by_target, me, 0, keepdims=False)]
    for steps in range(1, count):
        piece = lax.dynamic_index_in_dim(by_target, (me + steps) % count, 0, keepdims=False)
        slots.append(lax.ppermute(piece, "site", shift_pairs(count, steps)))
    return to_source_order(jnp.stack(slots), count, me)


def halving_exchange(by_target, count, me):
    if not direct_ok(count):
        return lax.all_to_all(by_target, "site", split_axis=0, concat_axis=0, tiled=True)
    bits = count.bit_length() - 1
    rest = by_target.shape[1:]
    state = by_target.reshape((2,) * bits + rest)
    for bit in range(bits):
        axis = bits - 1 - bit
        mine = (me >> bit) & 1
        keep = lax.dynamic_index_in_dim(state, mine, axis, keepdims=True)
        send = lax.dynamic_index_in_dim(state, 1 - mine, axis, keepdims=True)
        recv = lax.ppermute(send, "site", xor_pairs(count, bit))
        state = jnp.where(
            mine == 0,
            jnp.concatenate([keep, recv], axis),
            jnp.concatenate([recv, keep], axis),
        )
    return state.reshape((count,) + rest)


def doubling_gather(value, count, me):
    if not direct_ok(count):
        return lax.all_gather(value, "site", axis=0, tiled=False)
    bits = count.bit_length() - 1
    state = value[None]
    for bit in range(bits):
        recv = lax.ppermute(state, "site", xor_pairs(count, bit))
        mine = (me >> bit) & 1
        state = jnp.where(
            mine == 0, jnp.concatenate([state, recv], 0), jnp.concatenate([recv, state], 0)
        )
    return state


def halving_sum(parts, count, me):
    if not direct_ok(count):
        return lax.psum_scatter(parts, "site", scatter_dimension=0, tiled=True)[0]
    bits = count.bit_length() - 1
    rest = parts.shape[1:]
    state = parts.reshape((2,) * bits + rest)
    for bit in range(bits):
        axis = bits - 1 - bit
        mine = (me >> bit) & 1
        keep = lax.dynamic_index_in_dim(state, mine, axis, keepdims=True)
        send = lax.dynamic_index_in_dim(state, 1 - mine, axis, keepdims=True)
        state = keep + lax.ppermute(send, "site", xor_pairs(count, bit))
    return state.reshape(rest)


def doubling_sum(parts, count):
    state = parts
    for bit in range(count.bit_length() - 1):
        state = state + lax.ppermute(state, "site", xor_pairs(count, bit))
    return state


class RingGather:
    def __init__(self, value, count, me):
        self.count = count
        self.direct = direct_ok(count)
        if not self.direct:
            self.slots = lax.all_gather(value, "site", axis=0, tiled=False)
            self.sources = jnp.arange(count, dtype=jnp.int32)
            return
        order = list(range(0, count, 2)) + [i for i in range(count - 1, -1, -1) if i % 2 == 1]
        place = [0] * count
        for position, device in enumerate(order):
            place[device] = position
        self.forward = [(order[p], order[(p + 1) % count]) for p in range(count)]
        self.backward = [(order[p], order[(p - 1) % count]) for p in range(count)]
        self.forward_left = count // 2
        self.backward_left = count - 1 - self.forward_left
        offsets = [0] + [-s for s in range(1, self.forward_left + 1)]
        offsets += list(range(1, self.backward_left + 1))
        my_place = jnp.array(place, dtype=jnp.int32)[me]
        self.sources = jnp.array(order, dtype=jnp.int32)[
            (my_place + jnp.array(offsets, dtype=jnp.int32)) % count
        ]
        self.forward_slots = []
        self.backward_slots = []
        self.ahead = value
        self.behind = value
        self.value = value
        self._issue()

    def _issue(self):
        if self.forward_left > 0:
            self.ahead = lax.ppermute(self.ahead, "site", self.forward)
            self.forward_slots.append(self.ahead)
            self.forward_left -= 1
        if self.backward_left > 0:
            self.behind = lax.ppermute(self.behind, "site", self.backward)
            self.backward_slots.append(self.behind)
            self.backward_left -= 1

    def step(self, tied):
        if not self.direct or (self.forward_left == 0 and self.backward_left == 0):
            return tied
        self.ahead, self.behind, tied = lax.optimization_barrier((self.ahead, self.behind, tied))
        self.forward_slots[-1] = self.ahead
        if self.backward_slots:
            self.backward_slots[-1] = self.behind
        self._issue()
        return tied

    def slots_in_arrival(self):
        if not self.direct:
            return [self.slots[i] for i in range(self.count)], [self.sources[i] for i in range(self.count)]
        while self.forward_left > 0 or self.backward_left > 0:
            self._issue()
        slots = [self.value]
        positions = [0]
        forward_count = len(self.forward_slots)
        for step in range(max(forward_count, len(self.backward_slots))):
            if step < forward_count:
                slots.append(self.forward_slots[step])
                positions.append(1 + step)
            if step < len(self.backward_slots):
                slots.append(self.backward_slots[step])
                positions.append(1 + forward_count + step)
        return slots, [self.sources[p] for p in positions]

    def finish(self):
        if not self.direct:
            return self.slots, self.sources
        while self.forward_left > 0 or self.backward_left > 0:
            self._issue()
        slots = [self.value] + self.forward_slots + self.backward_slots
        return jnp.stack(slots), self.sources


def shards(
    acts,
    patches,
    site_tiles,
    site_count,
    q_weight,
    q_gain,
    k_gain,
    tile_in,
    tile_out,
    out_weight,
    ffn_gain,
    gate_weight,
    up_weight,
    down_weight,
):
    group_size = lax.axis_size("site")
    section_count = lax.axis_size("section")
    my_index = lax.axis_index("site")
    sites_here = acts.shape[1]
    list_width = site_tiles.shape[1]
    tiles_here = patches.shape[1]
    head_size = q_gain.shape[1]
    capacity = max(2, 5 * sites_here * list_width // (4 * group_size))
    entries = sites_here * list_width
    current = acts[0]
    model_width = current.shape[-1]
    row_width = patches.shape[-1]

    ring_in = RingGather(tile_in[0], group_size, my_index)
    in_slots, in_sources = ring_in.finish()
    ring_out = RingGather(tile_out[0], group_size, my_index)
    weight_in = in_slots.reshape(-1, in_slots.shape[-1])
    own_rows = jnp.take(patches[0].reshape(tiles_here, group_size, -1), in_sources, axis=1)
    tile_hidden = jax.nn.gelu(
        jnp.dot(own_rows.reshape(tiles_here, -1), weight_in, preferred_element_type=jnp.float32),
        approximate=True,
    ).astype(jnp.bfloat16)
    hidden_width = tile_hidden.shape[-1]

    slot_index = jnp.arange(list_width, dtype=jnp.int32)
    live_all = (slot_index[None, :] < site_count[:, None]).reshape(group_size, entries)
    owner_all = (site_tiles // tiles_here).reshape(group_size, entries)
    local_all = (site_tiles % tiles_here).reshape(group_size, entries)
    mine_mask = jnp.logical_and(live_all, owner_all == my_index)
    slot_rank = jnp.cumsum(mine_mask.astype(jnp.int32), axis=1) - 1
    picks = jnp.logical_and(
        mine_mask[:, :, None],
        slot_rank[:, :, None] == jnp.arange(capacity, dtype=jnp.int32)[None, None, :],
    )
    send_index = jnp.sum(jnp.where(picks, local_all[:, :, None], 0), axis=1)
    send_rows = tile_hidden[send_index.reshape(-1)].reshape(group_size, capacity, hidden_width)
    act_rows = sites_here * model_width // hidden_width
    packed = model_width % hidden_width == 0
    if packed:
        act_block = jnp.broadcast_to(
            current.reshape(1, act_rows, hidden_width), (group_size, act_rows, hidden_width)
        )
        send_rows = jnp.concatenate([send_rows, act_block], axis=1)
    send_rows = ring_out.step(send_rows)
    arrived = lax.all_to_all(send_rows, "site", split_axis=0, concat_axis=0, tiled=True)
    if packed:
        everyone = arrived[:, capacity:].reshape(-1, model_width)
        arrived = arrived[:, :capacity]
    else:
        everyone = doubling_gather(current, group_size, my_index).reshape(-1, model_width)
    q_part = by_rows(everyone, q_weight[0]).astype(jnp.bfloat16)
    q_part = ring_out.step(q_part)
    q_blocks = halving_exchange(
        q_part.reshape(group_size, sites_here, -1), group_size, my_index
    )
    q_blocks = ring_out.step(q_blocks)

    my_tiles = lax.dynamic_slice_in_dim(site_tiles, my_index * sites_here, sites_here, 0)
    my_count = lax.dynamic_slice_in_dim(site_count, my_index * sites_here, sites_here, 0)
    my_live = slot_index[None, :] < my_count[:, None]
    my_owner = (my_tiles // tiles_here).reshape(-1)
    one_hot = jnp.logical_and(
        my_owner[:, None] == jnp.arange(group_size, dtype=jnp.int32)[None, :],
        my_live.reshape(-1)[:, None],
    ).astype(jnp.int32)
    my_rank = jnp.sum(jnp.cumsum(one_hot, axis=0) * one_hot, axis=1) - 1
    fetch_index = jnp.where(my_live.reshape(-1), my_owner * capacity + my_rank, 0)
    pair_hidden = arrived.reshape(group_size * capacity, hidden_width)[fetch_index]

    shard_rows = tile_out.shape[1]
    keyval = None
    if not ring_out.direct:
        out_slots, out_sources = [ring_out.slots.reshape(-1, ring_out.slots.shape[-1])], [0]
        shard_rows = hidden_width
    else:
        out_slots, out_sources = ring_out.slots_in_arrival()
    for slot, source in zip(out_slots, out_sources):
        columns_here = lax.dynamic_slice_in_dim(pair_hidden, source * shard_rows, shard_rows, 1)
        term = jnp.dot(columns_here, slot, preferred_element_type=jnp.float32)
        keyval = term if keyval is None else keyval + term
    half_width = keyval.shape[1] // 2
    normed_keys = head_norm(keyval[:, :half_width], k_gain[0])
    pair_kv = jnp.concatenate([normed_keys, keyval[:, half_width:]], axis=1).astype(jnp.bfloat16)
    pair_kv = pair_kv.reshape(sites_here, list_width, 2, HEADS, head_size)

    my_queries = jnp.moveaxis(q_blocks, 0, 1).reshape(sites_here, -1)
    queries = head_norm(my_queries, q_gain[0]).astype(jnp.bfloat16)
    query_heads = queries.reshape(sites_here, HEADS, head_size)
    scores = jnp.einsum(
        "nhd,nlhd->nhl", query_heads, pair_kv[:, :, 0], preferred_element_type=jnp.float32
    ) / math.sqrt(head_size)
    exponents = jnp.exp(scores) * my_live.astype(jnp.float32)[:, None, :]
    weights = (exponents / jnp.sum(exponents, axis=-1, keepdims=True)).astype(jnp.bfloat16)
    combined = jnp.einsum(
        "nhl,nlhd->nhd", weights, pair_kv[:, :, 1], preferred_element_type=jnp.float32
    )
    combined = combined.reshape(sites_here, -1).astype(jnp.bfloat16)
    column_blocks = jnp.moveaxis(combined.reshape(sites_here, group_size, -1), 1, 0)
    columns = halving_exchange(column_blocks, group_size, my_index).reshape(
        group_size * sites_here, -1
    )
    attn_part = jnp.dot(columns, out_weight[0], preferred_element_type=jnp.float32)
    attn_part = attn_part.reshape(group_size, sites_here, -1)
    if direct_ok(group_size):
        attn_all = doubling_sum(attn_part, group_size)
        residual_all = everyone.reshape(group_size, sites_here, -1).astype(jnp.float32) + attn_all
        residual = lax.dynamic_index_in_dim(residual_all, my_index, 0, keepdims=False)
        normed_rows = rms_norm(residual_all, ffn_gain[0]).astype(jnp.bfloat16)
        normed_rows = normed_rows.reshape(-1, model_width)
    else:
        attn_sum = halving_sum(attn_part, group_size, my_index)
        residual = current.astype(jnp.float32) + attn_sum
        normed = rms_norm(residual, ffn_gain[0]).astype(jnp.bfloat16)
        normed_rows = doubling_gather(normed, group_size, my_index).reshape(-1, model_width)
    gate_sum = by_rows(normed_rows, gate_weight[0])
    up_sum = by_rows(normed_rows, up_weight[0])
    hidden_ffn = (jax.nn.silu(gate_sum) * up_sum).astype(jnp.bfloat16)
    down_part = jnp.dot(hidden_ffn, down_weight[0], preferred_element_type=jnp.float32)
    down_part = down_part.reshape(group_size, sites_here, -1)
    if not direct_ok(group_size) or group_size == 1:
        down_sum = halving_sum(down_part, group_size, my_index)
        output_rows = (residual + down_sum).astype(jnp.bfloat16)
        return lax.ppermute(output_rows[None], "section", shift_pairs(section_count, 1))
    bits = group_size.bit_length() - 1
    rest = down_part.shape[1:]
    state = down_part.reshape((2,) * bits + rest)
    for bit in range(bits):
        axis = bits - 1 - bit
        mine = (my_index >> bit) & 1
        keep = lax.dynamic_index_in_dim(state, mine, axis, keepdims=True)
        send = lax.dynamic_index_in_dim(state, 1 - mine, axis, keepdims=True)
        if bit < bits - 1:
            state = keep + lax.ppermute(send, "site", xor_pairs(group_size, bit))
            continue
        own = keep.reshape(rest) + residual
        forward = [
            (section * group_size + site, ((section + 1) % section_count) * group_size + site)
            for section in range(section_count)
            for site in range(group_size)
        ]
        across = [
            (
                section * group_size + site,
                ((section + 1) % section_count) * group_size + (site ^ (1 << bit)),
            )
            for section in range(section_count)
            for site in range(group_size)
        ]
        mine_part = lax.ppermute(own, ("section", "site"), forward)
        other_part = lax.ppermute(send.reshape(rest), ("section", "site"), across)
        output_rows = (mine_part + other_part).astype(jnp.bfloat16)
    return output_rows[None]


def heads_split(
    acts,
    patches,
    site_tiles,
    site_count,
    q_weight,
    q_gain,
    k_gain,
    tile_in,
    tile_out,
    out_weight,
    ffn_gain,
    gate_weight,
    up_weight,
    down_weight,
):
    group_size = lax.axis_size("site")
    section_count = lax.axis_size("section")
    my_index = lax.axis_index("site")
    sites_here = acts.shape[1]
    list_width = site_tiles.shape[1]
    tiles_here = patches.shape[1]
    head_size = q_gain.shape[1]
    heads_here = HEADS // group_size
    current = acts[0]
    model_width = current.shape[-1]
    hidden_width = tile_in.shape[-1]
    all_sites = group_size * sites_here

    act_rows = sites_here * model_width // hidden_width
    ring_in = RingGather(
        jnp.concatenate([tile_in[0], current.reshape(act_rows, hidden_width)], axis=0),
        group_size,
        my_index,
    )
    in_slots, in_sources = ring_in.finish()
    in_rows = tile_in.shape[1]
    slot_of_source = jnp.argmax(
        in_sources[None, :] == jnp.arange(group_size, dtype=jnp.int32)[:, None], axis=1
    ).astype(jnp.int32)
    everyone = jnp.take(in_slots[:, in_rows:], slot_of_source, axis=0).reshape(all_sites, model_width)
    weight_in = in_slots[:, :in_rows].reshape(-1, hidden_width)
    own_rows = jnp.take(patches[0].reshape(tiles_here, group_size, -1), in_sources, axis=1)
    tile_hidden = jax.nn.gelu(
        jnp.dot(own_rows.reshape(tiles_here, -1), weight_in, preferred_element_type=jnp.float32),
        approximate=True,
    ).astype(jnp.bfloat16)

    kv_width = tile_out.shape[-1]
    my_cols = heads_here * head_size
    col_blocks = tile_out[0].reshape(tile_out.shape[1], 2, group_size, my_cols)
    col_blocks = jnp.transpose(col_blocks, (2, 0, 1, 3)).reshape(group_size, tile_out.shape[1], 2 * my_cols)
    weight_out = lax.all_to_all(col_blocks, "site", split_axis=0, concat_axis=0, tiled=True)
    weight_out = weight_out.reshape(-1, 2 * my_cols)
    del kv_width

    q_part = by_rows(everyone, q_weight[0]).astype(jnp.bfloat16)
    queries = head_norm(q_part, q_gain[0]).astype(jnp.bfloat16)
    query_heads = queries.reshape(all_sites, heads_here, head_size)

    ring_hidden = RingGather(tile_hidden, group_size, my_index)
    hidden_slots, hidden_sources = ring_hidden.finish()
    hidden_slot_of_source = jnp.argmax(
        hidden_sources[None, :] == jnp.arange(group_size, dtype=jnp.int32)[:, None], axis=1
    ).astype(jnp.int32)
    slot_kv = []
    for slot in range(group_size):
        keyval = jnp.dot(hidden_slots[slot], weight_out, preferred_element_type=jnp.float32)
        normed_keys = head_norm(keyval[:, :my_cols], k_gain[0])
        slot_kv.append(
            jnp.concatenate([normed_keys, keyval[:, my_cols:]], axis=1).astype(jnp.bfloat16)
        )
    table = jnp.stack(slot_kv).reshape(group_size * tiles_here, 2 * my_cols)
    owner = site_tiles // tiles_here
    rows = jnp.take(hidden_slot_of_source, owner) * tiles_here + site_tiles % tiles_here
    pair_kv = table[rows.reshape(-1)].reshape(all_sites, list_width, 2, heads_here, head_size)

    slot_index = jnp.arange(list_width, dtype=jnp.int32)
    live = (slot_index[None, :] < site_count[:, None]).astype(jnp.float32)
    scores = jnp.einsum(
        "nhd,nlhd->nhl", query_heads, pair_kv[:, :, 0], preferred_element_type=jnp.float32
    ) / math.sqrt(head_size)
    exponents = jnp.exp(scores) * live[:, None, :]
    weights = (exponents / jnp.sum(exponents, axis=-1, keepdims=True)).astype(jnp.bfloat16)
    combined = jnp.einsum(
        "nhl,nlhd->nhd", weights, pair_kv[:, :, 1], preferred_element_type=jnp.float32
    )
    combined = combined.reshape(all_sites, my_cols).astype(jnp.bfloat16)
    attn_part = jnp.dot(combined, out_weight[0], preferred_element_type=jnp.float32)
    attn_all = doubling_sum(attn_part.reshape(group_size, sites_here, -1), group_size)
    residual_all = everyone.reshape(group_size, sites_here, -1).astype(jnp.float32) + attn_all
    residual = lax.dynamic_index_in_dim(residual_all, my_index, 0, keepdims=False)
    normed_rows = rms_norm(residual_all, ffn_gain[0]).astype(jnp.bfloat16).reshape(-1, model_width)
    gate_sum = by_rows(normed_rows, gate_weight[0])
    up_sum = by_rows(normed_rows, up_weight[0])
    hidden_ffn = (jax.nn.silu(gate_sum) * up_sum).astype(jnp.bfloat16)
    down_part = jnp.dot(hidden_ffn, down_weight[0], preferred_element_type=jnp.float32)
    down_part = down_part.reshape(group_size, sites_here, -1)
    return last_round(down_part, residual, group_size, section_count, my_index)


def last_round(down_part, residual, group_size, section_count, my_index):
    bits = group_size.bit_length() - 1
    rest = down_part.shape[1:]
    state = down_part.reshape((2,) * bits + rest)
    for bit in range(bits):
        axis = bits - 1 - bit
        mine = (my_index >> bit) & 1
        keep = lax.dynamic_index_in_dim(state, mine, axis, keepdims=True)
        send = lax.dynamic_index_in_dim(state, 1 - mine, axis, keepdims=True)
        if bit < bits - 1:
            state = keep + lax.ppermute(send, "site", xor_pairs(group_size, bit))
            continue
        own = keep.reshape(rest) + residual
        forward = [
            (section * group_size + site, ((section + 1) % section_count) * group_size + site)
            for section in range(section_count)
            for site in range(group_size)
        ]
        across = [
            (
                section * group_size + site,
                ((section + 1) % section_count) * group_size + (site ^ (1 << bit)),
            )
            for section in range(section_count)
            for site in range(group_size)
        ]
        mine_part = lax.ppermute(own, ("section", "site"), forward)
        other_part = lax.ppermute(send.reshape(rest), ("section", "site"), across)
        return (mine_part + other_part).astype(jnp.bfloat16)[None]


def solution(mesh):
    group_size = mesh.shape["site"]
    split_heads = (
        direct_ok(group_size)
        and group_size > 1
        and HEADS % group_size == 0
        and mesh.shape["section"] > 0
    )
    return jax.shard_map(
        heads_split if split_heads else shards,
        mesh=mesh,
        in_specs=(
            P("section", "site", None),
            P("section", "site", None),
            P(),
            P(),
            P("section", "site", None),
            P("section", None),
            P("section", None),
            P("section", "site", None),
            P("section", "site", None),
            P("section", "site", None),
            P("section", None),
            P("section", "site", None),
            P("section", "site", None),
            P("section", "site", None),
        ),
        out_specs=P("section", "site", None),
        check_vma=False,
    )
```

```python
import math

import jax
import jax.numpy as jnp
from jax import lax
from jax.sharding import PartitionSpec as P

HEADS = 16


epsilon = 1e-05

DIRECT_LIMIT = 8


def shift_pairs(count, steps):
    return [(source, (source + steps) % count) for source in range(count)]


def by_rows(left, weight_rows):
    return lax.dot_general(
        left, weight_rows, (((1,), (1,)), ((), ())), preferred_element_type=jnp.float32
    )


def head_norm(values, gain_row):
    shaped = values.astype(jnp.float32).reshape(values.shape[0], -1, gain_row.shape[0])
    scaled = (
        shaped * lax.rsqrt(jnp.mean(shaped * shaped, axis=-1, keepdims=True) + epsilon) * gain_row
    )
    return scaled.reshape(values.shape[0], -1)


def rms_norm(values, gain_row):
    return (
        values * lax.rsqrt(jnp.mean(values * values, axis=-1, keepdims=True) + epsilon) * gain_row
    )


def to_source_order(slots, count, me):
    return jnp.take(slots, (me - jnp.arange(count, dtype=jnp.int32)) % count, axis=0)


def xor_pairs(count, bit):
    return [(source, source ^ (1 << bit)) for source in range(count)]


def direct_ok(count):
    return count <= DIRECT_LIMIT and count & (count - 1) == 0


def site_exchange(by_target, count, me):
    if not direct_ok(count):
        return lax.all_to_all(by_target, "site", split_axis=0, concat_axis=0, tiled=True)
    slots = [lax.dynamic_index_in_dim(by_target, me, 0, keepdims=False)]
    for steps in range(1, count):
        piece = lax.dynamic_index_in_dim(by_target, (me + steps) % count, 0, keepdims=False)
        slots.append(lax.ppermute(piece, "site", shift_pairs(count, steps)))
    return to_source_order(jnp.stack(slots), count, me)


def halving_exchange(by_target, count, me):
    if not direct_ok(count):
        return lax.all_to_all(by_target, "site", split_axis=0, concat_axis=0, tiled=True)
    bits = count.bit_length() - 1
    rest = by_target.shape[1:]
    state = by_target.reshape((2,) * bits + rest)
    for bit in range(bits):
        axis = bits - 1 - bit
        mine = (me >> bit) & 1
        keep = lax.dynamic_index_in_dim(state, mine, axis, keepdims=True)
        send = lax.dynamic_index_in_dim(state, 1 - mine, axis, keepdims=True)
        recv = lax.ppermute(send, "site", xor_pairs(count, bit))
        state = jnp.where(
            mine == 0,
            jnp.concatenate([keep, recv], axis),
            jnp.concatenate([recv, keep], axis),
        )
    return state.reshape((count,) + rest)


def doubling_gather(value, count, me):
    if not direct_ok(count):
        return lax.all_gather(value, "site", axis=0, tiled=False)
    bits = count.bit_length() - 1
    state = value[None]
    for bit in range(bits):
        recv = lax.ppermute(state, "site", xor_pairs(count, bit))
        mine = (me >> bit) & 1
        state = jnp.where(
            mine == 0, jnp.concatenate([state, recv], 0), jnp.concatenate([recv, state], 0)
        )
    return state


def halving_sum(parts, count, me):
    if not direct_ok(count):
        return lax.psum_scatter(parts, "site", scatter_dimension=0, tiled=True)[0]
    bits = count.bit_length() - 1
    rest = parts.shape[1:]
    state = parts.reshape((2,) * bits + rest)
    for bit in range(bits):
        axis = bits - 1 - bit
        mine = (me >> bit) & 1
        keep = lax.dynamic_index_in_dim(state, mine, axis, keepdims=True)
        send = lax.dynamic_index_in_dim(state, 1 - mine, axis, keepdims=True)
        state = keep + lax.ppermute(send, "site", xor_pairs(count, bit))
    return state.reshape(rest)


def doubling_sum(parts, count):
    state = parts
    for bit in range(count.bit_length() - 1):
        state = state + lax.ppermute(state, "site", xor_pairs(count, bit))
    return state


class RingGather:
    def __init__(self, value, count, me):
        self.count = count
        self.direct = direct_ok(count)
        if not self.direct:
            self.slots = lax.all_gather(value, "site", axis=0, tiled=False)
            self.sources = jnp.arange(count, dtype=jnp.int32)
            return
        order = list(range(0, count, 2)) + [i for i in range(count - 1, -1, -1) if i % 2 == 1]
        place = [0] * count
        for position, device in enumerate(order):
            place[device] = position
        self.forward = [(order[p], order[(p + 1) % count]) for p in range(count)]
        self.backward = [(order[p], order[(p - 1) % count]) for p in range(count)]
        self.forward_left = count // 2
        self.backward_left = count - 1 - self.forward_left
        offsets = [0] + [-s for s in range(1, self.forward_left + 1)]
        offsets += list(range(1, self.backward_left + 1))
        my_place = jnp.array(place, dtype=jnp.int32)[me]
        self.sources = jnp.array(order, dtype=jnp.int32)[
            (my_place + jnp.array(offsets, dtype=jnp.int32)) % count
        ]
        self.forward_slots = []
        self.backward_slots = []
        self.ahead = value
        self.behind = value
        self.value = value
        self._issue()

    def _issue(self):
        if self.forward_left > 0:
            self.ahead = lax.ppermute(self.ahead, "site", self.forward)
            self.forward_slots.append(self.ahead)
            self.forward_left -= 1
        if self.backward_left > 0:
            self.behind = lax.ppermute(self.behind, "site", self.backward)
            self.backward_slots.append(self.behind)
            self.backward_left -= 1

    def step(self, tied):
        if not self.direct or (self.forward_left == 0 and self.backward_left == 0):
            return tied
        self.ahead, self.behind, tied = lax.optimization_barrier((self.ahead, self.behind, tied))
        self.forward_slots[-1] = self.ahead
        if self.backward_slots:
            self.backward_slots[-1] = self.behind
        self._issue()
        return tied

    def slots_in_arrival(self):
        if not self.direct:
            return [self.slots[i] for i in range(self.count)], [self.sources[i] for i in range(self.count)]
        while self.forward_left > 0 or self.backward_left > 0:
            self._issue()
        slots = [self.value]
        positions = [0]
        forward_count = len(self.forward_slots)
        for step in range(max(forward_count, len(self.backward_slots))):
            if step < forward_count:
                slots.append(self.forward_slots[step])
                positions.append(1 + step)
            if step < len(self.backward_slots):
                slots.append(self.backward_slots[step])
                positions.append(1 + forward_count + step)
        return slots, [self.sources[p] for p in positions]

    def finish(self):
        if not self.direct:
            return self.slots, self.sources
        while self.forward_left > 0 or self.backward_left > 0:
            self._issue()
        slots = [self.value] + self.forward_slots + self.backward_slots
        return jnp.stack(slots), self.sources


def shards(
    acts,
    patches,
    site_tiles,
    site_count,
    q_weight,
    q_gain,
    k_gain,
    tile_in,
    tile_out,
    out_weight,
    ffn_gain,
    gate_weight,
    up_weight,
    down_weight,
):
    group_size = lax.axis_size("site")
    section_count = lax.axis_size("section")
    my_index = lax.axis_index("site")
    sites_here = acts.shape[1]
    list_width = site_tiles.shape[1]
    tiles_here = patches.shape[1]
    head_size = q_gain.shape[1]
    capacity = max(2, 5 * sites_here * list_width // (4 * group_size))
    entries = sites_here * list_width
    current = acts[0]
    model_width = current.shape[-1]
    row_width = patches.shape[-1]

    ring_in = RingGather(tile_in[0], group_size, my_index)
    in_slots, in_sources = ring_in.finish()
    ring_out = RingGather(tile_out[0], group_size, my_index)
    weight_in = in_slots.reshape(-1, in_slots.shape[-1])
    own_rows = jnp.take(patches[0].reshape(tiles_here, group_size, -1), in_sources, axis=1)
    tile_hidden = jax.nn.gelu(
        jnp.dot(own_rows.reshape(tiles_here, -1), weight_in, preferred_element_type=jnp.float32),
        approximate=True,
    ).astype(jnp.bfloat16)
    hidden_width = tile_hidden.shape[-1]

    slot_index = jnp.arange(list_width, dtype=jnp.int32)
    live_all = (slot_index[None, :] < site_count[:, None]).reshape(group_size, entries)
    owner_all = (site_tiles // tiles_here).reshape(group_size, entries)
    local_all = (site_tiles % tiles_here).reshape(group_size, entries)
    mine_mask = jnp.logical_and(live_all, owner_all == my_index)
    slot_rank = jnp.cumsum(mine_mask.astype(jnp.int32), axis=1) - 1
    picks = jnp.logical_and(
        mine_mask[:, :, None],
        slot_rank[:, :, None] == jnp.arange(capacity, dtype=jnp.int32)[None, None, :],
    )
    send_index = jnp.sum(jnp.where(picks, local_all[:, :, None], 0), axis=1)
    send_rows = tile_hidden[send_index.reshape(-1)].reshape(group_size, capacity, hidden_width)
    act_rows = sites_here * model_width // hidden_width
    packed = model_width % hidden_width == 0
    if packed:
        act_block = jnp.broadcast_to(
            current.reshape(1, act_rows, hidden_width), (group_size, act_rows, hidden_width)
        )
        send_rows = jnp.concatenate([send_rows, act_block], axis=1)
    send_rows = ring_out.step(send_rows)
    arrived = lax.all_to_all(send_rows, "site", split_axis=0, concat_axis=0, tiled=True)
    if packed:
        everyone = arrived[:, capacity:].reshape(-1, model_width)
        arrived = arrived[:, :capacity]
    else:
        everyone = doubling_gather(current, group_size, my_index).reshape(-1, model_width)
    q_part = by_rows(everyone, q_weight[0]).astype(jnp.bfloat16)
    q_part = ring_out.step(q_part)
    q_blocks = halving_exchange(
        q_part.reshape(group_size, sites_here, -1), group_size, my_index
    )
    q_blocks = ring_out.step(q_blocks)

    my_tiles = lax.dynamic_slice_in_dim(site_tiles, my_index * sites_here, sites_here, 0)
    my_count = lax.dynamic_slice_in_dim(site_count, my_index * sites_here, sites_here, 0)
    my_live = slot_index[None, :] < my_count[:, None]
    my_owner = (my_tiles // tiles_here).reshape(-1)
    one_hot = jnp.logical_and(
        my_owner[:, None] == jnp.arange(group_size, dtype=jnp.int32)[None, :],
        my_live.reshape(-1)[:, None],
    ).astype(jnp.int32)
    my_rank = jnp.sum(jnp.cumsum(one_hot, axis=0) * one_hot, axis=1) - 1
    fetch_index = jnp.where(my_live.reshape(-1), my_owner * capacity + my_rank, 0)
    pair_hidden = arrived.reshape(group_size * capacity, hidden_width)[fetch_index]

    shard_rows = tile_out.shape[1]
    keyval = None
    if not ring_out.direct:
        out_slots, out_sources = [ring_out.slots.reshape(-1, ring_out.slots.shape[-1])], [0]
        shard_rows = hidden_width
    else:
        out_slots, out_sources = ring_out.slots_in_arrival()
    for slot, source in zip(out_slots, out_sources):
        columns_here = lax.dynamic_slice_in_dim(pair_hidden, source * shard_rows, shard_rows, 1)
        term = jnp.dot(columns_here, slot, preferred_element_type=jnp.float32)
        keyval = term if keyval is None else keyval + term
    half_width = keyval.shape[1] // 2
    normed_keys = head_norm(keyval[:, :half_width], k_gain[0])
    pair_kv = jnp.concatenate([normed_keys, keyval[:, half_width:]], axis=1).astype(jnp.bfloat16)
    pair_kv = pair_kv.reshape(sites_here, list_width, 2, HEADS, head_size)

    my_queries = jnp.moveaxis(q_blocks, 0, 1).reshape(sites_here, -1)
    queries = head_norm(my_queries, q_gain[0]).astype(jnp.bfloat16)
    query_heads = queries.reshape(sites_here, HEADS, head_size)
    scores = jnp.einsum(
        "nhd,nlhd->nhl", query_heads, pair_kv[:, :, 0], preferred_element_type=jnp.float32
    ) / math.sqrt(head_size)
    exponents = jnp.exp(scores) * my_live.astype(jnp.float32)[:, None, :]
    weights = (exponents / jnp.sum(exponents, axis=-1, keepdims=True)).astype(jnp.bfloat16)
    combined = jnp.einsum(
        "nhl,nlhd->nhd", weights, pair_kv[:, :, 1], preferred_element_type=jnp.float32
    )
    combined = combined.reshape(sites_here, -1).astype(jnp.bfloat16)
    column_blocks = jnp.moveaxis(combined.reshape(sites_here, group_size, -1), 1, 0)
    columns = halving_exchange(column_blocks, group_size, my_index).reshape(
        group_size * sites_here, -1
    )
    attn_part = jnp.dot(columns, out_weight[0], preferred_element_type=jnp.float32)
    attn_part = attn_part.reshape(group_size, sites_here, -1)
    if direct_ok(group_size):
        attn_all = doubling_sum(attn_part, group_size)
        residual_all = everyone.reshape(group_size, sites_here, -1).astype(jnp.float32) + attn_all
        residual = lax.dynamic_index_in_dim(residual_all, my_index, 0, keepdims=False)
        normed_rows = rms_norm(residual_all, ffn_gain[0]).astype(jnp.bfloat16)
        normed_rows = normed_rows.reshape(-1, model_width)
    else:
        attn_sum = halving_sum(attn_part, group_size, my_index)
        residual = current.astype(jnp.float32) + attn_sum
        normed = rms_norm(residual, ffn_gain[0]).astype(jnp.bfloat16)
        normed_rows = doubling_gather(normed, group_size, my_index).reshape(-1, model_width)
    gate_sum = by_rows(normed_rows, gate_weight[0])
    up_sum = by_rows(normed_rows, up_weight[0])
    hidden_ffn = (jax.nn.silu(gate_sum) * up_sum).astype(jnp.bfloat16)
    down_part = jnp.dot(hidden_ffn, down_weight[0], preferred_element_type=jnp.float32)
    down_part = down_part.reshape(group_size, sites_here, -1)
    if not direct_ok(group_size) or group_size == 1:
        down_sum = halving_sum(down_part, group_size, my_index)
        output_rows = (residual + down_sum).astype(jnp.bfloat16)
        return lax.ppermute(output_rows[None], "section", shift_pairs(section_count, 1))
    bits = group_size.bit_length() - 1
    rest = down_part.shape[1:]
    state = down_part.reshape((2,) * bits + rest)
    for bit in range(bits):
        axis = bits - 1 - bit
        mine = (my_index >> bit) & 1
        keep = lax.dynamic_index_in_dim(state, mine, axis, keepdims=True)
        send = lax.dynamic_index_in_dim(state, 1 - mine, axis, keepdims=True)
        if bit < bits - 1:
            state = keep + lax.ppermute(send, "site", xor_pairs(group_size, bit))
            continue
        own = keep.reshape(rest) + residual
        forward = [
            (section * group_size + site, ((section + 1) % section_count) * group_size + site)
            for section in range(section_count)
            for site in range(group_size)
        ]
        across = [
            (
                section * group_size + site,
                ((section + 1) % section_count) * group_size + (site ^ (1 << bit)),
            )
            for section in range(section_count)
            for site in range(group_size)
        ]
        mine_part = lax.ppermute(own, ("section", "site"), forward)
        other_part = lax.ppermute(send.reshape(rest), ("section", "site"), across)
        output_rows = (mine_part + other_part).astype(jnp.bfloat16)
    return output_rows[None]


def heads_split(
    acts,
    patches,
    site_tiles,
    site_count,
    q_weight,
    q_gain,
    k_gain,
    tile_in,
    tile_out,
    out_weight,
    ffn_gain,
    gate_weight,
    up_weight,
    down_weight,
):
    group_size = lax.axis_size("site")
    section_count = lax.axis_size("section")
    my_index = lax.axis_index("site")
    sites_here = acts.shape[1]
    list_width = site_tiles.shape[1]
    tiles_here = patches.shape[1]
    head_size = q_gain.shape[1]
    heads_here = HEADS // group_size
    current = acts[0]
    model_width = current.shape[-1]
    hidden_width = tile_in.shape[-1]
    all_sites = group_size * sites_here

    act_rows = sites_here * model_width // hidden_width
    ring_in = RingGather(
        jnp.concatenate([tile_in[0], current.reshape(act_rows, hidden_width)], axis=0),
        group_size,
        my_index,
    )
    in_slots, in_sources = ring_in.finish()
    in_rows = tile_in.shape[1]
    slot_of_source = jnp.argmax(
        in_sources[None, :] == jnp.arange(group_size, dtype=jnp.int32)[:, None], axis=1
    ).astype(jnp.int32)
    everyone = jnp.take(in_slots[:, in_rows:], slot_of_source, axis=0).reshape(all_sites, model_width)
    weight_in = in_slots[:, :in_rows].reshape(-1, hidden_width)
    own_rows = jnp.take(patches[0].reshape(tiles_here, group_size, -1), in_sources, axis=1)
    tile_hidden = jax.nn.gelu(
        jnp.dot(own_rows.reshape(tiles_here, -1), weight_in, preferred_element_type=jnp.float32),
        approximate=True,
    ).astype(jnp.bfloat16)

    kv_width = tile_out.shape[-1]
    my_cols = heads_here * head_size
    col_blocks = tile_out[0].reshape(tile_out.shape[1], 2, group_size, my_cols)
    col_blocks = jnp.transpose(col_blocks, (2, 0, 1, 3)).reshape(group_size, tile_out.shape[1], 2 * my_cols)
    weight_out = lax.all_to_all(col_blocks, "site", split_axis=0, concat_axis=0, tiled=True)
    weight_out = weight_out.reshape(-1, 2 * my_cols)
    del kv_width

    q_part = by_rows(everyone, q_weight[0]).astype(jnp.bfloat16)
    queries = head_norm(q_part, q_gain[0]).astype(jnp.bfloat16)
    query_heads = queries.reshape(all_sites, heads_here, head_size)

    ring_hidden = RingGather(tile_hidden, group_size, my_index)
    hidden_slots, hidden_sources = ring_hidden.finish()
    table_hidden = hidden_slots.reshape(group_size * tiles_here, hidden_width)
    keyval = jnp.dot(table_hidden, weight_out, preferred_element_type=jnp.float32)
    normed_keys = head_norm(keyval[:, :my_cols], k_gain[0])
    table = jnp.concatenate([normed_keys, keyval[:, my_cols:]], axis=1).astype(jnp.bfloat16)
    table = table.reshape(group_size * tiles_here, 2, heads_here, head_size)

    tile_of_row = (
        hidden_sources[:, None] * tiles_here + jnp.arange(tiles_here, dtype=jnp.int32)[None, :]
    ).reshape(-1)
    slot_index = jnp.arange(list_width, dtype=jnp.int32)
    live = slot_index[None, :] < site_count[:, None]
    named = jnp.logical_and(
        site_tiles[:, :, None] == tile_of_row[None, None, :], live[:, :, None]
    )
    uses = jnp.sum(named.astype(jnp.float32), axis=1)
    scores = jnp.einsum(
        "nhd,rhd->nhr", query_heads, table[:, 0], preferred_element_type=jnp.float32
    ) / math.sqrt(head_size)
    exponents = jnp.exp(scores) * uses[:, None, :]
    weights = (exponents / jnp.sum(exponents, axis=-1, keepdims=True)).astype(jnp.bfloat16)
    combined = jnp.einsum(
        "nhr,rhd->nhd", weights, table[:, 1], preferred_element_type=jnp.float32
    )
    combined = combined.reshape(all_sites, my_cols).astype(jnp.bfloat16)
    attn_part = jnp.dot(combined, out_weight[0], preferred_element_type=jnp.float32)
    attn_all = doubling_sum(attn_part.reshape(group_size, sites_here, -1), group_size)
    residual_all = everyone.reshape(group_size, sites_here, -1).astype(jnp.float32) + attn_all
    residual = lax.dynamic_index_in_dim(residual_all, my_index, 0, keepdims=False)
    normed_rows = rms_norm(residual_all, ffn_gain[0]).astype(jnp.bfloat16).reshape(-1, model_width)
    gate_sum = by_rows(normed_rows, gate_weight[0])
    up_sum = by_rows(normed_rows, up_weight[0])
    hidden_ffn = (jax.nn.silu(gate_sum) * up_sum).astype(jnp.bfloat16)
    down_part = jnp.dot(hidden_ffn, down_weight[0], preferred_element_type=jnp.float32)
    down_part = down_part.reshape(group_size, sites_here, -1)
    return last_round(down_part, residual, group_size, section_count, my_index)


def last_round(down_part, residual, group_size, section_count, my_index):
    bits = group_size.bit_length() - 1
    rest = down_part.shape[1:]
    state = down_part.reshape((2,) * bits + rest)
    for bit in range(bits):
        axis = bits - 1 - bit
        mine = (my_index >> bit) & 1
        keep = lax.dynamic_index_in_dim(state, mine, axis, keepdims=True)
        send = lax.dynamic_index_in_dim(state, 1 - mine, axis, keepdims=True)
        if bit < bits - 1:
            state = keep + lax.ppermute(send, "site", xor_pairs(group_size, bit))
            continue
        own = keep.reshape(rest) + residual
        forward = [
            (section * group_size + site, ((section + 1) % section_count) * group_size + site)
            for section in range(section_count)
            for site in range(group_size)
        ]
        across = [
            (
                section * group_size + site,
                ((section + 1) % section_count) * group_size + (site ^ (1 << bit)),
            )
            for section in range(section_count)
            for site in range(group_size)
        ]
        mine_part = lax.ppermute(own, ("section", "site"), forward)
        other_part = lax.ppermute(send.reshape(rest), ("section", "site"), across)
        return (mine_part + other_part).astype(jnp.bfloat16)[None]


def solution(mesh):
    group_size = mesh.shape["site"]
    split_heads = (
        direct_ok(group_size)
        and group_size > 1
        and HEADS % group_size == 0
        and mesh.shape["section"] > 0
    )
    return jax.shard_map(
        heads_split if split_heads else shards,
        mesh=mesh,
        in_specs=(
            P("section", "site", None),
            P("section", "site", None),
            P(),
            P(),
            P("section", "site", None),
            P("section", None),
            P("section", None),
            P("section", "site", None),
            P("section", "site", None),
            P("section", "site", None),
            P("section", None),
            P("section", "site", None),
            P("section", "site", None),
            P("section", "site", None),
        ),
        out_specs=P("section", "site", None),
        check_vma=False,
    )
```

```python
import math

import jax
import jax.numpy as jnp
from jax import lax
from jax.sharding import PartitionSpec as P

HEADS = 16


epsilon = 1e-05

DIRECT_LIMIT = 8


def shift_pairs(count, steps):
    return [(source, (source + steps) % count) for source in range(count)]


def by_rows(left, weight_rows):
    return lax.dot_general(
        left, weight_rows, (((1,), (1,)), ((), ())), preferred_element_type=jnp.float32
    )


def head_norm(values, gain_row):
    shaped = values.astype(jnp.float32).reshape(values.shape[0], -1, gain_row.shape[0])
    scaled = (
        shaped * lax.rsqrt(jnp.mean(shaped * shaped, axis=-1, keepdims=True) + epsilon) * gain_row
    )
    return scaled.reshape(values.shape[0], -1)


def rms_norm(values, gain_row):
    return (
        values * lax.rsqrt(jnp.mean(values * values, axis=-1, keepdims=True) + epsilon) * gain_row
    )


def to_source_order(slots, count, me):
    return jnp.take(slots, (me - jnp.arange(count, dtype=jnp.int32)) % count, axis=0)


def xor_pairs(count, bit):
    return [(source, source ^ (1 << bit)) for source in range(count)]


def direct_ok(count):
    return count <= DIRECT_LIMIT and count & (count - 1) == 0


def site_exchange(by_target, count, me):
    if not direct_ok(count):
        return lax.all_to_all(by_target, "site", split_axis=0, concat_axis=0, tiled=True)
    slots = [lax.dynamic_index_in_dim(by_target, me, 0, keepdims=False)]
    for steps in range(1, count):
        piece = lax.dynamic_index_in_dim(by_target, (me + steps) % count, 0, keepdims=False)
        slots.append(lax.ppermute(piece, "site", shift_pairs(count, steps)))
    return to_source_order(jnp.stack(slots), count, me)


def halving_exchange(by_target, count, me):
    if not direct_ok(count):
        return lax.all_to_all(by_target, "site", split_axis=0, concat_axis=0, tiled=True)
    bits = count.bit_length() - 1
    rest = by_target.shape[1:]
    state = by_target.reshape((2,) * bits + rest)
    for bit in range(bits):
        axis = bits - 1 - bit
        mine = (me >> bit) & 1
        keep = lax.dynamic_index_in_dim(state, mine, axis, keepdims=True)
        send = lax.dynamic_index_in_dim(state, 1 - mine, axis, keepdims=True)
        recv = lax.ppermute(send, "site", xor_pairs(count, bit))
        state = jnp.where(
            mine == 0,
            jnp.concatenate([keep, recv], axis),
            jnp.concatenate([recv, keep], axis),
        )
    return state.reshape((count,) + rest)


def doubling_gather(value, count, me):
    if not direct_ok(count):
        return lax.all_gather(value, "site", axis=0, tiled=False)
    bits = count.bit_length() - 1
    state = value[None]
    for bit in range(bits):
        recv = lax.ppermute(state, "site", xor_pairs(count, bit))
        mine = (me >> bit) & 1
        state = jnp.where(
            mine == 0, jnp.concatenate([state, recv], 0), jnp.concatenate([recv, state], 0)
        )
    return state


def halving_sum(parts, count, me):
    if not direct_ok(count):
        return lax.psum_scatter(parts, "site", scatter_dimension=0, tiled=True)[0]
    bits = count.bit_length() - 1
    rest = parts.shape[1:]
    state = parts.reshape((2,) * bits + rest)
    for bit in range(bits):
        axis = bits - 1 - bit
        mine = (me >> bit) & 1
        keep = lax.dynamic_index_in_dim(state, mine, axis, keepdims=True)
        send = lax.dynamic_index_in_dim(state, 1 - mine, axis, keepdims=True)
        state = keep + lax.ppermute(send, "site", xor_pairs(count, bit))
    return state.reshape(rest)


def doubling_sum(parts, count):
    state = parts
    for bit in range(count.bit_length() - 1):
        state = state + lax.ppermute(state, "site", xor_pairs(count, bit))
    return state


class RingGather:
    def __init__(self, value, count, me):
        self.count = count
        self.direct = direct_ok(count)
        if not self.direct:
            self.slots = lax.all_gather(value, "site", axis=0, tiled=False)
            self.sources = jnp.arange(count, dtype=jnp.int32)
            return
        order = list(range(0, count, 2)) + [i for i in range(count - 1, -1, -1) if i % 2 == 1]
        place = [0] * count
        for position, device in enumerate(order):
            place[device] = position
        self.forward = [(order[p], order[(p + 1) % count]) for p in range(count)]
        self.backward = [(order[p], order[(p - 1) % count]) for p in range(count)]
        self.forward_left = count // 2
        self.backward_left = count - 1 - self.forward_left
        offsets = [0] + [-s for s in range(1, self.forward_left + 1)]
        offsets += list(range(1, self.backward_left + 1))
        my_place = jnp.array(place, dtype=jnp.int32)[me]
        self.sources = jnp.array(order, dtype=jnp.int32)[
            (my_place + jnp.array(offsets, dtype=jnp.int32)) % count
        ]
        self.forward_slots = []
        self.backward_slots = []
        self.ahead = value
        self.behind = value
        self.value = value
        self._issue()

    def _issue(self):
        if self.forward_left > 0:
            self.ahead = lax.ppermute(self.ahead, "site", self.forward)
            self.forward_slots.append(self.ahead)
            self.forward_left -= 1
        if self.backward_left > 0:
            self.behind = lax.ppermute(self.behind, "site", self.backward)
            self.backward_slots.append(self.behind)
            self.backward_left -= 1

    def step(self, tied):
        if not self.direct or (self.forward_left == 0 and self.backward_left == 0):
            return tied
        self.ahead, self.behind, tied = lax.optimization_barrier((self.ahead, self.behind, tied))
        self.forward_slots[-1] = self.ahead
        if self.backward_slots:
            self.backward_slots[-1] = self.behind
        self._issue()
        return tied

    def slots_in_arrival(self):
        if not self.direct:
            return [self.slots[i] for i in range(self.count)], [self.sources[i] for i in range(self.count)]
        while self.forward_left > 0 or self.backward_left > 0:
            self._issue()
        slots = [self.value]
        positions = [0]
        forward_count = len(self.forward_slots)
        for step in range(max(forward_count, len(self.backward_slots))):
            if step < forward_count:
                slots.append(self.forward_slots[step])
                positions.append(1 + step)
            if step < len(self.backward_slots):
                slots.append(self.backward_slots[step])
                positions.append(1 + forward_count + step)
        return slots, [self.sources[p] for p in positions]

    def finish(self):
        if not self.direct:
            return self.slots, self.sources
        while self.forward_left > 0 or self.backward_left > 0:
            self._issue()
        slots = [self.value] + self.forward_slots + self.backward_slots
        return jnp.stack(slots), self.sources


def shards(
    acts,
    patches,
    site_tiles,
    site_count,
    q_weight,
    q_gain,
    k_gain,
    tile_in,
    tile_out,
    out_weight,
    ffn_gain,
    gate_weight,
    up_weight,
    down_weight,
):
    group_size = lax.axis_size("site")
    section_count = lax.axis_size("section")
    my_index = lax.axis_index("site")
    sites_here = acts.shape[1]
    list_width = site_tiles.shape[1]
    tiles_here = patches.shape[1]
    head_size = q_gain.shape[1]
    capacity = max(2, 5 * sites_here * list_width // (4 * group_size))
    entries = sites_here * list_width
    current = acts[0]
    model_width = current.shape[-1]
    row_width = patches.shape[-1]

    ring_in = RingGather(tile_in[0], group_size, my_index)
    in_slots, in_sources = ring_in.finish()
    ring_out = RingGather(tile_out[0], group_size, my_index)
    weight_in = in_slots.reshape(-1, in_slots.shape[-1])
    own_rows = jnp.take(patches[0].reshape(tiles_here, group_size, -1), in_sources, axis=1)
    tile_hidden = jax.nn.gelu(
        jnp.dot(own_rows.reshape(tiles_here, -1), weight_in, preferred_element_type=jnp.float32),
        approximate=True,
    ).astype(jnp.bfloat16)
    hidden_width = tile_hidden.shape[-1]

    slot_index = jnp.arange(list_width, dtype=jnp.int32)
    live_all = (slot_index[None, :] < site_count[:, None]).reshape(group_size, entries)
    owner_all = (site_tiles // tiles_here).reshape(group_size, entries)
    local_all = (site_tiles % tiles_here).reshape(group_size, entries)
    mine_mask = jnp.logical_and(live_all, owner_all == my_index)
    slot_rank = jnp.cumsum(mine_mask.astype(jnp.int32), axis=1) - 1
    picks = jnp.logical_and(
        mine_mask[:, :, None],
        slot_rank[:, :, None] == jnp.arange(capacity, dtype=jnp.int32)[None, None, :],
    )
    send_index = jnp.sum(jnp.where(picks, local_all[:, :, None], 0), axis=1)
    send_rows = tile_hidden[send_index.reshape(-1)].reshape(group_size, capacity, hidden_width)
    act_rows = sites_here * model_width // hidden_width
    packed = model_width % hidden_width == 0
    if packed:
        act_block = jnp.broadcast_to(
            current.reshape(1, act_rows, hidden_width), (group_size, act_rows, hidden_width)
        )
        send_rows = jnp.concatenate([send_rows, act_block], axis=1)
    send_rows = ring_out.step(send_rows)
    arrived = lax.all_to_all(send_rows, "site", split_axis=0, concat_axis=0, tiled=True)
    if packed:
        everyone = arrived[:, capacity:].reshape(-1, model_width)
        arrived = arrived[:, :capacity]
    else:
        everyone = doubling_gather(current, group_size, my_index).reshape(-1, model_width)
    q_part = by_rows(everyone, q_weight[0]).astype(jnp.bfloat16)
    q_part = ring_out.step(q_part)
    q_blocks = halving_exchange(
        q_part.reshape(group_size, sites_here, -1), group_size, my_index
    )
    q_blocks = ring_out.step(q_blocks)

    my_tiles = lax.dynamic_slice_in_dim(site_tiles, my_index * sites_here, sites_here, 0)
    my_count = lax.dynamic_slice_in_dim(site_count, my_index * sites_here, sites_here, 0)
    my_live = slot_index[None, :] < my_count[:, None]
    my_owner = (my_tiles // tiles_here).reshape(-1)
    one_hot = jnp.logical_and(
        my_owner[:, None] == jnp.arange(group_size, dtype=jnp.int32)[None, :],
        my_live.reshape(-1)[:, None],
    ).astype(jnp.int32)
    my_rank = jnp.sum(jnp.cumsum(one_hot, axis=0) * one_hot, axis=1) - 1
    fetch_index = jnp.where(my_live.reshape(-1), my_owner * capacity + my_rank, 0)
    pair_hidden = arrived.reshape(group_size * capacity, hidden_width)[fetch_index]

    shard_rows = tile_out.shape[1]
    keyval = None
    if not ring_out.direct:
        out_slots, out_sources = [ring_out.slots.reshape(-1, ring_out.slots.shape[-1])], [0]
        shard_rows = hidden_width
    else:
        out_slots, out_sources = ring_out.slots_in_arrival()
    for slot, source in zip(out_slots, out_sources):
        columns_here = lax.dynamic_slice_in_dim(pair_hidden, source * shard_rows, shard_rows, 1)
        term = jnp.dot(columns_here, slot, preferred_element_type=jnp.float32)
        keyval = term if keyval is None else keyval + term
    half_width = keyval.shape[1] // 2
    normed_keys = head_norm(keyval[:, :half_width], k_gain[0])
    pair_kv = jnp.concatenate([normed_keys, keyval[:, half_width:]], axis=1).astype(jnp.bfloat16)
    pair_kv = pair_kv.reshape(sites_here, list_width, 2, HEADS, head_size)

    my_queries = jnp.moveaxis(q_blocks, 0, 1).reshape(sites_here, -1)
    queries = head_norm(my_queries, q_gain[0]).astype(jnp.bfloat16)
    query_heads = queries.reshape(sites_here, HEADS, head_size)
    scores = jnp.einsum(
        "nhd,nlhd->nhl", query_heads, pair_kv[:, :, 0], preferred_element_type=jnp.float32
    ) / math.sqrt(head_size)
    exponents = jnp.exp(scores) * my_live.astype(jnp.float32)[:, None, :]
    weights = (exponents / jnp.sum(exponents, axis=-1, keepdims=True)).astype(jnp.bfloat16)
    combined = jnp.einsum(
        "nhl,nlhd->nhd", weights, pair_kv[:, :, 1], preferred_element_type=jnp.float32
    )
    combined = combined.reshape(sites_here, -1).astype(jnp.bfloat16)
    column_blocks = jnp.moveaxis(combined.reshape(sites_here, group_size, -1), 1, 0)
    columns = halving_exchange(column_blocks, group_size, my_index).reshape(
        group_size * sites_here, -1
    )
    attn_part = jnp.dot(columns, out_weight[0], preferred_element_type=jnp.float32)
    attn_part = attn_part.reshape(group_size, sites_here, -1)
    if direct_ok(group_size):
        attn_all = doubling_sum(attn_part, group_size)
        residual_all = everyone.reshape(group_size, sites_here, -1).astype(jnp.float32) + attn_all
        residual = lax.dynamic_index_in_dim(residual_all, my_index, 0, keepdims=False)
        normed_rows = rms_norm(residual_all, ffn_gain[0]).astype(jnp.bfloat16)
        normed_rows = normed_rows.reshape(-1, model_width)
    else:
        attn_sum = halving_sum(attn_part, group_size, my_index)
        residual = current.astype(jnp.float32) + attn_sum
        normed = rms_norm(residual, ffn_gain[0]).astype(jnp.bfloat16)
        normed_rows = doubling_gather(normed, group_size, my_index).reshape(-1, model_width)
    gate_sum = by_rows(normed_rows, gate_weight[0])
    up_sum = by_rows(normed_rows, up_weight[0])
    hidden_ffn = (jax.nn.silu(gate_sum) * up_sum).astype(jnp.bfloat16)
    down_part = jnp.dot(hidden_ffn, down_weight[0], preferred_element_type=jnp.float32)
    down_part = down_part.reshape(group_size, sites_here, -1)
    if not direct_ok(group_size) or group_size == 1:
        down_sum = halving_sum(down_part, group_size, my_index)
        output_rows = (residual + down_sum).astype(jnp.bfloat16)
        return lax.ppermute(output_rows[None], "section", shift_pairs(section_count, 1))
    bits = group_size.bit_length() - 1
    rest = down_part.shape[1:]
    state = down_part.reshape((2,) * bits + rest)
    for bit in range(bits):
        axis = bits - 1 - bit
        mine = (my_index >> bit) & 1
        keep = lax.dynamic_index_in_dim(state, mine, axis, keepdims=True)
        send = lax.dynamic_index_in_dim(state, 1 - mine, axis, keepdims=True)
        if bit < bits - 1:
            state = keep + lax.ppermute(send, "site", xor_pairs(group_size, bit))
            continue
        own = keep.reshape(rest) + residual
        forward = [
            (section * group_size + site, ((section + 1) % section_count) * group_size + site)
            for section in range(section_count)
            for site in range(group_size)
        ]
        across = [
            (
                section * group_size + site,
                ((section + 1) % section_count) * group_size + (site ^ (1 << bit)),
            )
            for section in range(section_count)
            for site in range(group_size)
        ]
        mine_part = lax.ppermute(own, ("section", "site"), forward)
        other_part = lax.ppermute(send.reshape(rest), ("section", "site"), across)
        output_rows = (mine_part + other_part).astype(jnp.bfloat16)
    return output_rows[None]


def heads_split(
    acts,
    patches,
    site_tiles,
    site_count,
    q_weight,
    q_gain,
    k_gain,
    tile_in,
    tile_out,
    out_weight,
    ffn_gain,
    gate_weight,
    up_weight,
    down_weight,
):
    group_size = lax.axis_size("site")
    section_count = lax.axis_size("section")
    my_index = lax.axis_index("site")
    sites_here = acts.shape[1]
    list_width = site_tiles.shape[1]
    tiles_here = patches.shape[1]
    head_size = q_gain.shape[1]
    heads_here = HEADS // group_size
    current = acts[0]
    model_width = current.shape[-1]
    hidden_width = tile_in.shape[-1]
    all_sites = group_size * sites_here

    row_width = patches.shape[-1]
    in_rows = tile_in.shape[1] * hidden_width // row_width
    act_rows = sites_here * model_width // row_width
    ring_in = RingGather(
        jnp.concatenate(
            [
                patches[0],
                tile_in[0].reshape(in_rows, row_width),
                current.reshape(act_rows, row_width),
            ],
            axis=0,
        ),
        group_size,
        my_index,
    )
    in_slots, in_sources = ring_in.finish()
    slot_of_source = jnp.argmax(
        in_sources[None, :] == jnp.arange(group_size, dtype=jnp.int32)[:, None], axis=1
    ).astype(jnp.int32)
    by_source = jnp.take(in_slots[:, tiles_here:], slot_of_source, axis=0)
    everyone = by_source[:, in_rows:].reshape(all_sites, model_width)
    weight_in = by_source[:, :in_rows].reshape(-1, hidden_width)
    table_hidden = jax.nn.gelu(
        jnp.dot(
            in_slots[:, :tiles_here].reshape(group_size * tiles_here, row_width),
            weight_in,
            preferred_element_type=jnp.float32,
        ),
        approximate=True,
    ).astype(jnp.bfloat16)
    hidden_sources = in_sources

    kv_width = tile_out.shape[-1]
    my_cols = heads_here * head_size
    col_blocks = tile_out[0].reshape(tile_out.shape[1], 2, group_size, my_cols)
    col_blocks = jnp.transpose(col_blocks, (2, 0, 1, 3)).reshape(group_size, tile_out.shape[1], 2 * my_cols)
    weight_out = lax.all_to_all(col_blocks, "site", split_axis=0, concat_axis=0, tiled=True)
    weight_out = weight_out.reshape(-1, 2 * my_cols)
    del kv_width

    q_part = by_rows(everyone, q_weight[0]).astype(jnp.bfloat16)
    queries = head_norm(q_part, q_gain[0]).astype(jnp.bfloat16)
    query_heads = queries.reshape(all_sites, heads_here, head_size)

    keyval = jnp.dot(table_hidden, weight_out, preferred_element_type=jnp.float32)
    normed_keys = head_norm(keyval[:, :my_cols], k_gain[0])
    table = jnp.concatenate([normed_keys, keyval[:, my_cols:]], axis=1).astype(jnp.bfloat16)
    table = table.reshape(group_size * tiles_here, 2, heads_here, head_size)

    tile_of_row = (
        hidden_sources[:, None] * tiles_here + jnp.arange(tiles_here, dtype=jnp.int32)[None, :]
    ).reshape(-1)
    slot_index = jnp.arange(list_width, dtype=jnp.int32)
    live = slot_index[None, :] < site_count[:, None]
    named = jnp.logical_and(
        site_tiles[:, :, None] == tile_of_row[None, None, :], live[:, :, None]
    )
    uses = jnp.sum(named.astype(jnp.float32), axis=1)
    scores = jnp.einsum(
        "nhd,rhd->nhr", query_heads, table[:, 0], preferred_element_type=jnp.float32
    ) / math.sqrt(head_size)
    exponents = jnp.exp(scores) * uses[:, None, :]
    weights = (exponents / jnp.sum(exponents, axis=-1, keepdims=True)).astype(jnp.bfloat16)
    combined = jnp.einsum(
        "nhr,rhd->nhd", weights, table[:, 1], preferred_element_type=jnp.float32
    )
    combined = combined.reshape(all_sites, my_cols).astype(jnp.bfloat16)
    attn_part = jnp.dot(combined, out_weight[0], preferred_element_type=jnp.float32)
    attn_all = doubling_sum(attn_part.reshape(group_size, sites_here, -1), group_size)
    residual_all = everyone.reshape(group_size, sites_here, -1).astype(jnp.float32) + attn_all
    residual = lax.dynamic_index_in_dim(residual_all, my_index, 0, keepdims=False)
    normed_rows = rms_norm(residual_all, ffn_gain[0]).astype(jnp.bfloat16).reshape(-1, model_width)
    gate_sum = by_rows(normed_rows, gate_weight[0])
    up_sum = by_rows(normed_rows, up_weight[0])
    hidden_ffn = (jax.nn.silu(gate_sum) * up_sum).astype(jnp.bfloat16)
    down_part = jnp.dot(hidden_ffn, down_weight[0], preferred_element_type=jnp.float32)
    down_part = down_part.reshape(group_size, sites_here, -1)
    return last_round(down_part, residual, group_size, section_count, my_index)


def last_round(down_part, residual, group_size, section_count, my_index):
    bits = group_size.bit_length() - 1
    rest = down_part.shape[1:]
    state = down_part.reshape((2,) * bits + rest)
    for bit in range(bits):
        axis = bits - 1 - bit
        mine = (my_index >> bit) & 1
        keep = lax.dynamic_index_in_dim(state, mine, axis, keepdims=True)
        send = lax.dynamic_index_in_dim(state, 1 - mine, axis, keepdims=True)
        if bit < bits - 1:
            state = keep + lax.ppermute(send, "site", xor_pairs(group_size, bit))
            continue
        own = keep.reshape(rest) + residual
        forward = [
            (section * group_size + site, ((section + 1) % section_count) * group_size + site)
            for section in range(section_count)
            for site in range(group_size)
        ]
        across = [
            (
                section * group_size + site,
                ((section + 1) % section_count) * group_size + (site ^ (1 << bit)),
            )
            for section in range(section_count)
            for site in range(group_size)
        ]
        mine_part = lax.ppermute(own, ("section", "site"), forward)
        other_part = lax.ppermute(send.reshape(rest), ("section", "site"), across)
        return (mine_part + other_part).astype(jnp.bfloat16)[None]


def solution(mesh):
    group_size = mesh.shape["site"]
    split_heads = (
        direct_ok(group_size)
        and group_size > 1
        and HEADS % group_size == 0
        and mesh.shape["section"] > 0
    )
    return jax.shard_map(
        heads_split if split_heads else shards,
        mesh=mesh,
        in_specs=(
            P("section", "site", None),
            P("section", "site", None),
            P(),
            P(),
            P("section", "site", None),
            P("section", None),
            P("section", None),
            P("section", "site", None),
            P("section", "site", None),
            P("section", "site", None),
            P("section", None),
            P("section", "site", None),
            P("section", "site", None),
            P("section", "site", None),
        ),
        out_specs=P("section", "site", None),
        check_vma=False,
    )
```

```python
import math

import jax
import jax.numpy as jnp
from jax import lax
from jax.sharding import PartitionSpec as P

HEADS = 16


epsilon = 1e-05

DIRECT_LIMIT = 8


def shift_pairs(count, steps):
    return [(source, (source + steps) % count) for source in range(count)]


def by_rows(left, weight_rows):
    return lax.dot_general(
        left, weight_rows, (((1,), (1,)), ((), ())), preferred_element_type=jnp.float32
    )


def head_norm(values, gain_row):
    shaped = values.astype(jnp.float32).reshape(values.shape[0], -1, gain_row.shape[0])
    scaled = (
        shaped * lax.rsqrt(jnp.mean(shaped * shaped, axis=-1, keepdims=True) + epsilon) * gain_row
    )
    return scaled.reshape(values.shape[0], -1)


def rms_norm(values, gain_row):
    return (
        values * lax.rsqrt(jnp.mean(values * values, axis=-1, keepdims=True) + epsilon) * gain_row
    )


def to_source_order(slots, count, me):
    return jnp.take(slots, (me - jnp.arange(count, dtype=jnp.int32)) % count, axis=0)


def xor_pairs(count, bit):
    return [(source, source ^ (1 << bit)) for source in range(count)]


def direct_ok(count):
    return count <= DIRECT_LIMIT and count & (count - 1) == 0


def site_exchange(by_target, count, me):
    if not direct_ok(count):
        return lax.all_to_all(by_target, "site", split_axis=0, concat_axis=0, tiled=True)
    slots = [lax.dynamic_index_in_dim(by_target, me, 0, keepdims=False)]
    for steps in range(1, count):
        piece = lax.dynamic_index_in_dim(by_target, (me + steps) % count, 0, keepdims=False)
        slots.append(lax.ppermute(piece, "site", shift_pairs(count, steps)))
    return to_source_order(jnp.stack(slots), count, me)


def halving_exchange(by_target, count, me):
    if not direct_ok(count):
        return lax.all_to_all(by_target, "site", split_axis=0, concat_axis=0, tiled=True)
    bits = count.bit_length() - 1
    rest = by_target.shape[1:]
    state = by_target.reshape((2,) * bits + rest)
    for bit in range(bits):
        axis = bits - 1 - bit
        mine = (me >> bit) & 1
        keep = lax.dynamic_index_in_dim(state, mine, axis, keepdims=True)
        send = lax.dynamic_index_in_dim(state, 1 - mine, axis, keepdims=True)
        recv = lax.ppermute(send, "site", xor_pairs(count, bit))
        state = jnp.where(
            mine == 0,
            jnp.concatenate([keep, recv], axis),
            jnp.concatenate([recv, keep], axis),
        )
    return state.reshape((count,) + rest)


def doubling_gather(value, count, me):
    if not direct_ok(count):
        return lax.all_gather(value, "site", axis=0, tiled=False)
    bits = count.bit_length() - 1
    state = value[None]
    for bit in range(bits):
        recv = lax.ppermute(state, "site", xor_pairs(count, bit))
        mine = (me >> bit) & 1
        state = jnp.where(
            mine == 0, jnp.concatenate([state, recv], 0), jnp.concatenate([recv, state], 0)
        )
    return state


def halving_sum(parts, count, me):
    if not direct_ok(count):
        return lax.psum_scatter(parts, "site", scatter_dimension=0, tiled=True)[0]
    bits = count.bit_length() - 1
    rest = parts.shape[1:]
    state = parts.reshape((2,) * bits + rest)
    for bit in range(bits):
        axis = bits - 1 - bit
        mine = (me >> bit) & 1
        keep = lax.dynamic_index_in_dim(state, mine, axis, keepdims=True)
        send = lax.dynamic_index_in_dim(state, 1 - mine, axis, keepdims=True)
        state = keep + lax.ppermute(send, "site", xor_pairs(count, bit))
    return state.reshape(rest)


def doubling_sum(parts, count):
    state = parts
    for bit in range(count.bit_length() - 1):
        state = state + lax.ppermute(state, "site", xor_pairs(count, bit))
    return state


class RingGather:
    def __init__(self, value, count, me):
        self.count = count
        self.direct = direct_ok(count)
        if not self.direct:
            self.slots = lax.all_gather(value, "site", axis=0, tiled=False)
            self.sources = jnp.arange(count, dtype=jnp.int32)
            return
        order = list(range(0, count, 2)) + [i for i in range(count - 1, -1, -1) if i % 2 == 1]
        place = [0] * count
        for position, device in enumerate(order):
            place[device] = position
        self.forward = [(order[p], order[(p + 1) % count]) for p in range(count)]
        self.backward = [(order[p], order[(p - 1) % count]) for p in range(count)]
        self.forward_left = count // 2
        self.backward_left = count - 1 - self.forward_left
        offsets = [0] + [-s for s in range(1, self.forward_left + 1)]
        offsets += list(range(1, self.backward_left + 1))
        my_place = jnp.array(place, dtype=jnp.int32)[me]
        self.sources = jnp.array(order, dtype=jnp.int32)[
            (my_place + jnp.array(offsets, dtype=jnp.int32)) % count
        ]
        self.forward_slots = []
        self.backward_slots = []
        self.ahead = value
        self.behind = value
        self.value = value
        self._issue()

    def _issue(self):
        if self.forward_left > 0:
            self.ahead = lax.ppermute(self.ahead, "site", self.forward)
            self.forward_slots.append(self.ahead)
            self.forward_left -= 1
        if self.backward_left > 0:
            self.behind = lax.ppermute(self.behind, "site", self.backward)
            self.backward_slots.append(self.behind)
            self.backward_left -= 1

    def step(self, tied):
        if not self.direct or (self.forward_left == 0 and self.backward_left == 0):
            return tied
        self.ahead, self.behind, tied = lax.optimization_barrier((self.ahead, self.behind, tied))
        self.forward_slots[-1] = self.ahead
        if self.backward_slots:
            self.backward_slots[-1] = self.behind
        self._issue()
        return tied

    def slots_in_arrival(self):
        if not self.direct:
            return [self.slots[i] for i in range(self.count)], [self.sources[i] for i in range(self.count)]
        while self.forward_left > 0 or self.backward_left > 0:
            self._issue()
        slots = [self.value]
        positions = [0]
        forward_count = len(self.forward_slots)
        for step in range(max(forward_count, len(self.backward_slots))):
            if step < forward_count:
                slots.append(self.forward_slots[step])
                positions.append(1 + step)
            if step < len(self.backward_slots):
                slots.append(self.backward_slots[step])
                positions.append(1 + forward_count + step)
        return slots, [self.sources[p] for p in positions]

    def finish(self):
        if not self.direct:
            return self.slots, self.sources
        while self.forward_left > 0 or self.backward_left > 0:
            self._issue()
        slots = [self.value] + self.forward_slots + self.backward_slots
        return jnp.stack(slots), self.sources


def shards(
    acts,
    patches,
    site_tiles,
    site_count,
    q_weight,
    q_gain,
    k_gain,
    tile_in,
    tile_out,
    out_weight,
    ffn_gain,
    gate_weight,
    up_weight,
    down_weight,
):
    group_size = lax.axis_size("site")
    section_count = lax.axis_size("section")
    my_index = lax.axis_index("site")
    sites_here = acts.shape[1]
    list_width = site_tiles.shape[1]
    tiles_here = patches.shape[1]
    head_size = q_gain.shape[1]
    capacity = max(2, 5 * sites_here * list_width // (4 * group_size))
    entries = sites_here * list_width
    current = acts[0]
    model_width = current.shape[-1]
    row_width = patches.shape[-1]

    ring_in = RingGather(tile_in[0], group_size, my_index)
    in_slots, in_sources = ring_in.finish()
    ring_out = RingGather(tile_out[0], group_size, my_index)
    weight_in = in_slots.reshape(-1, in_slots.shape[-1])
    own_rows = jnp.take(patches[0].reshape(tiles_here, group_size, -1), in_sources, axis=1)
    tile_hidden = jax.nn.gelu(
        jnp.dot(own_rows.reshape(tiles_here, -1), weight_in, preferred_element_type=jnp.float32),
        approximate=True,
    ).astype(jnp.bfloat16)
    hidden_width = tile_hidden.shape[-1]

    slot_index = jnp.arange(list_width, dtype=jnp.int32)
    live_all = (slot_index[None, :] < site_count[:, None]).reshape(group_size, entries)
    owner_all = (site_tiles // tiles_here).reshape(group_size, entries)
    local_all = (site_tiles % tiles_here).reshape(group_size, entries)
    mine_mask = jnp.logical_and(live_all, owner_all == my_index)
    slot_rank = jnp.cumsum(mine_mask.astype(jnp.int32), axis=1) - 1
    picks = jnp.logical_and(
        mine_mask[:, :, None],
        slot_rank[:, :, None] == jnp.arange(capacity, dtype=jnp.int32)[None, None, :],
    )
    send_index = jnp.sum(jnp.where(picks, local_all[:, :, None], 0), axis=1)
    send_rows = tile_hidden[send_index.reshape(-1)].reshape(group_size, capacity, hidden_width)
    act_rows = sites_here * model_width // hidden_width
    packed = model_width % hidden_width == 0
    if packed:
        act_block = jnp.broadcast_to(
            current.reshape(1, act_rows, hidden_width), (group_size, act_rows, hidden_width)
        )
        send_rows = jnp.concatenate([send_rows, act_block], axis=1)
    send_rows = ring_out.step(send_rows)
    arrived = lax.all_to_all(send_rows, "site", split_axis=0, concat_axis=0, tiled=True)
    if packed:
        everyone = arrived[:, capacity:].reshape(-1, model_width)
        arrived = arrived[:, :capacity]
    else:
        everyone = doubling_gather(current, group_size, my_index).reshape(-1, model_width)
    q_part = by_rows(everyone, q_weight[0]).astype(jnp.bfloat16)
    q_part = ring_out.step(q_part)
    q_blocks = halving_exchange(
        q_part.reshape(group_size, sites_here, -1), group_size, my_index
    )
    q_blocks = ring_out.step(q_blocks)

    my_tiles = lax.dynamic_slice_in_dim(site_tiles, my_index * sites_here, sites_here, 0)
    my_count = lax.dynamic_slice_in_dim(site_count, my_index * sites_here, sites_here, 0)
    my_live = slot_index[None, :] < my_count[:, None]
    my_owner = (my_tiles // tiles_here).reshape(-1)
    one_hot = jnp.logical_and(
        my_owner[:, None] == jnp.arange(group_size, dtype=jnp.int32)[None, :],
        my_live.reshape(-1)[:, None],
    ).astype(jnp.int32)
    my_rank = jnp.sum(jnp.cumsum(one_hot, axis=0) * one_hot, axis=1) - 1
    fetch_index = jnp.where(my_live.reshape(-1), my_owner * capacity + my_rank, 0)
    pair_hidden = arrived.reshape(group_size * capacity, hidden_width)[fetch_index]

    shard_rows = tile_out.shape[1]
    keyval = None
    if not ring_out.direct:
        out_slots, out_sources = [ring_out.slots.reshape(-1, ring_out.slots.shape[-1])], [0]
        shard_rows = hidden_width
    else:
        out_slots, out_sources = ring_out.slots_in_arrival()
    for slot, source in zip(out_slots, out_sources):
        columns_here = lax.dynamic_slice_in_dim(pair_hidden, source * shard_rows, shard_rows, 1)
        term = jnp.dot(columns_here, slot, preferred_element_type=jnp.float32)
        keyval = term if keyval is None else keyval + term
    half_width = keyval.shape[1] // 2
    normed_keys = head_norm(keyval[:, :half_width], k_gain[0])
    pair_kv = jnp.concatenate([normed_keys, keyval[:, half_width:]], axis=1).astype(jnp.bfloat16)
    pair_kv = pair_kv.reshape(sites_here, list_width, 2, HEADS, head_size)

    my_queries = jnp.moveaxis(q_blocks, 0, 1).reshape(sites_here, -1)
    queries = head_norm(my_queries, q_gain[0]).astype(jnp.bfloat16)
    query_heads = queries.reshape(sites_here, HEADS, head_size)
    scores = jnp.einsum(
        "nhd,nlhd->nhl", query_heads, pair_kv[:, :, 0], preferred_element_type=jnp.float32
    ) / math.sqrt(head_size)
    exponents = jnp.exp(scores) * my_live.astype(jnp.float32)[:, None, :]
    weights = (exponents / jnp.sum(exponents, axis=-1, keepdims=True)).astype(jnp.bfloat16)
    combined = jnp.einsum(
        "nhl,nlhd->nhd", weights, pair_kv[:, :, 1], preferred_element_type=jnp.float32
    )
    combined = combined.reshape(sites_here, -1).astype(jnp.bfloat16)
    column_blocks = jnp.moveaxis(combined.reshape(sites_here, group_size, -1), 1, 0)
    columns = halving_exchange(column_blocks, group_size, my_index).reshape(
        group_size * sites_here, -1
    )
    attn_part = jnp.dot(columns, out_weight[0], preferred_element_type=jnp.float32)
    attn_part = attn_part.reshape(group_size, sites_here, -1)
    if direct_ok(group_size):
        attn_all = doubling_sum(attn_part, group_size)
        residual_all = everyone.reshape(group_size, sites_here, -1).astype(jnp.float32) + attn_all
        residual = lax.dynamic_index_in_dim(residual_all, my_index, 0, keepdims=False)
        normed_rows = rms_norm(residual_all, ffn_gain[0]).astype(jnp.bfloat16)
        normed_rows = normed_rows.reshape(-1, model_width)
    else:
        attn_sum = halving_sum(attn_part, group_size, my_index)
        residual = current.astype(jnp.float32) + attn_sum
        normed = rms_norm(residual, ffn_gain[0]).astype(jnp.bfloat16)
        normed_rows = doubling_gather(normed, group_size, my_index).reshape(-1, model_width)
    gate_sum = by_rows(normed_rows, gate_weight[0])
    up_sum = by_rows(normed_rows, up_weight[0])
    hidden_ffn = (jax.nn.silu(gate_sum) * up_sum).astype(jnp.bfloat16)
    down_part = jnp.dot(hidden_ffn, down_weight[0], preferred_element_type=jnp.float32)
    down_part = down_part.reshape(group_size, sites_here, -1)
    if not direct_ok(group_size) or group_size == 1:
        down_sum = halving_sum(down_part, group_size, my_index)
        output_rows = (residual + down_sum).astype(jnp.bfloat16)
        return lax.ppermute(output_rows[None], "section", shift_pairs(section_count, 1))
    bits = group_size.bit_length() - 1
    rest = down_part.shape[1:]
    state = down_part.reshape((2,) * bits + rest)
    for bit in range(bits):
        axis = bits - 1 - bit
        mine = (my_index >> bit) & 1
        keep = lax.dynamic_index_in_dim(state, mine, axis, keepdims=True)
        send = lax.dynamic_index_in_dim(state, 1 - mine, axis, keepdims=True)
        if bit < bits - 1:
            state = keep + lax.ppermute(send, "site", xor_pairs(group_size, bit))
            continue
        own = keep.reshape(rest) + residual
        forward = [
            (section * group_size + site, ((section + 1) % section_count) * group_size + site)
            for section in range(section_count)
            for site in range(group_size)
        ]
        across = [
            (
                section * group_size + site,
                ((section + 1) % section_count) * group_size + (site ^ (1 << bit)),
            )
            for section in range(section_count)
            for site in range(group_size)
        ]
        mine_part = lax.ppermute(own, ("section", "site"), forward)
        other_part = lax.ppermute(send.reshape(rest), ("section", "site"), across)
        output_rows = (mine_part + other_part).astype(jnp.bfloat16)
    return output_rows[None]


def heads_split(
    acts,
    patches,
    site_tiles,
    site_count,
    q_weight,
    q_gain,
    k_gain,
    tile_in,
    tile_out,
    out_weight,
    ffn_gain,
    gate_weight,
    up_weight,
    down_weight,
):
    group_size = lax.axis_size("site")
    section_count = lax.axis_size("section")
    my_index = lax.axis_index("site")
    sites_here = acts.shape[1]
    list_width = site_tiles.shape[1]
    tiles_here = patches.shape[1]
    head_size = q_gain.shape[1]
    heads_here = HEADS // group_size
    current = acts[0]
    model_width = current.shape[-1]
    hidden_width = tile_in.shape[-1]
    all_sites = group_size * sites_here

    act_rows = sites_here * model_width // hidden_width
    ring_in = RingGather(
        jnp.concatenate([tile_in[0], current.reshape(act_rows, hidden_width)], axis=0),
        group_size,
        my_index,
    )
    kv_width = tile_out.shape[-1]
    my_cols = heads_here * head_size
    col_blocks = tile_out[0].reshape(tile_out.shape[1], 2, group_size, my_cols)
    col_blocks = jnp.transpose(col_blocks, (2, 0, 1, 3)).reshape(group_size, tile_out.shape[1], 2 * my_cols)
    col_blocks, site_tiles, site_count = ring_in.step((col_blocks, site_tiles, site_count))
    weight_out = lax.all_to_all(col_blocks, "site", split_axis=0, concat_axis=0, tiled=True)
    weight_out = weight_out.reshape(-1, 2 * my_cols)
    del kv_width

    in_slots, in_sources = ring_in.finish()
    in_rows = tile_in.shape[1]
    slot_of_source = jnp.argmax(
        in_sources[None, :] == jnp.arange(group_size, dtype=jnp.int32)[:, None], axis=1
    ).astype(jnp.int32)
    everyone = jnp.take(in_slots[:, in_rows:], slot_of_source, axis=0).reshape(all_sites, model_width)
    weight_in = in_slots[:, :in_rows].reshape(-1, hidden_width)
    own_rows = jnp.take(patches[0].reshape(tiles_here, group_size, -1), in_sources, axis=1)
    tile_hidden = jax.nn.gelu(
        jnp.dot(own_rows.reshape(tiles_here, -1), weight_in, preferred_element_type=jnp.float32),
        approximate=True,
    ).astype(jnp.bfloat16)

    q_part = by_rows(everyone, q_weight[0]).astype(jnp.bfloat16)
    queries = head_norm(q_part, q_gain[0]).astype(jnp.bfloat16)
    query_heads = queries.reshape(all_sites, heads_here, head_size)

    ring_hidden = RingGather(tile_hidden, group_size, my_index)
    hidden_slots, hidden_sources = ring_hidden.finish()
    table_hidden = hidden_slots.reshape(group_size * tiles_here, hidden_width)
    keyval = jnp.dot(table_hidden, weight_out, preferred_element_type=jnp.float32)
    normed_keys = head_norm(keyval[:, :my_cols], k_gain[0])
    table = jnp.concatenate([normed_keys, keyval[:, my_cols:]], axis=1).astype(jnp.bfloat16)
    table = table.reshape(group_size * tiles_here, 2, heads_here, head_size)

    tile_of_row = (
        hidden_sources[:, None] * tiles_here + jnp.arange(tiles_here, dtype=jnp.int32)[None, :]
    ).reshape(-1)
    slot_index = jnp.arange(list_width, dtype=jnp.int32)
    live = slot_index[None, :] < site_count[:, None]
    named = jnp.logical_and(
        site_tiles[:, :, None] == tile_of_row[None, None, :], live[:, :, None]
    )
    uses = jnp.sum(named.astype(jnp.float32), axis=1)
    scores = jnp.einsum(
        "nhd,rhd->nhr", query_heads, table[:, 0], preferred_element_type=jnp.float32
    ) / math.sqrt(head_size)
    exponents = jnp.exp(scores) * uses[:, None, :]
    weights = (exponents / jnp.sum(exponents, axis=-1, keepdims=True)).astype(jnp.bfloat16)
    combined = jnp.einsum(
        "nhr,rhd->nhd", weights, table[:, 1], preferred_element_type=jnp.float32
    )
    combined = combined.reshape(all_sites, my_cols).astype(jnp.bfloat16)
    attn_part = jnp.dot(combined, out_weight[0], preferred_element_type=jnp.float32)
    attn_all = doubling_sum(attn_part.reshape(group_size, sites_here, -1), group_size)
    residual_all = everyone.reshape(group_size, sites_here, -1).astype(jnp.float32) + attn_all
    residual = lax.dynamic_index_in_dim(residual_all, my_index, 0, keepdims=False)
    normed_rows = rms_norm(residual_all, ffn_gain[0]).astype(jnp.bfloat16).reshape(-1, model_width)
    gate_sum = by_rows(normed_rows, gate_weight[0])
    up_sum = by_rows(normed_rows, up_weight[0])
    hidden_ffn = (jax.nn.silu(gate_sum) * up_sum).astype(jnp.bfloat16)
    down_part = jnp.dot(hidden_ffn, down_weight[0], preferred_element_type=jnp.float32)
    down_part = down_part.reshape(group_size, sites_here, -1)
    return last_round(down_part, residual, group_size, section_count, my_index)


def last_round(down_part, residual, group_size, section_count, my_index):
    bits = group_size.bit_length() - 1
    rest = down_part.shape[1:]
    state = down_part.reshape((2,) * bits + rest)
    for bit in range(bits):
        axis = bits - 1 - bit
        mine = (my_index >> bit) & 1
        keep = lax.dynamic_index_in_dim(state, mine, axis, keepdims=True)
        send = lax.dynamic_index_in_dim(state, 1 - mine, axis, keepdims=True)
        if bit < bits - 1:
            state = keep + lax.ppermute(send, "site", xor_pairs(group_size, bit))
            continue
        own = keep.reshape(rest) + residual
        forward = [
            (section * group_size + site, ((section + 1) % section_count) * group_size + site)
            for section in range(section_count)
            for site in range(group_size)
        ]
        across = [
            (
                section * group_size + site,
                ((section + 1) % section_count) * group_size + (site ^ (1 << bit)),
            )
            for section in range(section_count)
            for site in range(group_size)
        ]
        mine_part = lax.ppermute(own, ("section", "site"), forward)
        other_part = lax.ppermute(send.reshape(rest), ("section", "site"), across)
        return (mine_part + other_part).astype(jnp.bfloat16)[None]


def solution(mesh):
    group_size = mesh.shape["site"]
    split_heads = (
        direct_ok(group_size)
        and group_size > 1
        and HEADS % group_size == 0
        and mesh.shape["section"] > 0
    )
    return jax.shard_map(
        heads_split if split_heads else shards,
        mesh=mesh,
        in_specs=(
            P("section", "site", None),
            P("section", "site", None),
            P(),
            P(),
            P("section", "site", None),
            P("section", None),
            P("section", None),
            P("section", "site", None),
            P("section", "site", None),
            P("section", "site", None),
            P("section", None),
            P("section", "site", None),
            P("section", "site", None),
            P("section", "site", None),
        ),
        out_specs=P("section", "site", None),
        check_vma=False,
    )
```

```python
import math

import jax
import jax.numpy as jnp
from jax import lax
from jax.experimental import pallas as pl
from jax.experimental.pallas import tpu as pltpu
from jax.sharding import PartitionSpec as P

HEADS = 16


epsilon = 1e-05

DIRECT_LIMIT = 8


def shift_pairs(count, steps):
    return [(source, (source + steps) % count) for source in range(count)]


def by_rows(left, weight_rows):
    return lax.dot_general(
        left, weight_rows, (((1,), (1,)), ((), ())), preferred_element_type=jnp.float32
    )


def head_norm(values, gain_row):
    shaped = values.astype(jnp.float32).reshape(values.shape[0], -1, gain_row.shape[0])
    scaled = (
        shaped * lax.rsqrt(jnp.mean(shaped * shaped, axis=-1, keepdims=True) + epsilon) * gain_row
    )
    return scaled.reshape(values.shape[0], -1)


def rms_norm(values, gain_row):
    return (
        values * lax.rsqrt(jnp.mean(values * values, axis=-1, keepdims=True) + epsilon) * gain_row
    )


def to_source_order(slots, count, me):
    return jnp.take(slots, (me - jnp.arange(count, dtype=jnp.int32)) % count, axis=0)


def xor_pairs(count, bit):
    return [(source, source ^ (1 << bit)) for source in range(count)]


def direct_ok(count):
    return count <= DIRECT_LIMIT and count & (count - 1) == 0


def site_exchange(by_target, count, me):
    if not direct_ok(count):
        return lax.all_to_all(by_target, "site", split_axis=0, concat_axis=0, tiled=True)
    slots = [lax.dynamic_index_in_dim(by_target, me, 0, keepdims=False)]
    for steps in range(1, count):
        piece = lax.dynamic_index_in_dim(by_target, (me + steps) % count, 0, keepdims=False)
        slots.append(lax.ppermute(piece, "site", shift_pairs(count, steps)))
    return to_source_order(jnp.stack(slots), count, me)


def halving_exchange(by_target, count, me):
    if not direct_ok(count):
        return lax.all_to_all(by_target, "site", split_axis=0, concat_axis=0, tiled=True)
    bits = count.bit_length() - 1
    rest = by_target.shape[1:]
    state = by_target.reshape((2,) * bits + rest)
    for bit in range(bits):
        axis = bits - 1 - bit
        mine = (me >> bit) & 1
        keep = lax.dynamic_index_in_dim(state, mine, axis, keepdims=True)
        send = lax.dynamic_index_in_dim(state, 1 - mine, axis, keepdims=True)
        recv = lax.ppermute(send, "site", xor_pairs(count, bit))
        state = jnp.where(
            mine == 0,
            jnp.concatenate([keep, recv], axis),
            jnp.concatenate([recv, keep], axis),
        )
    return state.reshape((count,) + rest)


def doubling_gather(value, count, me):
    if not direct_ok(count):
        return lax.all_gather(value, "site", axis=0, tiled=False)
    bits = count.bit_length() - 1
    state = value[None]
    for bit in range(bits):
        recv = lax.ppermute(state, "site", xor_pairs(count, bit))
        mine = (me >> bit) & 1
        state = jnp.where(
            mine == 0, jnp.concatenate([state, recv], 0), jnp.concatenate([recv, state], 0)
        )
    return state


def halving_sum(parts, count, me):
    if not direct_ok(count):
        return lax.psum_scatter(parts, "site", scatter_dimension=0, tiled=True)[0]
    bits = count.bit_length() - 1
    rest = parts.shape[1:]
    state = parts.reshape((2,) * bits + rest)
    for bit in range(bits):
        axis = bits - 1 - bit
        mine = (me >> bit) & 1
        keep = lax.dynamic_index_in_dim(state, mine, axis, keepdims=True)
        send = lax.dynamic_index_in_dim(state, 1 - mine, axis, keepdims=True)
        state = keep + lax.ppermute(send, "site", xor_pairs(count, bit))
    return state.reshape(rest)


def doubling_sum(parts, count):
    state = parts
    for bit in range(count.bit_length() - 1):
        state = state + lax.ppermute(state, "site", xor_pairs(count, bit))
    return state


class RingGather:
    def __init__(self, value, count, me):
        self.count = count
        self.direct = direct_ok(count)
        if not self.direct:
            self.slots = lax.all_gather(value, "site", axis=0, tiled=False)
            self.sources = jnp.arange(count, dtype=jnp.int32)
            return
        order = list(range(0, count, 2)) + [i for i in range(count - 1, -1, -1) if i % 2 == 1]
        place = [0] * count
        for position, device in enumerate(order):
            place[device] = position
        self.forward = [(order[p], order[(p + 1) % count]) for p in range(count)]
        self.backward = [(order[p], order[(p - 1) % count]) for p in range(count)]
        self.forward_left = count // 2
        self.backward_left = count - 1 - self.forward_left
        offsets = [0] + [-s for s in range(1, self.forward_left + 1)]
        offsets += list(range(1, self.backward_left + 1))
        my_place = jnp.array(place, dtype=jnp.int32)[me]
        self.sources = jnp.array(order, dtype=jnp.int32)[
            (my_place + jnp.array(offsets, dtype=jnp.int32)) % count
        ]
        self.forward_slots = []
        self.backward_slots = []
        self.ahead = value
        self.behind = value
        self.value = value
        self._issue()

    def _issue(self):
        if self.forward_left > 0:
            self.ahead = lax.ppermute(self.ahead, "site", self.forward)
            self.forward_slots.append(self.ahead)
            self.forward_left -= 1
        if self.backward_left > 0:
            self.behind = lax.ppermute(self.behind, "site", self.backward)
            self.backward_slots.append(self.behind)
            self.backward_left -= 1

    def step(self, tied):
        if not self.direct or (self.forward_left == 0 and self.backward_left == 0):
            return tied
        self.ahead, self.behind, tied = lax.optimization_barrier((self.ahead, self.behind, tied))
        self.forward_slots[-1] = self.ahead
        if self.backward_slots:
            self.backward_slots[-1] = self.behind
        self._issue()
        return tied

    def slots_in_arrival(self):
        if not self.direct:
            return [self.slots[i] for i in range(self.count)], [self.sources[i] for i in range(self.count)]
        while self.forward_left > 0 or self.backward_left > 0:
            self._issue()
        slots = [self.value]
        positions = [0]
        forward_count = len(self.forward_slots)
        for step in range(max(forward_count, len(self.backward_slots))):
            if step < forward_count:
                slots.append(self.forward_slots[step])
                positions.append(1 + step)
            if step < len(self.backward_slots):
                slots.append(self.backward_slots[step])
                positions.append(1 + forward_count + step)
        return slots, [self.sources[p] for p in positions]

    def finish(self):
        if not self.direct:
            return self.slots, self.sources
        while self.forward_left > 0 or self.backward_left > 0:
            self._issue()
        slots = [self.value] + self.forward_slots + self.backward_slots
        return jnp.stack(slots), self.sources


def shards(
    acts,
    patches,
    site_tiles,
    site_count,
    q_weight,
    q_gain,
    k_gain,
    tile_in,
    tile_out,
    out_weight,
    ffn_gain,
    gate_weight,
    up_weight,
    down_weight,
):
    group_size = lax.axis_size("site")
    section_count = lax.axis_size("section")
    my_index = lax.axis_index("site")
    sites_here = acts.shape[1]
    list_width = site_tiles.shape[1]
    tiles_here = patches.shape[1]
    head_size = q_gain.shape[1]
    capacity = max(2, 5 * sites_here * list_width // (4 * group_size))
    entries = sites_here * list_width
    current = acts[0]
    model_width = current.shape[-1]
    row_width = patches.shape[-1]

    ring_in = RingGather(tile_in[0], group_size, my_index)
    in_slots, in_sources = ring_in.finish()
    ring_out = RingGather(tile_out[0], group_size, my_index)
    weight_in = in_slots.reshape(-1, in_slots.shape[-1])
    own_rows = jnp.take(patches[0].reshape(tiles_here, group_size, -1), in_sources, axis=1)
    tile_hidden = jax.nn.gelu(
        jnp.dot(own_rows.reshape(tiles_here, -1), weight_in, preferred_element_type=jnp.float32),
        approximate=True,
    ).astype(jnp.bfloat16)
    hidden_width = tile_hidden.shape[-1]

    slot_index = jnp.arange(list_width, dtype=jnp.int32)
    live_all = (slot_index[None, :] < site_count[:, None]).reshape(group_size, entries)
    owner_all = (site_tiles // tiles_here).reshape(group_size, entries)
    local_all = (site_tiles % tiles_here).reshape(group_size, entries)
    mine_mask = jnp.logical_and(live_all, owner_all == my_index)
    slot_rank = jnp.cumsum(mine_mask.astype(jnp.int32), axis=1) - 1
    picks = jnp.logical_and(
        mine_mask[:, :, None],
        slot_rank[:, :, None] == jnp.arange(capacity, dtype=jnp.int32)[None, None, :],
    )
    send_index = jnp.sum(jnp.where(picks, local_all[:, :, None], 0), axis=1)
    send_rows = tile_hidden[send_index.reshape(-1)].reshape(group_size, capacity, hidden_width)
    act_rows = sites_here * model_width // hidden_width
    packed = model_width % hidden_width == 0
    if packed:
        act_block = jnp.broadcast_to(
            current.reshape(1, act_rows, hidden_width), (group_size, act_rows, hidden_width)
        )
        send_rows = jnp.concatenate([send_rows, act_block], axis=1)
    send_rows = ring_out.step(send_rows)
    arrived = lax.all_to_all(send_rows, "site", split_axis=0, concat_axis=0, tiled=True)
    if packed:
        everyone = arrived[:, capacity:].reshape(-1, model_width)
        arrived = arrived[:, :capacity]
    else:
        everyone = doubling_gather(current, group_size, my_index).reshape(-1, model_width)
    q_part = by_rows(everyone, q_weight[0]).astype(jnp.bfloat16)
    q_part = ring_out.step(q_part)
    q_blocks = halving_exchange(
        q_part.reshape(group_size, sites_here, -1), group_size, my_index
    )
    q_blocks = ring_out.step(q_blocks)

    my_tiles = lax.dynamic_slice_in_dim(site_tiles, my_index * sites_here, sites_here, 0)
    my_count = lax.dynamic_slice_in_dim(site_count, my_index * sites_here, sites_here, 0)
    my_live = slot_index[None, :] < my_count[:, None]
    my_owner = (my_tiles // tiles_here).reshape(-1)
    one_hot = jnp.logical_and(
        my_owner[:, None] == jnp.arange(group_size, dtype=jnp.int32)[None, :],
        my_live.reshape(-1)[:, None],
    ).astype(jnp.int32)
    my_rank = jnp.sum(jnp.cumsum(one_hot, axis=0) * one_hot, axis=1) - 1
    fetch_index = jnp.where(my_live.reshape(-1), my_owner * capacity + my_rank, 0)
    pair_hidden = arrived.reshape(group_size * capacity, hidden_width)[fetch_index]

    shard_rows = tile_out.shape[1]
    keyval = None
    if not ring_out.direct:
        out_slots, out_sources = [ring_out.slots.reshape(-1, ring_out.slots.shape[-1])], [0]
        shard_rows = hidden_width
    else:
        out_slots, out_sources = ring_out.slots_in_arrival()
    for slot, source in zip(out_slots, out_sources):
        columns_here = lax.dynamic_slice_in_dim(pair_hidden, source * shard_rows, shard_rows, 1)
        term = jnp.dot(columns_here, slot, preferred_element_type=jnp.float32)
        keyval = term if keyval is None else keyval + term
    half_width = keyval.shape[1] // 2
    normed_keys = head_norm(keyval[:, :half_width], k_gain[0])
    pair_kv = jnp.concatenate([normed_keys, keyval[:, half_width:]], axis=1).astype(jnp.bfloat16)
    pair_kv = pair_kv.reshape(sites_here, list_width, 2, HEADS, head_size)

    my_queries = jnp.moveaxis(q_blocks, 0, 1).reshape(sites_here, -1)
    queries = head_norm(my_queries, q_gain[0]).astype(jnp.bfloat16)
    query_heads = queries.reshape(sites_here, HEADS, head_size)
    scores = jnp.einsum(
        "nhd,nlhd->nhl", query_heads, pair_kv[:, :, 0], preferred_element_type=jnp.float32
    ) / math.sqrt(head_size)
    exponents = jnp.exp(scores) * my_live.astype(jnp.float32)[:, None, :]
    weights = (exponents / jnp.sum(exponents, axis=-1, keepdims=True)).astype(jnp.bfloat16)
    combined = jnp.einsum(
        "nhl,nlhd->nhd", weights, pair_kv[:, :, 1], preferred_element_type=jnp.float32
    )
    combined = combined.reshape(sites_here, -1).astype(jnp.bfloat16)
    column_blocks = jnp.moveaxis(combined.reshape(sites_here, group_size, -1), 1, 0)
    columns = halving_exchange(column_blocks, group_size, my_index).reshape(
        group_size * sites_here, -1
    )
    attn_part = jnp.dot(columns, out_weight[0], preferred_element_type=jnp.float32)
    attn_part = attn_part.reshape(group_size, sites_here, -1)
    if direct_ok(group_size):
        attn_all = doubling_sum(attn_part, group_size)
        residual_all = everyone.reshape(group_size, sites_here, -1).astype(jnp.float32) + attn_all
        residual = lax.dynamic_index_in_dim(residual_all, my_index, 0, keepdims=False)
        normed_rows = rms_norm(residual_all, ffn_gain[0]).astype(jnp.bfloat16)
        normed_rows = normed_rows.reshape(-1, model_width)
    else:
        attn_sum = halving_sum(attn_part, group_size, my_index)
        residual = current.astype(jnp.float32) + attn_sum
        normed = rms_norm(residual, ffn_gain[0]).astype(jnp.bfloat16)
        normed_rows = doubling_gather(normed, group_size, my_index).reshape(-1, model_width)
    gate_sum = by_rows(normed_rows, gate_weight[0])
    up_sum = by_rows(normed_rows, up_weight[0])
    hidden_ffn = (jax.nn.silu(gate_sum) * up_sum).astype(jnp.bfloat16)
    down_part = jnp.dot(hidden_ffn, down_weight[0], preferred_element_type=jnp.float32)
    down_part = down_part.reshape(group_size, sites_here, -1)
    if not direct_ok(group_size) or group_size == 1:
        down_sum = halving_sum(down_part, group_size, my_index)
        output_rows = (residual + down_sum).astype(jnp.bfloat16)
        return lax.ppermute(output_rows[None], "section", shift_pairs(section_count, 1))
    bits = group_size.bit_length() - 1
    rest = down_part.shape[1:]
    state = down_part.reshape((2,) * bits + rest)
    for bit in range(bits):
        axis = bits - 1 - bit
        mine = (my_index >> bit) & 1
        keep = lax.dynamic_index_in_dim(state, mine, axis, keepdims=True)
        send = lax.dynamic_index_in_dim(state, 1 - mine, axis, keepdims=True)
        if bit < bits - 1:
            state = keep + lax.ppermute(send, "site", xor_pairs(group_size, bit))
            continue
        own = keep.reshape(rest) + residual
        forward = [
            (section * group_size + site, ((section + 1) % section_count) * group_size + site)
            for section in range(section_count)
            for site in range(group_size)
        ]
        across = [
            (
                section * group_size + site,
                ((section + 1) % section_count) * group_size + (site ^ (1 << bit)),
            )
            for section in range(section_count)
            for site in range(group_size)
        ]
        mine_part = lax.ppermute(own, ("section", "site"), forward)
        other_part = lax.ppermute(send.reshape(rest), ("section", "site"), across)
        output_rows = (mine_part + other_part).astype(jnp.bfloat16)
    return output_rows[None]


def ffn_block(rows_ref, gate_ref, up_ref, down_ref, out_ref):
    step = pl.program_id(0)

    @pl.when(step == 0)
    def _():
        out_ref[...] = jnp.zeros_like(out_ref)

    rows = rows_ref[...]
    dims = (((1,), (1,)), ((), ()))
    gate_sum = lax.dot_general(rows, gate_ref[...], dims, preferred_element_type=jnp.float32)
    up_sum = lax.dot_general(rows, up_ref[...], dims, preferred_element_type=jnp.float32)
    hidden = (gate_sum * jax.nn.sigmoid(gate_sum) * up_sum).astype(jnp.bfloat16)
    out_ref[...] += jnp.dot(hidden, down_ref[...], preferred_element_type=jnp.float32)


def gated_ffn(rows, gate, up, down):
    units, width = gate.shape
    block = 128 if units % 128 == 0 else units
    count = rows.shape[0]
    return pl.pallas_call(
        ffn_block,
        grid=(units // block,),
        in_specs=[
            pl.BlockSpec((count, width), lambda i: (0, 0)),
            pl.BlockSpec((block, width), lambda i: (i, 0)),
            pl.BlockSpec((block, width), lambda i: (i, 0)),
            pl.BlockSpec((block, width), lambda i: (i, 0)),
        ],
        out_specs=pl.BlockSpec((count, width), lambda i: (0, 0)),
        out_shape=jax.ShapeDtypeStruct((count, width), jnp.float32),
        compiler_params=pltpu.CompilerParams(dimension_semantics=("arbitrary",)),
    )(rows, gate, up, down)


def heads_split(
    acts,
    patches,
    site_tiles,
    site_count,
    q_weight,
    q_gain,
    k_gain,
    tile_in,
    tile_out,
    out_weight,
    ffn_gain,
    gate_weight,
    up_weight,
    down_weight,
):
    group_size = lax.axis_size("site")
    section_count = lax.axis_size("section")
    my_index = lax.axis_index("site")
    sites_here = acts.shape[1]
    list_width = site_tiles.shape[1]
    tiles_here = patches.shape[1]
    head_size = q_gain.shape[1]
    heads_here = HEADS // group_size
    current = acts[0]
    model_width = current.shape[-1]
    hidden_width = tile_in.shape[-1]
    all_sites = group_size * sites_here

    act_rows = sites_here * model_width // hidden_width
    ring_in = RingGather(
        jnp.concatenate([tile_in[0], current.reshape(act_rows, hidden_width)], axis=0),
        group_size,
        my_index,
    )
    in_slots, in_sources = ring_in.finish()
    in_rows = tile_in.shape[1]
    slot_of_source = jnp.argmax(
        in_sources[None, :] == jnp.arange(group_size, dtype=jnp.int32)[:, None], axis=1
    ).astype(jnp.int32)
    everyone = jnp.take(in_slots[:, in_rows:], slot_of_source, axis=0).reshape(all_sites, model_width)
    weight_in = in_slots[:, :in_rows].reshape(-1, hidden_width)
    own_rows = jnp.take(patches[0].reshape(tiles_here, group_size, -1), in_sources, axis=1)
    tile_hidden = jax.nn.gelu(
        jnp.dot(own_rows.reshape(tiles_here, -1), weight_in, preferred_element_type=jnp.float32),
        approximate=True,
    ).astype(jnp.bfloat16)

    kv_width = tile_out.shape[-1]
    my_cols = heads_here * head_size
    col_blocks = tile_out[0].reshape(tile_out.shape[1], 2, group_size, my_cols)
    col_blocks = jnp.transpose(col_blocks, (2, 0, 1, 3)).reshape(group_size, tile_out.shape[1], 2 * my_cols)
    weight_out = lax.all_to_all(col_blocks, "site", split_axis=0, concat_axis=0, tiled=True)
    weight_out = weight_out.reshape(-1, 2 * my_cols)
    del kv_width

    q_part = by_rows(everyone, q_weight[0]).astype(jnp.bfloat16)
    queries = head_norm(q_part, q_gain[0]).astype(jnp.bfloat16)
    query_heads = queries.reshape(all_sites, heads_here, head_size)

    ring_hidden = RingGather(tile_hidden, group_size, my_index)
    hidden_slots, hidden_sources = ring_hidden.finish()
    table_hidden = hidden_slots.reshape(group_size * tiles_here, hidden_width)
    keyval = jnp.dot(table_hidden, weight_out, preferred_element_type=jnp.float32)
    normed_keys = head_norm(keyval[:, :my_cols], k_gain[0])
    table = jnp.concatenate([normed_keys, keyval[:, my_cols:]], axis=1).astype(jnp.bfloat16)
    table = table.reshape(group_size * tiles_here, 2, heads_here, head_size)

    tile_of_row = (
        hidden_sources[:, None] * tiles_here + jnp.arange(tiles_here, dtype=jnp.int32)[None, :]
    ).reshape(-1)
    slot_index = jnp.arange(list_width, dtype=jnp.int32)
    live = slot_index[None, :] < site_count[:, None]
    named = jnp.logical_and(
        site_tiles[:, :, None] == tile_of_row[None, None, :], live[:, :, None]
    )
    uses = jnp.sum(named.astype(jnp.float32), axis=1)
    scores = jnp.einsum(
        "nhd,rhd->nhr", query_heads, table[:, 0], preferred_element_type=jnp.float32
    ) / math.sqrt(head_size)
    exponents = jnp.exp(scores) * uses[:, None, :]
    weights = (exponents / jnp.sum(exponents, axis=-1, keepdims=True)).astype(jnp.bfloat16)
    combined = jnp.einsum(
        "nhr,rhd->nhd", weights, table[:, 1], preferred_element_type=jnp.float32
    )
    combined = combined.reshape(all_sites, my_cols).astype(jnp.bfloat16)
    attn_part = jnp.dot(combined, out_weight[0], preferred_element_type=jnp.float32)
    attn_all = doubling_sum(attn_part.reshape(group_size, sites_here, -1), group_size)
    residual_all = everyone.reshape(group_size, sites_here, -1).astype(jnp.float32) + attn_all
    residual = lax.dynamic_index_in_dim(residual_all, my_index, 0, keepdims=False)
    normed_rows = rms_norm(residual_all, ffn_gain[0]).astype(jnp.bfloat16).reshape(-1, model_width)
    down_part = gated_ffn(normed_rows, gate_weight[0], up_weight[0], down_weight[0])
    down_part = down_part.reshape(group_size, sites_here, -1)
    return last_round(down_part, residual, group_size, section_count, my_index)


def last_round(down_part, residual, group_size, section_count, my_index):
    bits = group_size.bit_length() - 1
    rest = down_part.shape[1:]
    state = down_part.reshape((2,) * bits + rest)
    for bit in range(bits):
        axis = bits - 1 - bit
        mine = (my_index >> bit) & 1
        keep = lax.dynamic_index_in_dim(state, mine, axis, keepdims=True)
        send = lax.dynamic_index_in_dim(state, 1 - mine, axis, keepdims=True)
        if bit < bits - 1:
            state = keep + lax.ppermute(send, "site", xor_pairs(group_size, bit))
            continue
        own = keep.reshape(rest) + residual
        forward = [
            (section * group_size + site, ((section + 1) % section_count) * group_size + site)
            for section in range(section_count)
            for site in range(group_size)
        ]
        across = [
            (
                section * group_size + site,
                ((section + 1) % section_count) * group_size + (site ^ (1 << bit)),
            )
            for section in range(section_count)
            for site in range(group_size)
        ]
        mine_part = lax.ppermute(own, ("section", "site"), forward)
        other_part = lax.ppermute(send.reshape(rest), ("section", "site"), across)
        return (mine_part + other_part).astype(jnp.bfloat16)[None]


def solution(mesh):
    group_size = mesh.shape["site"]
    split_heads = (
        direct_ok(group_size)
        and group_size > 1
        and HEADS % group_size == 0
        and mesh.shape["section"] > 0
    )
    return jax.shard_map(
        heads_split if split_heads else shards,
        mesh=mesh,
        in_specs=(
            P("section", "site", None),
            P("section", "site", None),
            P(),
            P(),
            P("section", "site", None),
            P("section", None),
            P("section", None),
            P("section", "site", None),
            P("section", "site", None),
            P("section", "site", None),
            P("section", None),
            P("section", "site", None),
            P("section", "site", None),
            P("section", "site", None),
        ),
        out_specs=P("section", "site", None),
        check_vma=False,
    )
```

```python
import math

import jax
import jax.numpy as jnp
from jax import lax
from jax.experimental import pallas as pl
from jax.experimental.pallas import tpu as pltpu
from jax.sharding import PartitionSpec as P

HEADS = 16


epsilon = 1e-05

DIRECT_LIMIT = 8


def shift_pairs(count, steps):
    return [(source, (source + steps) % count) for source in range(count)]


def by_rows(left, weight_rows):
    return lax.dot_general(
        left, weight_rows, (((1,), (1,)), ((), ())), preferred_element_type=jnp.float32
    )


def head_norm(values, gain_row):
    shaped = values.astype(jnp.float32).reshape(values.shape[0], -1, gain_row.shape[0])
    scaled = (
        shaped * lax.rsqrt(jnp.mean(shaped * shaped, axis=-1, keepdims=True) + epsilon) * gain_row
    )
    return scaled.reshape(values.shape[0], -1)


def rms_norm(values, gain_row):
    return (
        values * lax.rsqrt(jnp.mean(values * values, axis=-1, keepdims=True) + epsilon) * gain_row
    )


def to_source_order(slots, count, me):
    return jnp.take(slots, (me - jnp.arange(count, dtype=jnp.int32)) % count, axis=0)


def xor_pairs(count, bit):
    return [(source, source ^ (1 << bit)) for source in range(count)]


def direct_ok(count):
    return count <= DIRECT_LIMIT and count & (count - 1) == 0


def site_exchange(by_target, count, me):
    if not direct_ok(count):
        return lax.all_to_all(by_target, "site", split_axis=0, concat_axis=0, tiled=True)
    slots = [lax.dynamic_index_in_dim(by_target, me, 0, keepdims=False)]
    for steps in range(1, count):
        piece = lax.dynamic_index_in_dim(by_target, (me + steps) % count, 0, keepdims=False)
        slots.append(lax.ppermute(piece, "site", shift_pairs(count, steps)))
    return to_source_order(jnp.stack(slots), count, me)


def halving_exchange(by_target, count, me):
    if not direct_ok(count):
        return lax.all_to_all(by_target, "site", split_axis=0, concat_axis=0, tiled=True)
    bits = count.bit_length() - 1
    rest = by_target.shape[1:]
    state = by_target.reshape((2,) * bits + rest)
    for bit in range(bits):
        axis = bits - 1 - bit
        mine = (me >> bit) & 1
        keep = lax.dynamic_index_in_dim(state, mine, axis, keepdims=True)
        send = lax.dynamic_index_in_dim(state, 1 - mine, axis, keepdims=True)
        recv = lax.ppermute(send, "site", xor_pairs(count, bit))
        state = jnp.where(
            mine == 0,
            jnp.concatenate([keep, recv], axis),
            jnp.concatenate([recv, keep], axis),
        )
    return state.reshape((count,) + rest)


def doubling_gather(value, count, me):
    if not direct_ok(count):
        return lax.all_gather(value, "site", axis=0, tiled=False)
    bits = count.bit_length() - 1
    state = value[None]
    for bit in range(bits):
        recv = lax.ppermute(state, "site", xor_pairs(count, bit))
        mine = (me >> bit) & 1
        state = jnp.where(
            mine == 0, jnp.concatenate([state, recv], 0), jnp.concatenate([recv, state], 0)
        )
    return state


def halving_sum(parts, count, me):
    if not direct_ok(count):
        return lax.psum_scatter(parts, "site", scatter_dimension=0, tiled=True)[0]
    bits = count.bit_length() - 1
    rest = parts.shape[1:]
    state = parts.reshape((2,) * bits + rest)
    for bit in range(bits):
        axis = bits - 1 - bit
        mine = (me >> bit) & 1
        keep = lax.dynamic_index_in_dim(state, mine, axis, keepdims=True)
        send = lax.dynamic_index_in_dim(state, 1 - mine, axis, keepdims=True)
        state = keep + lax.ppermute(send, "site", xor_pairs(count, bit))
    return state.reshape(rest)


def doubling_sum(parts, count):
    state = parts
    for bit in range(count.bit_length() - 1):
        state = state + lax.ppermute(state, "site", xor_pairs(count, bit))
    return state


class RingGather:
    def __init__(self, value, count, me):
        self.count = count
        self.direct = direct_ok(count)
        if not self.direct:
            self.slots = lax.all_gather(value, "site", axis=0, tiled=False)
            self.sources = jnp.arange(count, dtype=jnp.int32)
            return
        order = list(range(0, count, 2)) + [i for i in range(count - 1, -1, -1) if i % 2 == 1]
        place = [0] * count
        for position, device in enumerate(order):
            place[device] = position
        self.forward = [(order[p], order[(p + 1) % count]) for p in range(count)]
        self.backward = [(order[p], order[(p - 1) % count]) for p in range(count)]
        self.forward_left = count // 2
        self.backward_left = count - 1 - self.forward_left
        offsets = [0] + [-s for s in range(1, self.forward_left + 1)]
        offsets += list(range(1, self.backward_left + 1))
        my_place = jnp.array(place, dtype=jnp.int32)[me]
        self.sources = jnp.array(order, dtype=jnp.int32)[
            (my_place + jnp.array(offsets, dtype=jnp.int32)) % count
        ]
        self.forward_slots = []
        self.backward_slots = []
        self.ahead = value
        self.behind = value
        self.value = value
        self._issue()

    def _issue(self):
        if self.forward_left > 0:
            self.ahead = lax.ppermute(self.ahead, "site", self.forward)
            self.forward_slots.append(self.ahead)
            self.forward_left -= 1
        if self.backward_left > 0:
            self.behind = lax.ppermute(self.behind, "site", self.backward)
            self.backward_slots.append(self.behind)
            self.backward_left -= 1

    def step(self, tied):
        if not self.direct or (self.forward_left == 0 and self.backward_left == 0):
            return tied
        self.ahead, self.behind, tied = lax.optimization_barrier((self.ahead, self.behind, tied))
        self.forward_slots[-1] = self.ahead
        if self.backward_slots:
            self.backward_slots[-1] = self.behind
        self._issue()
        return tied

    def slots_in_arrival(self):
        if not self.direct:
            return [self.slots[i] for i in range(self.count)], [self.sources[i] for i in range(self.count)]
        while self.forward_left > 0 or self.backward_left > 0:
            self._issue()
        slots = [self.value]
        positions = [0]
        forward_count = len(self.forward_slots)
        for step in range(max(forward_count, len(self.backward_slots))):
            if step < forward_count:
                slots.append(self.forward_slots[step])
                positions.append(1 + step)
            if step < len(self.backward_slots):
                slots.append(self.backward_slots[step])
                positions.append(1 + forward_count + step)
        return slots, [self.sources[p] for p in positions]

    def finish(self):
        if not self.direct:
            return self.slots, self.sources
        while self.forward_left > 0 or self.backward_left > 0:
            self._issue()
        slots = [self.value] + self.forward_slots + self.backward_slots
        return jnp.stack(slots), self.sources


def shards(
    acts,
    patches,
    site_tiles,
    site_count,
    q_weight,
    q_gain,
    k_gain,
    tile_in,
    tile_out,
    out_weight,
    ffn_gain,
    gate_weight,
    up_weight,
    down_weight,
):
    group_size = lax.axis_size("site")
    section_count = lax.axis_size("section")
    my_index = lax.axis_index("site")
    sites_here = acts.shape[1]
    list_width = site_tiles.shape[1]
    tiles_here = patches.shape[1]
    head_size = q_gain.shape[1]
    capacity = max(2, 5 * sites_here * list_width // (4 * group_size))
    entries = sites_here * list_width
    current = acts[0]
    model_width = current.shape[-1]
    row_width = patches.shape[-1]

    ring_in = RingGather(tile_in[0], group_size, my_index)
    in_slots, in_sources = ring_in.finish()
    ring_out = RingGather(tile_out[0], group_size, my_index)
    weight_in = in_slots.reshape(-1, in_slots.shape[-1])
    own_rows = jnp.take(patches[0].reshape(tiles_here, group_size, -1), in_sources, axis=1)
    tile_hidden = jax.nn.gelu(
        jnp.dot(own_rows.reshape(tiles_here, -1), weight_in, preferred_element_type=jnp.float32),
        approximate=True,
    ).astype(jnp.bfloat16)
    hidden_width = tile_hidden.shape[-1]

    slot_index = jnp.arange(list_width, dtype=jnp.int32)
    live_all = (slot_index[None, :] < site_count[:, None]).reshape(group_size, entries)
    owner_all = (site_tiles // tiles_here).reshape(group_size, entries)
    local_all = (site_tiles % tiles_here).reshape(group_size, entries)
    mine_mask = jnp.logical_and(live_all, owner_all == my_index)
    slot_rank = jnp.cumsum(mine_mask.astype(jnp.int32), axis=1) - 1
    picks = jnp.logical_and(
        mine_mask[:, :, None],
        slot_rank[:, :, None] == jnp.arange(capacity, dtype=jnp.int32)[None, None, :],
    )
    send_index = jnp.sum(jnp.where(picks, local_all[:, :, None], 0), axis=1)
    send_rows = tile_hidden[send_index.reshape(-1)].reshape(group_size, capacity, hidden_width)
    act_rows = sites_here * model_width // hidden_width
    packed = model_width % hidden_width == 0
    if packed:
        act_block = jnp.broadcast_to(
            current.reshape(1, act_rows, hidden_width), (group_size, act_rows, hidden_width)
        )
        send_rows = jnp.concatenate([send_rows, act_block], axis=1)
    send_rows = ring_out.step(send_rows)
    arrived = lax.all_to_all(send_rows, "site", split_axis=0, concat_axis=0, tiled=True)
    if packed:
        everyone = arrived[:, capacity:].reshape(-1, model_width)
        arrived = arrived[:, :capacity]
    else:
        everyone = doubling_gather(current, group_size, my_index).reshape(-1, model_width)
    q_part = by_rows(everyone, q_weight[0]).astype(jnp.bfloat16)
    q_part = ring_out.step(q_part)
    q_blocks = halving_exchange(
        q_part.reshape(group_size, sites_here, -1), group_size, my_index
    )
    q_blocks = ring_out.step(q_blocks)

    my_tiles = lax.dynamic_slice_in_dim(site_tiles, my_index * sites_here, sites_here, 0)
    my_count = lax.dynamic_slice_in_dim(site_count, my_index * sites_here, sites_here, 0)
    my_live = slot_index[None, :] < my_count[:, None]
    my_owner = (my_tiles // tiles_here).reshape(-1)
    one_hot = jnp.logical_and(
        my_owner[:, None] == jnp.arange(group_size, dtype=jnp.int32)[None, :],
        my_live.reshape(-1)[:, None],
    ).astype(jnp.int32)
    my_rank = jnp.sum(jnp.cumsum(one_hot, axis=0) * one_hot, axis=1) - 1
    fetch_index = jnp.where(my_live.reshape(-1), my_owner * capacity + my_rank, 0)
    pair_hidden = arrived.reshape(group_size * capacity, hidden_width)[fetch_index]

    shard_rows = tile_out.shape[1]
    keyval = None
    if not ring_out.direct:
        out_slots, out_sources = [ring_out.slots.reshape(-1, ring_out.slots.shape[-1])], [0]
        shard_rows = hidden_width
    else:
        out_slots, out_sources = ring_out.slots_in_arrival()
    for slot, source in zip(out_slots, out_sources):
        columns_here = lax.dynamic_slice_in_dim(pair_hidden, source * shard_rows, shard_rows, 1)
        term = jnp.dot(columns_here, slot, preferred_element_type=jnp.float32)
        keyval = term if keyval is None else keyval + term
    half_width = keyval.shape[1] // 2
    normed_keys = head_norm(keyval[:, :half_width], k_gain[0])
    pair_kv = jnp.concatenate([normed_keys, keyval[:, half_width:]], axis=1).astype(jnp.bfloat16)
    pair_kv = pair_kv.reshape(sites_here, list_width, 2, HEADS, head_size)

    my_queries = jnp.moveaxis(q_blocks, 0, 1).reshape(sites_here, -1)
    queries = head_norm(my_queries, q_gain[0]).astype(jnp.bfloat16)
    query_heads = queries.reshape(sites_here, HEADS, head_size)
    scores = jnp.einsum(
        "nhd,nlhd->nhl", query_heads, pair_kv[:, :, 0], preferred_element_type=jnp.float32
    ) / math.sqrt(head_size)
    exponents = jnp.exp(scores) * my_live.astype(jnp.float32)[:, None, :]
    weights = (exponents / jnp.sum(exponents, axis=-1, keepdims=True)).astype(jnp.bfloat16)
    combined = jnp.einsum(
        "nhl,nlhd->nhd", weights, pair_kv[:, :, 1], preferred_element_type=jnp.float32
    )
    combined = combined.reshape(sites_here, -1).astype(jnp.bfloat16)
    column_blocks = jnp.moveaxis(combined.reshape(sites_here, group_size, -1), 1, 0)
    columns = halving_exchange(column_blocks, group_size, my_index).reshape(
        group_size * sites_here, -1
    )
    attn_part = jnp.dot(columns, out_weight[0], preferred_element_type=jnp.float32)
    attn_part = attn_part.reshape(group_size, sites_here, -1)
    if direct_ok(group_size):
        attn_all = doubling_sum(attn_part, group_size)
        residual_all = everyone.reshape(group_size, sites_here, -1).astype(jnp.float32) + attn_all
        residual = lax.dynamic_index_in_dim(residual_all, my_index, 0, keepdims=False)
        normed_rows = rms_norm(residual_all, ffn_gain[0]).astype(jnp.bfloat16)
        normed_rows = normed_rows.reshape(-1, model_width)
    else:
        attn_sum = halving_sum(attn_part, group_size, my_index)
        residual = current.astype(jnp.float32) + attn_sum
        normed = rms_norm(residual, ffn_gain[0]).astype(jnp.bfloat16)
        normed_rows = doubling_gather(normed, group_size, my_index).reshape(-1, model_width)
    gate_sum = by_rows(normed_rows, gate_weight[0])
    up_sum = by_rows(normed_rows, up_weight[0])
    hidden_ffn = (jax.nn.silu(gate_sum) * up_sum).astype(jnp.bfloat16)
    down_part = jnp.dot(hidden_ffn, down_weight[0], preferred_element_type=jnp.float32)
    down_part = down_part.reshape(group_size, sites_here, -1)
    if not direct_ok(group_size) or group_size == 1:
        down_sum = halving_sum(down_part, group_size, my_index)
        output_rows = (residual + down_sum).astype(jnp.bfloat16)
        return lax.ppermute(output_rows[None], "section", shift_pairs(section_count, 1))
    bits = group_size.bit_length() - 1
    rest = down_part.shape[1:]
    state = down_part.reshape((2,) * bits + rest)
    for bit in range(bits):
        axis = bits - 1 - bit
        mine = (my_index >> bit) & 1
        keep = lax.dynamic_index_in_dim(state, mine, axis, keepdims=True)
        send = lax.dynamic_index_in_dim(state, 1 - mine, axis, keepdims=True)
        if bit < bits - 1:
            state = keep + lax.ppermute(send, "site", xor_pairs(group_size, bit))
            continue
        own = keep.reshape(rest) + residual
        forward = [
            (section * group_size + site, ((section + 1) % section_count) * group_size + site)
            for section in range(section_count)
            for site in range(group_size)
        ]
        across = [
            (
                section * group_size + site,
                ((section + 1) % section_count) * group_size + (site ^ (1 << bit)),
            )
            for section in range(section_count)
            for site in range(group_size)
        ]
        mine_part = lax.ppermute(own, ("section", "site"), forward)
        other_part = lax.ppermute(send.reshape(rest), ("section", "site"), across)
        output_rows = (mine_part + other_part).astype(jnp.bfloat16)
    return output_rows[None]


def ffn_block(rows_ref, gate_ref, up_ref, down_ref, out_ref):
    step = pl.program_id(0)

    @pl.when(step == 0)
    def _():
        out_ref[...] = jnp.zeros_like(out_ref)

    rows = rows_ref[...]
    dims = (((1,), (1,)), ((), ()))
    gate_sum = lax.dot_general(rows, gate_ref[...], dims, preferred_element_type=jnp.float32)
    up_sum = lax.dot_general(rows, up_ref[...], dims, preferred_element_type=jnp.float32)
    hidden = (gate_sum * jax.nn.sigmoid(gate_sum) * up_sum).astype(jnp.bfloat16)
    out_ref[...] += jnp.dot(hidden, down_ref[...], preferred_element_type=jnp.float32)


def gated_ffn(rows, gate, up, down):
    units, width = gate.shape
    block = 128 if units % 128 == 0 else units
    count = rows.shape[0]
    return pl.pallas_call(
        ffn_block,
        grid=(units // block,),
        in_specs=[
            pl.BlockSpec((count, width), lambda i: (0, 0)),
            pl.BlockSpec((block, width), lambda i: (i, 0)),
            pl.BlockSpec((block, width), lambda i: (i, 0)),
            pl.BlockSpec((block, width), lambda i: (i, 0)),
        ],
        out_specs=pl.BlockSpec((count, width), lambda i: (0, 0)),
        out_shape=jax.ShapeDtypeStruct((count, width), jnp.float32),
        compiler_params=pltpu.CompilerParams(dimension_semantics=("arbitrary",)),
    )(rows, gate, up, down)


class DirectGather:
    def __init__(self, value, count, me):
        self.slots = [value] + [
            lax.ppermute(value, "site", shift_pairs(count, steps)) for steps in range(1, count)
        ]
        self.sources = (me - jnp.arange(count, dtype=jnp.int32)) % count

    def finish(self):
        return jnp.stack(self.slots), self.sources


def heads_split(
    acts,
    patches,
    site_tiles,
    site_count,
    q_weight,
    q_gain,
    k_gain,
    tile_in,
    tile_out,
    out_weight,
    ffn_gain,
    gate_weight,
    up_weight,
    down_weight,
):
    group_size = lax.axis_size("site")
    section_count = lax.axis_size("section")
    my_index = lax.axis_index("site")
    sites_here = acts.shape[1]
    list_width = site_tiles.shape[1]
    tiles_here = patches.shape[1]
    head_size = q_gain.shape[1]
    heads_here = HEADS // group_size
    current = acts[0]
    model_width = current.shape[-1]
    hidden_width = tile_in.shape[-1]
    all_sites = group_size * sites_here

    act_rows = sites_here * model_width // hidden_width
    ring_in = DirectGather(
        jnp.concatenate([tile_in[0], current.reshape(act_rows, hidden_width)], axis=0),
        group_size,
        my_index,
    )
    in_slots, in_sources = ring_in.finish()
    in_rows = tile_in.shape[1]
    slot_of_source = jnp.argmax(
        in_sources[None, :] == jnp.arange(group_size, dtype=jnp.int32)[:, None], axis=1
    ).astype(jnp.int32)
    everyone = jnp.take(in_slots[:, in_rows:], slot_of_source, axis=0).reshape(all_sites, model_width)
    weight_in = in_slots[:, :in_rows].reshape(-1, hidden_width)
    own_rows = jnp.take(patches[0].reshape(tiles_here, group_size, -1), in_sources, axis=1)
    tile_hidden = jax.nn.gelu(
        jnp.dot(own_rows.reshape(tiles_here, -1), weight_in, preferred_element_type=jnp.float32),
        approximate=True,
    ).astype(jnp.bfloat16)

    kv_width = tile_out.shape[-1]
    my_cols = heads_here * head_size
    col_blocks = tile_out[0].reshape(tile_out.shape[1], 2, group_size, my_cols)
    col_blocks = jnp.transpose(col_blocks, (2, 0, 1, 3)).reshape(group_size, tile_out.shape[1], 2 * my_cols)
    weight_out = lax.all_to_all(col_blocks, "site", split_axis=0, concat_axis=0, tiled=True)
    weight_out = weight_out.reshape(-1, 2 * my_cols)
    del kv_width

    q_part = by_rows(everyone, q_weight[0]).astype(jnp.bfloat16)
    queries = head_norm(q_part, q_gain[0]).astype(jnp.bfloat16)
    query_heads = queries.reshape(all_sites, heads_here, head_size)

    ring_hidden = RingGather(tile_hidden, group_size, my_index)
    hidden_slots, hidden_sources = ring_hidden.finish()
    table_hidden = hidden_slots.reshape(group_size * tiles_here, hidden_width)
    keyval = jnp.dot(table_hidden, weight_out, preferred_element_type=jnp.float32)
    normed_keys = head_norm(keyval[:, :my_cols], k_gain[0])
    table = jnp.concatenate([normed_keys, keyval[:, my_cols:]], axis=1).astype(jnp.bfloat16)
    table = table.reshape(group_size * tiles_here, 2, heads_here, head_size)

    tile_of_row = (
        hidden_sources[:, None] * tiles_here + jnp.arange(tiles_here, dtype=jnp.int32)[None, :]
    ).reshape(-1)
    slot_index = jnp.arange(list_width, dtype=jnp.int32)
    live = slot_index[None, :] < site_count[:, None]
    named = jnp.logical_and(
        site_tiles[:, :, None] == tile_of_row[None, None, :], live[:, :, None]
    )
    uses = jnp.sum(named.astype(jnp.float32), axis=1)
    scores = jnp.einsum(
        "nhd,rhd->nhr", query_heads, table[:, 0], preferred_element_type=jnp.float32
    ) / math.sqrt(head_size)
    exponents = jnp.exp(scores) * uses[:, None, :]
    weights = (exponents / jnp.sum(exponents, axis=-1, keepdims=True)).astype(jnp.bfloat16)
    combined = jnp.einsum(
        "nhr,rhd->nhd", weights, table[:, 1], preferred_element_type=jnp.float32
    )
    combined = combined.reshape(all_sites, my_cols).astype(jnp.bfloat16)
    attn_part = jnp.dot(combined, out_weight[0], preferred_element_type=jnp.float32)
    attn_all = doubling_sum(attn_part.reshape(group_size, sites_here, -1), group_size)
    residual_all = everyone.reshape(group_size, sites_here, -1).astype(jnp.float32) + attn_all
    residual = lax.dynamic_index_in_dim(residual_all, my_index, 0, keepdims=False)
    normed_rows = rms_norm(residual_all, ffn_gain[0]).astype(jnp.bfloat16).reshape(-1, model_width)
    down_part = gated_ffn(normed_rows, gate_weight[0], up_weight[0], down_weight[0])
    down_part = down_part.reshape(group_size, sites_here, -1)
    return last_round(down_part, residual, group_size, section_count, my_index)


def last_round(down_part, residual, group_size, section_count, my_index):
    bits = group_size.bit_length() - 1
    rest = down_part.shape[1:]
    state = down_part.reshape((2,) * bits + rest)
    for bit in range(bits):
        axis = bits - 1 - bit
        mine = (my_index >> bit) & 1
        keep = lax.dynamic_index_in_dim(state, mine, axis, keepdims=True)
        send = lax.dynamic_index_in_dim(state, 1 - mine, axis, keepdims=True)
        if bit < bits - 1:
            state = keep + lax.ppermute(send, "site", xor_pairs(group_size, bit))
            continue
        own = keep.reshape(rest) + residual
        forward = [
            (section * group_size + site, ((section + 1) % section_count) * group_size + site)
            for section in range(section_count)
            for site in range(group_size)
        ]
        across = [
            (
                section * group_size + site,
                ((section + 1) % section_count) * group_size + (site ^ (1 << bit)),
            )
            for section in range(section_count)
            for site in range(group_size)
        ]
        mine_part = lax.ppermute(own, ("section", "site"), forward)
        other_part = lax.ppermute(send.reshape(rest), ("section", "site"), across)
        return (mine_part + other_part).astype(jnp.bfloat16)[None]


def solution(mesh):
    group_size = mesh.shape["site"]
    split_heads = (
        direct_ok(group_size)
        and group_size > 1
        and HEADS % group_size == 0
        and mesh.shape["section"] > 0
    )
    return jax.shard_map(
        heads_split if split_heads else shards,
        mesh=mesh,
        in_specs=(
            P("section", "site", None),
            P("section", "site", None),
            P(),
            P(),
            P("section", "site", None),
            P("section", None),
            P("section", None),
            P("section", "site", None),
            P("section", "site", None),
            P("section", "site", None),
            P("section", None),
            P("section", "site", None),
            P("section", "site", None),
            P("section", "site", None),
        ),
        out_specs=P("section", "site", None),
        check_vma=False,
    )
```

```python
import math

import jax
import jax.numpy as jnp
from jax import lax
from jax.experimental import pallas as pl
from jax.experimental.pallas import tpu as pltpu
from jax.sharding import PartitionSpec as P

HEADS = 16


epsilon = 1e-05

DIRECT_LIMIT = 8


def shift_pairs(count, steps):
    return [(source, (source + steps) % count) for source in range(count)]


def by_rows(left, weight_rows):
    return lax.dot_general(
        left, weight_rows, (((1,), (1,)), ((), ())), preferred_element_type=jnp.float32
    )


def head_norm(values, gain_row):
    shaped = values.astype(jnp.float32).reshape(values.shape[0], -1, gain_row.shape[0])
    scaled = (
        shaped * lax.rsqrt(jnp.mean(shaped * shaped, axis=-1, keepdims=True) + epsilon) * gain_row
    )
    return scaled.reshape(values.shape[0], -1)


def rms_norm(values, gain_row):
    return (
        values * lax.rsqrt(jnp.mean(values * values, axis=-1, keepdims=True) + epsilon) * gain_row
    )


def to_source_order(slots, count, me):
    return jnp.take(slots, (me - jnp.arange(count, dtype=jnp.int32)) % count, axis=0)


def xor_pairs(count, bit):
    return [(source, source ^ (1 << bit)) for source in range(count)]


def direct_ok(count):
    return count <= DIRECT_LIMIT and count & (count - 1) == 0


def site_exchange(by_target, count, me):
    if not direct_ok(count):
        return lax.all_to_all(by_target, "site", split_axis=0, concat_axis=0, tiled=True)
    slots = [lax.dynamic_index_in_dim(by_target, me, 0, keepdims=False)]
    for steps in range(1, count):
        piece = lax.dynamic_index_in_dim(by_target, (me + steps) % count, 0, keepdims=False)
        slots.append(lax.ppermute(piece, "site", shift_pairs(count, steps)))
    return to_source_order(jnp.stack(slots), count, me)


def halving_exchange(by_target, count, me):
    if not direct_ok(count):
        return lax.all_to_all(by_target, "site", split_axis=0, concat_axis=0, tiled=True)
    bits = count.bit_length() - 1
    rest = by_target.shape[1:]
    state = by_target.reshape((2,) * bits + rest)
    for bit in range(bits):
        axis = bits - 1 - bit
        mine = (me >> bit) & 1
        keep = lax.dynamic_index_in_dim(state, mine, axis, keepdims=True)
        send = lax.dynamic_index_in_dim(state, 1 - mine, axis, keepdims=True)
        recv = lax.ppermute(send, "site", xor_pairs(count, bit))
        state = jnp.where(
            mine == 0,
            jnp.concatenate([keep, recv], axis),
            jnp.concatenate([recv, keep], axis),
        )
    return state.reshape((count,) + rest)


def doubling_gather(value, count, me):
    if not direct_ok(count):
        return lax.all_gather(value, "site", axis=0, tiled=False)
    bits = count.bit_length() - 1
    state = value[None]
    for bit in range(bits):
        recv = lax.ppermute(state, "site", xor_pairs(count, bit))
        mine = (me >> bit) & 1
        state = jnp.where(
            mine == 0, jnp.concatenate([state, recv], 0), jnp.concatenate([recv, state], 0)
        )
    return state


def halving_sum(parts, count, me):
    if not direct_ok(count):
        return lax.psum_scatter(parts, "site", scatter_dimension=0, tiled=True)[0]
    bits = count.bit_length() - 1
    rest = parts.shape[1:]
    state = parts.reshape((2,) * bits + rest)
    for bit in range(bits):
        axis = bits - 1 - bit
        mine = (me >> bit) & 1
        keep = lax.dynamic_index_in_dim(state, mine, axis, keepdims=True)
        send = lax.dynamic_index_in_dim(state, 1 - mine, axis, keepdims=True)
        state = keep + lax.ppermute(send, "site", xor_pairs(count, bit))
    return state.reshape(rest)


def doubling_sum(parts, count):
    state = parts
    for bit in range(count.bit_length() - 1):
        state = state + lax.ppermute(state, "site", xor_pairs(count, bit))
    return state


class RingGather:
    def __init__(self, value, count, me):
        self.count = count
        self.direct = direct_ok(count)
        if not self.direct:
            self.slots = lax.all_gather(value, "site", axis=0, tiled=False)
            self.sources = jnp.arange(count, dtype=jnp.int32)
            return
        order = list(range(0, count, 2)) + [i for i in range(count - 1, -1, -1) if i % 2 == 1]
        place = [0] * count
        for position, device in enumerate(order):
            place[device] = position
        self.forward = [(order[p], order[(p + 1) % count]) for p in range(count)]
        self.backward = [(order[p], order[(p - 1) % count]) for p in range(count)]
        self.forward_left = count // 2
        self.backward_left = count - 1 - self.forward_left
        offsets = [0] + [-s for s in range(1, self.forward_left + 1)]
        offsets += list(range(1, self.backward_left + 1))
        my_place = jnp.array(place, dtype=jnp.int32)[me]
        self.sources = jnp.array(order, dtype=jnp.int32)[
            (my_place + jnp.array(offsets, dtype=jnp.int32)) % count
        ]
        self.forward_slots = []
        self.backward_slots = []
        self.ahead = value
        self.behind = value
        self.value = value
        self._issue()

    def _issue(self):
        if self.forward_left > 0:
            self.ahead = lax.ppermute(self.ahead, "site", self.forward)
            self.forward_slots.append(self.ahead)
            self.forward_left -= 1
        if self.backward_left > 0:
            self.behind = lax.ppermute(self.behind, "site", self.backward)
            self.backward_slots.append(self.behind)
            self.backward_left -= 1

    def step(self, tied):
        if not self.direct or (self.forward_left == 0 and self.backward_left == 0):
            return tied
        self.ahead, self.behind, tied = lax.optimization_barrier((self.ahead, self.behind, tied))
        self.forward_slots[-1] = self.ahead
        if self.backward_slots:
            self.backward_slots[-1] = self.behind
        self._issue()
        return tied

    def slots_in_arrival(self):
        if not self.direct:
            return [self.slots[i] for i in range(self.count)], [self.sources[i] for i in range(self.count)]
        while self.forward_left > 0 or self.backward_left > 0:
            self._issue()
        slots = [self.value]
        positions = [0]
        forward_count = len(self.forward_slots)
        for step in range(max(forward_count, len(self.backward_slots))):
            if step < forward_count:
                slots.append(self.forward_slots[step])
                positions.append(1 + step)
            if step < len(self.backward_slots):
                slots.append(self.backward_slots[step])
                positions.append(1 + forward_count + step)
        return slots, [self.sources[p] for p in positions]

    def finish(self):
        if not self.direct:
            return self.slots, self.sources
        while self.forward_left > 0 or self.backward_left > 0:
            self._issue()
        slots = [self.value] + self.forward_slots + self.backward_slots
        return jnp.stack(slots), self.sources


def shards(
    acts,
    patches,
    site_tiles,
    site_count,
    q_weight,
    q_gain,
    k_gain,
    tile_in,
    tile_out,
    out_weight,
    ffn_gain,
    gate_weight,
    up_weight,
    down_weight,
):
    group_size = lax.axis_size("site")
    section_count = lax.axis_size("section")
    my_index = lax.axis_index("site")
    sites_here = acts.shape[1]
    list_width = site_tiles.shape[1]
    tiles_here = patches.shape[1]
    head_size = q_gain.shape[1]
    capacity = max(2, 5 * sites_here * list_width // (4 * group_size))
    entries = sites_here * list_width
    current = acts[0]
    model_width = current.shape[-1]
    row_width = patches.shape[-1]

    ring_in = RingGather(tile_in[0], group_size, my_index)
    in_slots, in_sources = ring_in.finish()
    ring_out = RingGather(tile_out[0], group_size, my_index)
    weight_in = in_slots.reshape(-1, in_slots.shape[-1])
    own_rows = jnp.take(patches[0].reshape(tiles_here, group_size, -1), in_sources, axis=1)
    tile_hidden = jax.nn.gelu(
        jnp.dot(own_rows.reshape(tiles_here, -1), weight_in, preferred_element_type=jnp.float32),
        approximate=True,
    ).astype(jnp.bfloat16)
    hidden_width = tile_hidden.shape[-1]

    slot_index = jnp.arange(list_width, dtype=jnp.int32)
    live_all = (slot_index[None, :] < site_count[:, None]).reshape(group_size, entries)
    owner_all = (site_tiles // tiles_here).reshape(group_size, entries)
    local_all = (site_tiles % tiles_here).reshape(group_size, entries)
    mine_mask = jnp.logical_and(live_all, owner_all == my_index)
    slot_rank = jnp.cumsum(mine_mask.astype(jnp.int32), axis=1) - 1
    picks = jnp.logical_and(
        mine_mask[:, :, None],
        slot_rank[:, :, None] == jnp.arange(capacity, dtype=jnp.int32)[None, None, :],
    )
    send_index = jnp.sum(jnp.where(picks, local_all[:, :, None], 0), axis=1)
    send_rows = tile_hidden[send_index.reshape(-1)].reshape(group_size, capacity, hidden_width)
    act_rows = sites_here * model_width // hidden_width
    packed = model_width % hidden_width == 0
    if packed:
        act_block = jnp.broadcast_to(
            current.reshape(1, act_rows, hidden_width), (group_size, act_rows, hidden_width)
        )
        send_rows = jnp.concatenate([send_rows, act_block], axis=1)
    send_rows = ring_out.step(send_rows)
    arrived = lax.all_to_all(send_rows, "site", split_axis=0, concat_axis=0, tiled=True)
    if packed:
        everyone = arrived[:, capacity:].reshape(-1, model_width)
        arrived = arrived[:, :capacity]
    else:
        everyone = doubling_gather(current, group_size, my_index).reshape(-1, model_width)
    q_part = by_rows(everyone, q_weight[0]).astype(jnp.bfloat16)
    q_part = ring_out.step(q_part)
    q_blocks = halving_exchange(
        q_part.reshape(group_size, sites_here, -1), group_size, my_index
    )
    q_blocks = ring_out.step(q_blocks)

    my_tiles = lax.dynamic_slice_in_dim(site_tiles, my_index * sites_here, sites_here, 0)
    my_count = lax.dynamic_slice_in_dim(site_count, my_index * sites_here, sites_here, 0)
    my_live = slot_index[None, :] < my_count[:, None]
    my_owner = (my_tiles // tiles_here).reshape(-1)
    one_hot = jnp.logical_and(
        my_owner[:, None] == jnp.arange(group_size, dtype=jnp.int32)[None, :],
        my_live.reshape(-1)[:, None],
    ).astype(jnp.int32)
    my_rank = jnp.sum(jnp.cumsum(one_hot, axis=0) * one_hot, axis=1) - 1
    fetch_index = jnp.where(my_live.reshape(-1), my_owner * capacity + my_rank, 0)
    pair_hidden = arrived.reshape(group_size * capacity, hidden_width)[fetch_index]

    shard_rows = tile_out.shape[1]
    keyval = None
    if not ring_out.direct:
        out_slots, out_sources = [ring_out.slots.reshape(-1, ring_out.slots.shape[-1])], [0]
        shard_rows = hidden_width
    else:
        out_slots, out_sources = ring_out.slots_in_arrival()
    for slot, source in zip(out_slots, out_sources):
        columns_here = lax.dynamic_slice_in_dim(pair_hidden, source * shard_rows, shard_rows, 1)
        term = jnp.dot(columns_here, slot, preferred_element_type=jnp.float32)
        keyval = term if keyval is None else keyval + term
    half_width = keyval.shape[1] // 2
    normed_keys = head_norm(keyval[:, :half_width], k_gain[0])
    pair_kv = jnp.concatenate([normed_keys, keyval[:, half_width:]], axis=1).astype(jnp.bfloat16)
    pair_kv = pair_kv.reshape(sites_here, list_width, 2, HEADS, head_size)

    my_queries = jnp.moveaxis(q_blocks, 0, 1).reshape(sites_here, -1)
    queries = head_norm(my_queries, q_gain[0]).astype(jnp.bfloat16)
    query_heads = queries.reshape(sites_here, HEADS, head_size)
    scores = jnp.einsum(
        "nhd,nlhd->nhl", query_heads, pair_kv[:, :, 0], preferred_element_type=jnp.float32
    ) / math.sqrt(head_size)
    exponents = jnp.exp(scores) * my_live.astype(jnp.float32)[:, None, :]
    weights = (exponents / jnp.sum(exponents, axis=-1, keepdims=True)).astype(jnp.bfloat16)
    combined = jnp.einsum(
        "nhl,nlhd->nhd", weights, pair_kv[:, :, 1], preferred_element_type=jnp.float32
    )
    combined = combined.reshape(sites_here, -1).astype(jnp.bfloat16)
    column_blocks = jnp.moveaxis(combined.reshape(sites_here, group_size, -1), 1, 0)
    columns = halving_exchange(column_blocks, group_size, my_index).reshape(
        group_size * sites_here, -1
    )
    attn_part = jnp.dot(columns, out_weight[0], preferred_element_type=jnp.float32)
    attn_part = attn_part.reshape(group_size, sites_here, -1)
    if direct_ok(group_size):
        attn_all = doubling_sum(attn_part, group_size)
        residual_all = everyone.reshape(group_size, sites_here, -1).astype(jnp.float32) + attn_all
        residual = lax.dynamic_index_in_dim(residual_all, my_index, 0, keepdims=False)
        normed_rows = rms_norm(residual_all, ffn_gain[0]).astype(jnp.bfloat16)
        normed_rows = normed_rows.reshape(-1, model_width)
    else:
        attn_sum = halving_sum(attn_part, group_size, my_index)
        residual = current.astype(jnp.float32) + attn_sum
        normed = rms_norm(residual, ffn_gain[0]).astype(jnp.bfloat16)
        normed_rows = doubling_gather(normed, group_size, my_index).reshape(-1, model_width)
    gate_sum = by_rows(normed_rows, gate_weight[0])
    up_sum = by_rows(normed_rows, up_weight[0])
    hidden_ffn = (jax.nn.silu(gate_sum) * up_sum).astype(jnp.bfloat16)
    down_part = jnp.dot(hidden_ffn, down_weight[0], preferred_element_type=jnp.float32)
    down_part = down_part.reshape(group_size, sites_here, -1)
    if not direct_ok(group_size) or group_size == 1:
        down_sum = halving_sum(down_part, group_size, my_index)
        output_rows = (residual + down_sum).astype(jnp.bfloat16)
        return lax.ppermute(output_rows[None], "section", shift_pairs(section_count, 1))
    bits = group_size.bit_length() - 1
    rest = down_part.shape[1:]
    state = down_part.reshape((2,) * bits + rest)
    for bit in range(bits):
        axis = bits - 1 - bit
        mine = (my_index >> bit) & 1
        keep = lax.dynamic_index_in_dim(state, mine, axis, keepdims=True)
        send = lax.dynamic_index_in_dim(state, 1 - mine, axis, keepdims=True)
        if bit < bits - 1:
            state = keep + lax.ppermute(send, "site", xor_pairs(group_size, bit))
            continue
        own = keep.reshape(rest) + residual
        forward = [
            (section * group_size + site, ((section + 1) % section_count) * group_size + site)
            for section in range(section_count)
            for site in range(group_size)
        ]
        across = [
            (
                section * group_size + site,
                ((section + 1) % section_count) * group_size + (site ^ (1 << bit)),
            )
            for section in range(section_count)
            for site in range(group_size)
        ]
        mine_part = lax.ppermute(own, ("section", "site"), forward)
        other_part = lax.ppermute(send.reshape(rest), ("section", "site"), across)
        output_rows = (mine_part + other_part).astype(jnp.bfloat16)
    return output_rows[None]


def ffn_block(rows_ref, gate_ref, up_ref, down_ref, out_ref):
    step = pl.program_id(0)

    @pl.when(step == 0)
    def _():
        out_ref[...] = jnp.zeros_like(out_ref)

    rows = rows_ref[...]
    dims = (((1,), (1,)), ((), ()))
    gate_sum = lax.dot_general(rows, gate_ref[...], dims, preferred_element_type=jnp.float32)
    up_sum = lax.dot_general(rows, up_ref[...], dims, preferred_element_type=jnp.float32)
    hidden = (gate_sum * jax.nn.sigmoid(gate_sum) * up_sum).astype(jnp.bfloat16)
    out_ref[...] += jnp.dot(hidden, down_ref[...], preferred_element_type=jnp.float32)


def gated_ffn(rows, gate, up, down):
    units, width = gate.shape
    block = 128 if units % 128 == 0 else units
    count = rows.shape[0]
    return pl.pallas_call(
        ffn_block,
        grid=(units // block,),
        in_specs=[
            pl.BlockSpec((count, width), lambda i: (0, 0)),
            pl.BlockSpec((block, width), lambda i: (i, 0)),
            pl.BlockSpec((block, width), lambda i: (i, 0)),
            pl.BlockSpec((block, width), lambda i: (i, 0)),
        ],
        out_specs=pl.BlockSpec((count, width), lambda i: (0, 0)),
        out_shape=jax.ShapeDtypeStruct((count, width), jnp.float32),
        compiler_params=pltpu.CompilerParams(dimension_semantics=("arbitrary",)),
    )(rows, gate, up, down)


def heads_split(
    acts,
    patches,
    site_tiles,
    site_count,
    q_weight,
    q_gain,
    k_gain,
    tile_in,
    tile_out,
    out_weight,
    ffn_gain,
    gate_weight,
    up_weight,
    down_weight,
):
    group_size = lax.axis_size("site")
    section_count = lax.axis_size("section")
    my_index = lax.axis_index("site")
    sites_here = acts.shape[1]
    list_width = site_tiles.shape[1]
    tiles_here = patches.shape[1]
    head_size = q_gain.shape[1]
    heads_here = HEADS // group_size
    current = acts[0]
    model_width = current.shape[-1]
    hidden_width = tile_in.shape[-1]
    all_sites = group_size * sites_here

    act_rows = sites_here * model_width // hidden_width
    ring_in = RingGather(
        jnp.concatenate([tile_in[0], current.reshape(act_rows, hidden_width)], axis=0),
        group_size,
        my_index,
    )
    in_slots, in_sources = ring_in.finish()
    in_rows = tile_in.shape[1]
    kv_width = tile_out.shape[-1]
    my_cols = heads_here * head_size
    col_blocks = tile_out[0].reshape(tile_out.shape[1], 2, group_size, my_cols)
    col_blocks = jnp.transpose(col_blocks, (2, 0, 1, 3)).reshape(group_size, tile_out.shape[1], 2 * my_cols)
    in_slots, col_blocks, site_tiles, site_count = lax.optimization_barrier(
        (in_slots, col_blocks, site_tiles, site_count)
    )
    weight_out = lax.all_to_all(col_blocks, "site", split_axis=0, concat_axis=0, tiled=True)
    weight_out = weight_out.reshape(-1, 2 * my_cols)
    del kv_width

    slot_of_source = jnp.argmax(
        in_sources[None, :] == jnp.arange(group_size, dtype=jnp.int32)[:, None], axis=1
    ).astype(jnp.int32)
    everyone = jnp.take(in_slots[:, in_rows:], slot_of_source, axis=0).reshape(all_sites, model_width)
    weight_in = in_slots[:, :in_rows].reshape(-1, hidden_width)
    own_rows = jnp.take(patches[0].reshape(tiles_here, group_size, -1), in_sources, axis=1)
    tile_hidden = jax.nn.gelu(
        jnp.dot(own_rows.reshape(tiles_here, -1), weight_in, preferred_element_type=jnp.float32),
        approximate=True,
    ).astype(jnp.bfloat16)

    q_part = by_rows(everyone, q_weight[0]).astype(jnp.bfloat16)
    queries = head_norm(q_part, q_gain[0]).astype(jnp.bfloat16)
    query_heads = queries.reshape(all_sites, heads_here, head_size)

    ring_hidden = RingGather(tile_hidden, group_size, my_index)
    hidden_slots, hidden_sources = ring_hidden.finish()
    table_hidden = hidden_slots.reshape(group_size * tiles_here, hidden_width)
    keyval = jnp.dot(table_hidden, weight_out, preferred_element_type=jnp.float32)
    normed_keys = head_norm(keyval[:, :my_cols], k_gain[0])
    table = jnp.concatenate([normed_keys, keyval[:, my_cols:]], axis=1).astype(jnp.bfloat16)
    table = table.reshape(group_size * tiles_here, 2, heads_here, head_size)

    tile_of_row = (
        hidden_sources[:, None] * tiles_here + jnp.arange(tiles_here, dtype=jnp.int32)[None, :]
    ).reshape(-1)
    slot_index = jnp.arange(list_width, dtype=jnp.int32)
    live = slot_index[None, :] < site_count[:, None]
    named = jnp.logical_and(
        site_tiles[:, :, None] == tile_of_row[None, None, :], live[:, :, None]
    )
    uses = jnp.sum(named.astype(jnp.float32), axis=1)
    scores = jnp.einsum(
        "nhd,rhd->nhr", query_heads, table[:, 0], preferred_element_type=jnp.float32
    ) / math.sqrt(head_size)
    exponents = jnp.exp(scores) * uses[:, None, :]
    weights = (exponents / jnp.sum(exponents, axis=-1, keepdims=True)).astype(jnp.bfloat16)
    combined = jnp.einsum(
        "nhr,rhd->nhd", weights, table[:, 1], preferred_element_type=jnp.float32
    )
    combined = combined.reshape(all_sites, my_cols).astype(jnp.bfloat16)
    attn_part = jnp.dot(combined, out_weight[0], preferred_element_type=jnp.float32)
    attn_all = doubling_sum(attn_part.reshape(group_size, sites_here, -1), group_size)
    residual_all = everyone.reshape(group_size, sites_here, -1).astype(jnp.float32) + attn_all
    residual = lax.dynamic_index_in_dim(residual_all, my_index, 0, keepdims=False)
    normed_rows = rms_norm(residual_all, ffn_gain[0]).astype(jnp.bfloat16).reshape(-1, model_width)
    down_part = gated_ffn(normed_rows, gate_weight[0], up_weight[0], down_weight[0])
    down_part = down_part.reshape(group_size, sites_here, -1)
    return last_round(down_part, residual, group_size, section_count, my_index)


def last_round(down_part, residual, group_size, section_count, my_index):
    bits = group_size.bit_length() - 1
    rest = down_part.shape[1:]
    state = down_part.reshape((2,) * bits + rest)
    for bit in range(bits):
        axis = bits - 1 - bit
        mine = (my_index >> bit) & 1
        keep = lax.dynamic_index_in_dim(state, mine, axis, keepdims=True)
        send = lax.dynamic_index_in_dim(state, 1 - mine, axis, keepdims=True)
        if bit < bits - 1:
            state = keep + lax.ppermute(send, "site", xor_pairs(group_size, bit))
            continue
        own = keep.reshape(rest) + residual
        forward = [
            (section * group_size + site, ((section + 1) % section_count) * group_size + site)
            for section in range(section_count)
            for site in range(group_size)
        ]
        across = [
            (
                section * group_size + site,
                ((section + 1) % section_count) * group_size + (site ^ (1 << bit)),
            )
            for section in range(section_count)
            for site in range(group_size)
        ]
        mine_part = lax.ppermute(own, ("section", "site"), forward)
        other_part = lax.ppermute(send.reshape(rest), ("section", "site"), across)
        return (mine_part + other_part).astype(jnp.bfloat16)[None]


def solution(mesh):
    group_size = mesh.shape["site"]
    split_heads = (
        direct_ok(group_size)
        and group_size > 1
        and HEADS % group_size == 0
        and mesh.shape["section"] > 0
    )
    return jax.shard_map(
        heads_split if split_heads else shards,
        mesh=mesh,
        in_specs=(
            P("section", "site", None),
            P("section", "site", None),
            P(),
            P(),
            P("section", "site", None),
            P("section", None),
            P("section", None),
            P("section", "site", None),
            P("section", "site", None),
            P("section", "site", None),
            P("section", None),
            P("section", "site", None),
            P("section", "site", None),
            P("section", "site", None),
        ),
        out_specs=P("section", "site", None),
        check_vma=False,
    )
```

```python
import math

import jax
import jax.numpy as jnp
from jax import lax
from jax.experimental import pallas as pl
from jax.experimental.pallas import tpu as pltpu
from jax.sharding import PartitionSpec as P

HEADS = 16


epsilon = 1e-05

DIRECT_LIMIT = 8


def shift_pairs(count, steps):
    return [(source, (source + steps) % count) for source in range(count)]


def by_rows(left, weight_rows):
    return lax.dot_general(
        left, weight_rows, (((1,), (1,)), ((), ())), preferred_element_type=jnp.float32
    )


def head_norm(values, gain_row):
    shaped = values.astype(jnp.float32).reshape(values.shape[0], -1, gain_row.shape[0])
    scaled = (
        shaped * lax.rsqrt(jnp.mean(shaped * shaped, axis=-1, keepdims=True) + epsilon) * gain_row
    )
    return scaled.reshape(values.shape[0], -1)


def rms_norm(values, gain_row):
    return (
        values * lax.rsqrt(jnp.mean(values * values, axis=-1, keepdims=True) + epsilon) * gain_row
    )


def to_source_order(slots, count, me):
    return jnp.take(slots, (me - jnp.arange(count, dtype=jnp.int32)) % count, axis=0)


def xor_pairs(count, bit):
    return [(source, source ^ (1 << bit)) for source in range(count)]


def direct_ok(count):
    return count <= DIRECT_LIMIT and count & (count - 1) == 0


def site_exchange(by_target, count, me):
    if not direct_ok(count):
        return lax.all_to_all(by_target, "site", split_axis=0, concat_axis=0, tiled=True)
    slots = [lax.dynamic_index_in_dim(by_target, me, 0, keepdims=False)]
    for steps in range(1, count):
        piece = lax.dynamic_index_in_dim(by_target, (me + steps) % count, 0, keepdims=False)
        slots.append(lax.ppermute(piece, "site", shift_pairs(count, steps)))
    return to_source_order(jnp.stack(slots), count, me)


def halving_exchange(by_target, count, me):
    if not direct_ok(count):
        return lax.all_to_all(by_target, "site", split_axis=0, concat_axis=0, tiled=True)
    bits = count.bit_length() - 1
    rest = by_target.shape[1:]
    state = by_target.reshape((2,) * bits + rest)
    for bit in range(bits):
        axis = bits - 1 - bit
        mine = (me >> bit) & 1
        keep = lax.dynamic_index_in_dim(state, mine, axis, keepdims=True)
        send = lax.dynamic_index_in_dim(state, 1 - mine, axis, keepdims=True)
        recv = lax.ppermute(send, "site", xor_pairs(count, bit))
        state = jnp.where(
            mine == 0,
            jnp.concatenate([keep, recv], axis),
            jnp.concatenate([recv, keep], axis),
        )
    return state.reshape((count,) + rest)


def doubling_gather(value, count, me):
    if not direct_ok(count):
        return lax.all_gather(value, "site", axis=0, tiled=False)
    bits = count.bit_length() - 1
    state = value[None]
    for bit in range(bits):
        recv = lax.ppermute(state, "site", xor_pairs(count, bit))
        mine = (me >> bit) & 1
        state = jnp.where(
            mine == 0, jnp.concatenate([state, recv], 0), jnp.concatenate([recv, state], 0)
        )
    return state


def halving_sum(parts, count, me):
    if not direct_ok(count):
        return lax.psum_scatter(parts, "site", scatter_dimension=0, tiled=True)[0]
    bits = count.bit_length() - 1
    rest = parts.shape[1:]
    state = parts.reshape((2,) * bits + rest)
    for bit in range(bits):
        axis = bits - 1 - bit
        mine = (me >> bit) & 1
        keep = lax.dynamic_index_in_dim(state, mine, axis, keepdims=True)
        send = lax.dynamic_index_in_dim(state, 1 - mine, axis, keepdims=True)
        state = keep + lax.ppermute(send, "site", xor_pairs(count, bit))
    return state.reshape(rest)


def doubling_sum(parts, count):
    state = parts
    for bit in range(count.bit_length() - 1):
        state = state + lax.ppermute(state, "site", xor_pairs(count, bit))
    return state


class RingGather:
    def __init__(self, value, count, me):
        self.count = count
        self.direct = direct_ok(count)
        if not self.direct:
            self.slots = lax.all_gather(value, "site", axis=0, tiled=False)
            self.sources = jnp.arange(count, dtype=jnp.int32)
            self.slot_of_source = self.sources
            return
        order = list(range(0, count, 2)) + [i for i in range(count - 1, -1, -1) if i % 2 == 1]
        place = [0] * count
        for position, device in enumerate(order):
            place[device] = position
        self.forward = [(order[p], order[(p + 1) % count]) for p in range(count)]
        self.backward = [(order[p], order[(p - 1) % count]) for p in range(count)]
        self.forward_left = count // 2
        self.backward_left = count - 1 - self.forward_left
        offsets = [0] + [count - s for s in range(1, self.forward_left + 1)]
        offsets += list(range(1, self.backward_left + 1))
        half = count // 2
        my_place = jnp.where(me % 2 == 0, me // 2, count - 1 - me // 2)
        place_of_slot = (my_place + jnp.array(offsets, dtype=jnp.int32)) % count
        self.sources = jnp.where(
            place_of_slot < half, 2 * place_of_slot, 2 * (count - 1 - place_of_slot) + 1
        )
        devices = jnp.arange(count, dtype=jnp.int32)
        their_place = jnp.where(devices % 2 == 0, devices // 2, count - 1 - devices // 2)
        delta = (their_place - my_place) % count
        forward_count = self.forward_left
        self.slot_of_source = jnp.where(
            delta == 0,
            0,
            jnp.where(delta >= count - forward_count, count - delta, forward_count + delta),
        )
        self.forward_slots = []
        self.backward_slots = []
        self.ahead = value
        self.behind = value
        self.value = value
        self._issue()

    def _issue(self):
        if self.forward_left > 0:
            self.ahead = lax.ppermute(self.ahead, "site", self.forward)
            self.forward_slots.append(self.ahead)
            self.forward_left -= 1
        if self.backward_left > 0:
            self.behind = lax.ppermute(self.behind, "site", self.backward)
            self.backward_slots.append(self.behind)
            self.backward_left -= 1

    def step(self, tied):
        if not self.direct or (self.forward_left == 0 and self.backward_left == 0):
            return tied
        self.ahead, self.behind, tied = lax.optimization_barrier((self.ahead, self.behind, tied))
        self.forward_slots[-1] = self.ahead
        if self.backward_slots:
            self.backward_slots[-1] = self.behind
        self._issue()
        return tied

    def slots_in_arrival(self):
        if not self.direct:
            return [self.slots[i] for i in range(self.count)], [self.sources[i] for i in range(self.count)]
        while self.forward_left > 0 or self.backward_left > 0:
            self._issue()
        slots = [self.value]
        positions = [0]
        forward_count = len(self.forward_slots)
        for step in range(max(forward_count, len(self.backward_slots))):
            if step < forward_count:
                slots.append(self.forward_slots[step])
                positions.append(1 + step)
            if step < len(self.backward_slots):
                slots.append(self.backward_slots[step])
                positions.append(1 + forward_count + step)
        return slots, [self.sources[p] for p in positions]

    def finish(self):
        if not self.direct:
            return self.slots, self.sources
        while self.forward_left > 0 or self.backward_left > 0:
            self._issue()
        slots = [self.value] + self.forward_slots + self.backward_slots
        return jnp.stack(slots), self.sources


def shards(
    acts,
    patches,
    site_tiles,
    site_count,
    q_weight,
    q_gain,
    k_gain,
    tile_in,
    tile_out,
    out_weight,
    ffn_gain,
    gate_weight,
    up_weight,
    down_weight,
):
    group_size = lax.axis_size("site")
    section_count = lax.axis_size("section")
    my_index = lax.axis_index("site")
    sites_here = acts.shape[1]
    list_width = site_tiles.shape[1]
    tiles_here = patches.shape[1]
    head_size = q_gain.shape[1]
    capacity = max(2, 5 * sites_here * list_width // (4 * group_size))
    entries = sites_here * list_width
    current = acts[0]
    model_width = current.shape[-1]
    row_width = patches.shape[-1]

    ring_in = RingGather(tile_in[0], group_size, my_index)
    in_slots, in_sources = ring_in.finish()
    ring_out = RingGather(tile_out[0], group_size, my_index)
    weight_in = in_slots.reshape(-1, in_slots.shape[-1])
    own_rows = jnp.take(patches[0].reshape(tiles_here, group_size, -1), in_sources, axis=1)
    tile_hidden = jax.nn.gelu(
        jnp.dot(own_rows.reshape(tiles_here, -1), weight_in, preferred_element_type=jnp.float32),
        approximate=True,
    ).astype(jnp.bfloat16)
    hidden_width = tile_hidden.shape[-1]

    slot_index = jnp.arange(list_width, dtype=jnp.int32)
    live_all = (slot_index[None, :] < site_count[:, None]).reshape(group_size, entries)
    owner_all = (site_tiles // tiles_here).reshape(group_size, entries)
    local_all = (site_tiles % tiles_here).reshape(group_size, entries)
    mine_mask = jnp.logical_and(live_all, owner_all == my_index)
    slot_rank = jnp.cumsum(mine_mask.astype(jnp.int32), axis=1) - 1
    picks = jnp.logical_and(
        mine_mask[:, :, None],
        slot_rank[:, :, None] == jnp.arange(capacity, dtype=jnp.int32)[None, None, :],
    )
    send_index = jnp.sum(jnp.where(picks, local_all[:, :, None], 0), axis=1)
    send_rows = tile_hidden[send_index.reshape(-1)].reshape(group_size, capacity, hidden_width)
    act_rows = sites_here * model_width // hidden_width
    packed = model_width % hidden_width == 0
    if packed:
        act_block = jnp.broadcast_to(
            current.reshape(1, act_rows, hidden_width), (group_size, act_rows, hidden_width)
        )
        send_rows = jnp.concatenate([send_rows, act_block], axis=1)
    send_rows = ring_out.step(send_rows)
    arrived = lax.all_to_all(send_rows, "site", split_axis=0, concat_axis=0, tiled=True)
    if packed:
        everyone = arrived[:, capacity:].reshape(-1, model_width)
        arrived = arrived[:, :capacity]
    else:
        everyone = doubling_gather(current, group_size, my_index).reshape(-1, model_width)
    q_part = by_rows(everyone, q_weight[0]).astype(jnp.bfloat16)
    q_part = ring_out.step(q_part)
    q_blocks = halving_exchange(
        q_part.reshape(group_size, sites_here, -1), group_size, my_index
    )
    q_blocks = ring_out.step(q_blocks)

    my_tiles = lax.dynamic_slice_in_dim(site_tiles, my_index * sites_here, sites_here, 0)
    my_count = lax.dynamic_slice_in_dim(site_count, my_index * sites_here, sites_here, 0)
    my_live = slot_index[None, :] < my_count[:, None]
    my_owner = (my_tiles // tiles_here).reshape(-1)
    one_hot = jnp.logical_and(
        my_owner[:, None] == jnp.arange(group_size, dtype=jnp.int32)[None, :],
        my_live.reshape(-1)[:, None],
    ).astype(jnp.int32)
    my_rank = jnp.sum(jnp.cumsum(one_hot, axis=0) * one_hot, axis=1) - 1
    fetch_index = jnp.where(my_live.reshape(-1), my_owner * capacity + my_rank, 0)
    pair_hidden = arrived.reshape(group_size * capacity, hidden_width)[fetch_index]

    shard_rows = tile_out.shape[1]
    keyval = None
    if not ring_out.direct:
        out_slots, out_sources = [ring_out.slots.reshape(-1, ring_out.slots.shape[-1])], [0]
        shard_rows = hidden_width
    else:
        out_slots, out_sources = ring_out.slots_in_arrival()
    for slot, source in zip(out_slots, out_sources):
        columns_here = lax.dynamic_slice_in_dim(pair_hidden, source * shard_rows, shard_rows, 1)
        term = jnp.dot(columns_here, slot, preferred_element_type=jnp.float32)
        keyval = term if keyval is None else keyval + term
    half_width = keyval.shape[1] // 2
    normed_keys = head_norm(keyval[:, :half_width], k_gain[0])
    pair_kv = jnp.concatenate([normed_keys, keyval[:, half_width:]], axis=1).astype(jnp.bfloat16)
    pair_kv = pair_kv.reshape(sites_here, list_width, 2, HEADS, head_size)

    my_queries = jnp.moveaxis(q_blocks, 0, 1).reshape(sites_here, -1)
    queries = head_norm(my_queries, q_gain[0]).astype(jnp.bfloat16)
    query_heads = queries.reshape(sites_here, HEADS, head_size)
    scores = jnp.einsum(
        "nhd,nlhd->nhl", query_heads, pair_kv[:, :, 0], preferred_element_type=jnp.float32
    ) / math.sqrt(head_size)
    exponents = jnp.exp(scores) * my_live.astype(jnp.float32)[:, None, :]
    weights = (exponents / jnp.sum(exponents, axis=-1, keepdims=True)).astype(jnp.bfloat16)
    combined = jnp.einsum(
        "nhl,nlhd->nhd", weights, pair_kv[:, :, 1], preferred_element_type=jnp.float32
    )
    combined = combined.reshape(sites_here, -1).astype(jnp.bfloat16)
    column_blocks = jnp.moveaxis(combined.reshape(sites_here, group_size, -1), 1, 0)
    columns = halving_exchange(column_blocks, group_size, my_index).reshape(
        group_size * sites_here, -1
    )
    attn_part = jnp.dot(columns, out_weight[0], preferred_element_type=jnp.float32)
    attn_part = attn_part.reshape(group_size, sites_here, -1)
    if direct_ok(group_size):
        attn_all = doubling_sum(attn_part, group_size)
        residual_all = everyone.reshape(group_size, sites_here, -1).astype(jnp.float32) + attn_all
        residual = lax.dynamic_index_in_dim(residual_all, my_index, 0, keepdims=False)
        normed_rows = rms_norm(residual_all, ffn_gain[0]).astype(jnp.bfloat16)
        normed_rows = normed_rows.reshape(-1, model_width)
    else:
        attn_sum = halving_sum(attn_part, group_size, my_index)
        residual = current.astype(jnp.float32) + attn_sum
        normed = rms_norm(residual, ffn_gain[0]).astype(jnp.bfloat16)
        normed_rows = doubling_gather(normed, group_size, my_index).reshape(-1, model_width)
    gate_sum = by_rows(normed_rows, gate_weight[0])
    up_sum = by_rows(normed_rows, up_weight[0])
    hidden_ffn = (jax.nn.silu(gate_sum) * up_sum).astype(jnp.bfloat16)
    down_part = jnp.dot(hidden_ffn, down_weight[0], preferred_element_type=jnp.float32)
    down_part = down_part.reshape(group_size, sites_here, -1)
    if not direct_ok(group_size) or group_size == 1:
        down_sum = halving_sum(down_part, group_size, my_index)
        output_rows = (residual + down_sum).astype(jnp.bfloat16)
        return lax.ppermute(output_rows[None], "section", shift_pairs(section_count, 1))
    bits = group_size.bit_length() - 1
    rest = down_part.shape[1:]
    state = down_part.reshape((2,) * bits + rest)
    for bit in range(bits):
        axis = bits - 1 - bit
        mine = (my_index >> bit) & 1
        keep = lax.dynamic_index_in_dim(state, mine, axis, keepdims=True)
        send = lax.dynamic_index_in_dim(state, 1 - mine, axis, keepdims=True)
        if bit < bits - 1:
            state = keep + lax.ppermute(send, "site", xor_pairs(group_size, bit))
            continue
        own = keep.reshape(rest) + residual
        forward = [
            (section * group_size + site, ((section + 1) % section_count) * group_size + site)
            for section in range(section_count)
            for site in range(group_size)
        ]
        across = [
            (
                section * group_size + site,
                ((section + 1) % section_count) * group_size + (site ^ (1 << bit)),
            )
            for section in range(section_count)
            for site in range(group_size)
        ]
        mine_part = lax.ppermute(own, ("section", "site"), forward)
        other_part = lax.ppermute(send.reshape(rest), ("section", "site"), across)
        output_rows = (mine_part + other_part).astype(jnp.bfloat16)
    return output_rows[None]


def ffn_block(rows_ref, gate_ref, up_ref, down_ref, out_ref):
    step = pl.program_id(0)

    @pl.when(step == 0)
    def _():
        out_ref[...] = jnp.zeros_like(out_ref)

    rows = rows_ref[...]
    dims = (((1,), (1,)), ((), ()))
    gate_sum = lax.dot_general(rows, gate_ref[...], dims, preferred_element_type=jnp.float32)
    up_sum = lax.dot_general(rows, up_ref[...], dims, preferred_element_type=jnp.float32)
    hidden = (gate_sum * jax.nn.sigmoid(gate_sum) * up_sum).astype(jnp.bfloat16)
    out_ref[...] += jnp.dot(hidden, down_ref[...], preferred_element_type=jnp.float32)


def gated_ffn(rows, gate, up, down):
    units, width = gate.shape
    block = 128 if units % 128 == 0 else units
    count = rows.shape[0]
    return pl.pallas_call(
        ffn_block,
        grid=(units // block,),
        in_specs=[
            pl.BlockSpec((count, width), lambda i: (0, 0)),
            pl.BlockSpec((block, width), lambda i: (i, 0)),
            pl.BlockSpec((block, width), lambda i: (i, 0)),
            pl.BlockSpec((block, width), lambda i: (i, 0)),
        ],
        out_specs=pl.BlockSpec((count, width), lambda i: (0, 0)),
        out_shape=jax.ShapeDtypeStruct((count, width), jnp.float32),
        compiler_params=pltpu.CompilerParams(dimension_semantics=("arbitrary",)),
    )(rows, gate, up, down)


def heads_split(
    acts,
    patches,
    site_tiles,
    site_count,
    q_weight,
    q_gain,
    k_gain,
    tile_in,
    tile_out,
    out_weight,
    ffn_gain,
    gate_weight,
    up_weight,
    down_weight,
):
    group_size = lax.axis_size("site")
    section_count = lax.axis_size("section")
    my_index = lax.axis_index("site")
    sites_here = acts.shape[1]
    list_width = site_tiles.shape[1]
    tiles_here = patches.shape[1]
    head_size = q_gain.shape[1]
    heads_here = HEADS // group_size
    current = acts[0]
    model_width = current.shape[-1]
    hidden_width = tile_in.shape[-1]
    all_sites = group_size * sites_here

    act_rows = sites_here * model_width // hidden_width
    ring_in = RingGather(
        jnp.concatenate([tile_in[0], current.reshape(act_rows, hidden_width)], axis=0),
        group_size,
        my_index,
    )
    in_slots, in_sources = ring_in.finish()
    in_rows = tile_in.shape[1]
    everyone = (
        in_slots[:, in_rows:]
        .at[ring_in.slot_of_source]
        .get(mode="promise_in_bounds")
        .reshape(all_sites, model_width)
    )
    weight_in = in_slots[:, :in_rows].reshape(-1, hidden_width)
    own_rows = (
        patches[0].reshape(tiles_here, group_size, -1).at[:, in_sources].get(mode="promise_in_bounds")
    )
    tile_hidden = jax.nn.gelu(
        jnp.dot(own_rows.reshape(tiles_here, -1), weight_in, preferred_element_type=jnp.float32),
        approximate=True,
    ).astype(jnp.bfloat16)

    kv_width = tile_out.shape[-1]
    my_cols = heads_here * head_size
    col_blocks = tile_out[0].reshape(tile_out.shape[1], 2, group_size, my_cols)
    col_blocks = jnp.transpose(col_blocks, (2, 0, 1, 3)).reshape(group_size, tile_out.shape[1], 2 * my_cols)
    weight_out = lax.all_to_all(col_blocks, "site", split_axis=0, concat_axis=0, tiled=True)
    weight_out = weight_out.reshape(-1, 2 * my_cols)
    del kv_width

    q_part = by_rows(everyone, q_weight[0]).astype(jnp.bfloat16)
    queries = head_norm(q_part, q_gain[0]).astype(jnp.bfloat16)
    query_heads = queries.reshape(all_sites, heads_here, head_size)

    ring_hidden = RingGather(tile_hidden, group_size, my_index)
    hidden_slots, hidden_sources = ring_hidden.finish()
    table_hidden = hidden_slots.reshape(group_size * tiles_here, hidden_width)
    keyval = jnp.dot(table_hidden, weight_out, preferred_element_type=jnp.float32)
    normed_keys = head_norm(keyval[:, :my_cols], k_gain[0])
    table = jnp.concatenate([normed_keys, keyval[:, my_cols:]], axis=1).astype(jnp.bfloat16)
    table = table.reshape(group_size * tiles_here, 2, heads_here, head_size)

    tile_of_row = (
        hidden_sources[:, None] * tiles_here + jnp.arange(tiles_here, dtype=jnp.int32)[None, :]
    ).reshape(-1)
    slot_index = jnp.arange(list_width, dtype=jnp.int32)
    live = slot_index[None, :] < site_count[:, None]
    named = jnp.logical_and(
        site_tiles[:, :, None] == tile_of_row[None, None, :], live[:, :, None]
    )
    uses = jnp.sum(named.astype(jnp.float32), axis=1)
    scores = jnp.einsum(
        "nhd,rhd->nhr", query_heads, table[:, 0], preferred_element_type=jnp.float32
    ) / math.sqrt(head_size)
    exponents = jnp.exp(scores) * uses[:, None, :]
    weights = (exponents / jnp.sum(exponents, axis=-1, keepdims=True)).astype(jnp.bfloat16)
    combined = jnp.einsum(
        "nhr,rhd->nhd", weights, table[:, 1], preferred_element_type=jnp.float32
    )
    combined = combined.reshape(all_sites, my_cols).astype(jnp.bfloat16)
    attn_part = jnp.dot(combined, out_weight[0], preferred_element_type=jnp.float32)
    attn_all = doubling_sum(attn_part.reshape(group_size, sites_here, -1), group_size)
    residual_all = everyone.reshape(group_size, sites_here, -1).astype(jnp.float32) + attn_all
    residual = lax.dynamic_index_in_dim(residual_all, my_index, 0, keepdims=False)
    normed_rows = rms_norm(residual_all, ffn_gain[0]).astype(jnp.bfloat16).reshape(-1, model_width)
    down_part = gated_ffn(normed_rows, gate_weight[0], up_weight[0], down_weight[0])
    down_part = down_part.reshape(group_size, sites_here, -1)
    return last_round(down_part, residual, group_size, section_count, my_index)


def last_round(down_part, residual, group_size, section_count, my_index):
    bits = group_size.bit_length() - 1
    rest = down_part.shape[1:]
    state = down_part.reshape((2,) * bits + rest)
    for bit in range(bits):
        axis = bits - 1 - bit
        mine = (my_index >> bit) & 1
        keep = lax.dynamic_index_in_dim(state, mine, axis, keepdims=True)
        send = lax.dynamic_index_in_dim(state, 1 - mine, axis, keepdims=True)
        if bit < bits - 1:
            state = keep + lax.ppermute(send, "site", xor_pairs(group_size, bit))
            continue
        own = keep.reshape(rest) + residual
        forward = [
            (section * group_size + site, ((section + 1) % section_count) * group_size + site)
            for section in range(section_count)
            for site in range(group_size)
        ]
        across = [
            (
                section * group_size + site,
                ((section + 1) % section_count) * group_size + (site ^ (1 << bit)),
            )
            for section in range(section_count)
            for site in range(group_size)
        ]
        mine_part = lax.ppermute(own, ("section", "site"), forward)
        other_part = lax.ppermute(send.reshape(rest), ("section", "site"), across)
        return (mine_part + other_part).astype(jnp.bfloat16)[None]


def solution(mesh):
    group_size = mesh.shape["site"]
    split_heads = (
        direct_ok(group_size)
        and group_size > 1
        and HEADS % group_size == 0
        and mesh.shape["section"] > 0
    )
    return jax.shard_map(
        heads_split if split_heads else shards,
        mesh=mesh,
        in_specs=(
            P("section", "site", None),
            P("section", "site", None),
            P(),
            P(),
            P("section", "site", None),
            P("section", None),
            P("section", None),
            P("section", "site", None),
            P("section", "site", None),
            P("section", "site", None),
            P("section", None),
            P("section", "site", None),
            P("section", "site", None),
            P("section", "site", None),
        ),
        out_specs=P("section", "site", None),
        check_vma=False,
    )
```

```python
import math

import jax
import jax.numpy as jnp
from jax import lax
from jax.experimental import pallas as pl
from jax.experimental.pallas import tpu as pltpu
from jax.sharding import PartitionSpec as P

HEADS = 16


epsilon = 1e-05

DIRECT_LIMIT = 8


def shift_pairs(count, steps):
    return [(source, (source + steps) % count) for source in range(count)]


def by_rows(left, weight_rows):
    return lax.dot_general(
        left, weight_rows, (((1,), (1,)), ((), ())), preferred_element_type=jnp.float32
    )


def head_norm(values, gain_row):
    shaped = values.astype(jnp.float32).reshape(values.shape[0], -1, gain_row.shape[0])
    scaled = (
        shaped * lax.rsqrt(jnp.mean(shaped * shaped, axis=-1, keepdims=True) + epsilon) * gain_row
    )
    return scaled.reshape(values.shape[0], -1)


def rms_norm(values, gain_row):
    return (
        values * lax.rsqrt(jnp.mean(values * values, axis=-1, keepdims=True) + epsilon) * gain_row
    )


def to_source_order(slots, count, me):
    return jnp.take(slots, (me - jnp.arange(count, dtype=jnp.int32)) % count, axis=0)


def xor_pairs(count, bit):
    return [(source, source ^ (1 << bit)) for source in range(count)]


def direct_ok(count):
    return count <= DIRECT_LIMIT and count & (count - 1) == 0


def site_exchange(by_target, count, me):
    if not direct_ok(count):
        return lax.all_to_all(by_target, "site", split_axis=0, concat_axis=0, tiled=True)
    slots = [lax.dynamic_index_in_dim(by_target, me, 0, keepdims=False)]
    for steps in range(1, count):
        piece = lax.dynamic_index_in_dim(by_target, (me + steps) % count, 0, keepdims=False)
        slots.append(lax.ppermute(piece, "site", shift_pairs(count, steps)))
    return to_source_order(jnp.stack(slots), count, me)


def halving_exchange(by_target, count, me):
    if not direct_ok(count):
        return lax.all_to_all(by_target, "site", split_axis=0, concat_axis=0, tiled=True)
    bits = count.bit_length() - 1
    rest = by_target.shape[1:]
    state = by_target.reshape((2,) * bits + rest)
    for bit in range(bits):
        axis = bits - 1 - bit
        mine = (me >> bit) & 1
        keep = lax.dynamic_index_in_dim(state, mine, axis, keepdims=True)
        send = lax.dynamic_index_in_dim(state, 1 - mine, axis, keepdims=True)
        recv = lax.ppermute(send, "site", xor_pairs(count, bit))
        state = jnp.where(
            mine == 0,
            jnp.concatenate([keep, recv], axis),
            jnp.concatenate([recv, keep], axis),
        )
    return state.reshape((count,) + rest)


def doubling_gather(value, count, me):
    if not direct_ok(count):
        return lax.all_gather(value, "site", axis=0, tiled=False)
    bits = count.bit_length() - 1
    state = value[None]
    for bit in range(bits):
        recv = lax.ppermute(state, "site", xor_pairs(count, bit))
        mine = (me >> bit) & 1
        state = jnp.where(
            mine == 0, jnp.concatenate([state, recv], 0), jnp.concatenate([recv, state], 0)
        )
    return state


def halving_sum(parts, count, me):
    if not direct_ok(count):
        return lax.psum_scatter(parts, "site", scatter_dimension=0, tiled=True)[0]
    bits = count.bit_length() - 1
    rest = parts.shape[1:]
    state = parts.reshape((2,) * bits + rest)
    for bit in range(bits):
        axis = bits - 1 - bit
        mine = (me >> bit) & 1
        keep = lax.dynamic_index_in_dim(state, mine, axis, keepdims=True)
        send = lax.dynamic_index_in_dim(state, 1 - mine, axis, keepdims=True)
        state = keep + lax.ppermute(send, "site", xor_pairs(count, bit))
    return state.reshape(rest)


def doubling_sum(parts, count):
    state = parts
    for bit in range(count.bit_length() - 1):
        state = state + lax.ppermute(state, "site", xor_pairs(count, bit))
    return state


class RingGather:
    def __init__(self, value, count, me):
        self.count = count
        self.direct = direct_ok(count)
        if not self.direct:
            self.slots = lax.all_gather(value, "site", axis=0, tiled=False)
            self.sources = jnp.arange(count, dtype=jnp.int32)
            self.slot_of_source = self.sources
            return
        order = list(range(0, count, 2)) + [i for i in range(count - 1, -1, -1) if i % 2 == 1]
        place = [0] * count
        for position, device in enumerate(order):
            place[device] = position
        self.forward = [(order[p], order[(p + 1) % count]) for p in range(count)]
        self.backward = [(order[p], order[(p - 1) % count]) for p in range(count)]
        self.forward_left = count // 2
        self.backward_left = count - 1 - self.forward_left
        offsets = [0] + [count - s for s in range(1, self.forward_left + 1)]
        offsets += list(range(1, self.backward_left + 1))
        half = count // 2
        my_place = jnp.where(me % 2 == 0, me // 2, count - 1 - me // 2)
        place_of_slot = (my_place + jnp.array(offsets, dtype=jnp.int32)) % count
        self.sources = jnp.where(
            place_of_slot < half, 2 * place_of_slot, 2 * (count - 1 - place_of_slot) + 1
        )
        devices = jnp.arange(count, dtype=jnp.int32)
        their_place = jnp.where(devices % 2 == 0, devices // 2, count - 1 - devices // 2)
        delta = (their_place - my_place) % count
        forward_count = self.forward_left
        self.slot_of_source = jnp.where(
            delta == 0,
            0,
            jnp.where(delta >= count - forward_count, count - delta, forward_count + delta),
        )
        self.forward_slots = []
        self.backward_slots = []
        self.ahead = value
        self.behind = value
        self.value = value
        self._issue()

    def _issue(self):
        if self.forward_left > 0:
            self.ahead = lax.ppermute(self.ahead, "site", self.forward)
            self.forward_slots.append(self.ahead)
            self.forward_left -= 1
        if self.backward_left > 0:
            self.behind = lax.ppermute(self.behind, "site", self.backward)
            self.backward_slots.append(self.behind)
            self.backward_left -= 1

    def step(self, tied):
        if not self.direct or (self.forward_left == 0 and self.backward_left == 0):
            return tied
        self.ahead, self.behind, tied = lax.optimization_barrier((self.ahead, self.behind, tied))
        self.forward_slots[-1] = self.ahead
        if self.backward_slots:
            self.backward_slots[-1] = self.behind
        self._issue()
        return tied

    def slots_in_arrival(self):
        if not self.direct:
            return [self.slots[i] for i in range(self.count)], [self.sources[i] for i in range(self.count)]
        while self.forward_left > 0 or self.backward_left > 0:
            self._issue()
        slots = [self.value]
        positions = [0]
        forward_count = len(self.forward_slots)
        for step in range(max(forward_count, len(self.backward_slots))):
            if step < forward_count:
                slots.append(self.forward_slots[step])
                positions.append(1 + step)
            if step < len(self.backward_slots):
                slots.append(self.backward_slots[step])
                positions.append(1 + forward_count + step)
        return slots, [self.sources[p] for p in positions]

    def finish(self):
        if not self.direct:
            return self.slots, self.sources
        while self.forward_left > 0 or self.backward_left > 0:
            self._issue()
        slots = [self.value] + self.forward_slots + self.backward_slots
        return jnp.stack(slots), self.sources


def shards(
    acts,
    patches,
    site_tiles,
    site_count,
    q_weight,
    q_gain,
    k_gain,
    tile_in,
    tile_out,
    out_weight,
    ffn_gain,
    gate_weight,
    up_weight,
    down_weight,
):
    group_size = lax.axis_size("site")
    section_count = lax.axis_size("section")
    my_index = lax.axis_index("site")
    sites_here = acts.shape[1]
    list_width = site_tiles.shape[1]
    tiles_here = patches.shape[1]
    head_size = q_gain.shape[1]
    capacity = max(2, 5 * sites_here * list_width // (4 * group_size))
    entries = sites_here * list_width
    current = acts[0]
    model_width = current.shape[-1]
    row_width = patches.shape[-1]

    ring_in = RingGather(tile_in[0], group_size, my_index)
    in_slots, in_sources = ring_in.finish()
    ring_out = RingGather(tile_out[0], group_size, my_index)
    weight_in = in_slots.reshape(-1, in_slots.shape[-1])
    own_rows = jnp.take(patches[0].reshape(tiles_here, group_size, -1), in_sources, axis=1)
    tile_hidden = jax.nn.gelu(
        jnp.dot(own_rows.reshape(tiles_here, -1), weight_in, preferred_element_type=jnp.float32),
        approximate=True,
    ).astype(jnp.bfloat16)
    hidden_width = tile_hidden.shape[-1]

    slot_index = jnp.arange(list_width, dtype=jnp.int32)
    live_all = (slot_index[None, :] < site_count[:, None]).reshape(group_size, entries)
    owner_all = (site_tiles // tiles_here).reshape(group_size, entries)
    local_all = (site_tiles % tiles_here).reshape(group_size, entries)
    mine_mask = jnp.logical_and(live_all, owner_all == my_index)
    slot_rank = jnp.cumsum(mine_mask.astype(jnp.int32), axis=1) - 1
    picks = jnp.logical_and(
        mine_mask[:, :, None],
        slot_rank[:, :, None] == jnp.arange(capacity, dtype=jnp.int32)[None, None, :],
    )
    send_index = jnp.sum(jnp.where(picks, local_all[:, :, None], 0), axis=1)
    send_rows = tile_hidden[send_index.reshape(-1)].reshape(group_size, capacity, hidden_width)
    act_rows = sites_here * model_width // hidden_width
    packed = model_width % hidden_width == 0
    if packed:
        act_block = jnp.broadcast_to(
            current.reshape(1, act_rows, hidden_width), (group_size, act_rows, hidden_width)
        )
        send_rows = jnp.concatenate([send_rows, act_block], axis=1)
    send_rows = ring_out.step(send_rows)
    arrived = lax.all_to_all(send_rows, "site", split_axis=0, concat_axis=0, tiled=True)
    if packed:
        everyone = arrived[:, capacity:].reshape(-1, model_width)
        arrived = arrived[:, :capacity]
    else:
        everyone = doubling_gather(current, group_size, my_index).reshape(-1, model_width)
    q_part = by_rows(everyone, q_weight[0]).astype(jnp.bfloat16)
    q_part = ring_out.step(q_part)
    q_blocks = halving_exchange(
        q_part.reshape(group_size, sites_here, -1), group_size, my_index
    )
    q_blocks = ring_out.step(q_blocks)

    my_tiles = lax.dynamic_slice_in_dim(site_tiles, my_index * sites_here, sites_here, 0)
    my_count = lax.dynamic_slice_in_dim(site_count, my_index * sites_here, sites_here, 0)
    my_live = slot_index[None, :] < my_count[:, None]
    my_owner = (my_tiles // tiles_here).reshape(-1)
    one_hot = jnp.logical_and(
        my_owner[:, None] == jnp.arange(group_size, dtype=jnp.int32)[None, :],
        my_live.reshape(-1)[:, None],
    ).astype(jnp.int32)
    my_rank = jnp.sum(jnp.cumsum(one_hot, axis=0) * one_hot, axis=1) - 1
    fetch_index = jnp.where(my_live.reshape(-1), my_owner * capacity + my_rank, 0)
    pair_hidden = arrived.reshape(group_size * capacity, hidden_width)[fetch_index]

    shard_rows = tile_out.shape[1]
    keyval = None
    if not ring_out.direct:
        out_slots, out_sources = [ring_out.slots.reshape(-1, ring_out.slots.shape[-1])], [0]
        shard_rows = hidden_width
    else:
        out_slots, out_sources = ring_out.slots_in_arrival()
    for slot, source in zip(out_slots, out_sources):
        columns_here = lax.dynamic_slice_in_dim(pair_hidden, source * shard_rows, shard_rows, 1)
        term = jnp.dot(columns_here, slot, preferred_element_type=jnp.float32)
        keyval = term if keyval is None else keyval + term
    half_width = keyval.shape[1] // 2
    normed_keys = head_norm(keyval[:, :half_width], k_gain[0])
    pair_kv = jnp.concatenate([normed_keys, keyval[:, half_width:]], axis=1).astype(jnp.bfloat16)
    pair_kv = pair_kv.reshape(sites_here, list_width, 2, HEADS, head_size)

    my_queries = jnp.moveaxis(q_blocks, 0, 1).reshape(sites_here, -1)
    queries = head_norm(my_queries, q_gain[0]).astype(jnp.bfloat16)
    query_heads = queries.reshape(sites_here, HEADS, head_size)
    scores = jnp.einsum(
        "nhd,nlhd->nhl", query_heads, pair_kv[:, :, 0], preferred_element_type=jnp.float32
    ) / math.sqrt(head_size)
    exponents = jnp.exp(scores) * my_live.astype(jnp.float32)[:, None, :]
    weights = (exponents / jnp.sum(exponents, axis=-1, keepdims=True)).astype(jnp.bfloat16)
    combined = jnp.einsum(
        "nhl,nlhd->nhd", weights, pair_kv[:, :, 1], preferred_element_type=jnp.float32
    )
    combined = combined.reshape(sites_here, -1).astype(jnp.bfloat16)
    column_blocks = jnp.moveaxis(combined.reshape(sites_here, group_size, -1), 1, 0)
    columns = halving_exchange(column_blocks, group_size, my_index).reshape(
        group_size * sites_here, -1
    )
    attn_part = jnp.dot(columns, out_weight[0], preferred_element_type=jnp.float32)
    attn_part = attn_part.reshape(group_size, sites_here, -1)
    if direct_ok(group_size):
        attn_all = doubling_sum(attn_part, group_size)
        residual_all = everyone.reshape(group_size, sites_here, -1).astype(jnp.float32) + attn_all
        residual = lax.dynamic_index_in_dim(residual_all, my_index, 0, keepdims=False)
        normed_rows = rms_norm(residual_all, ffn_gain[0]).astype(jnp.bfloat16)
        normed_rows = normed_rows.reshape(-1, model_width)
    else:
        attn_sum = halving_sum(attn_part, group_size, my_index)
        residual = current.astype(jnp.float32) + attn_sum
        normed = rms_norm(residual, ffn_gain[0]).astype(jnp.bfloat16)
        normed_rows = doubling_gather(normed, group_size, my_index).reshape(-1, model_width)
    gate_sum = by_rows(normed_rows, gate_weight[0])
    up_sum = by_rows(normed_rows, up_weight[0])
    hidden_ffn = (jax.nn.silu(gate_sum) * up_sum).astype(jnp.bfloat16)
    down_part = jnp.dot(hidden_ffn, down_weight[0], preferred_element_type=jnp.float32)
    down_part = down_part.reshape(group_size, sites_here, -1)
    if not direct_ok(group_size) or group_size == 1:
        down_sum = halving_sum(down_part, group_size, my_index)
        output_rows = (residual + down_sum).astype(jnp.bfloat16)
        return lax.ppermute(output_rows[None], "section", shift_pairs(section_count, 1))
    bits = group_size.bit_length() - 1
    rest = down_part.shape[1:]
    state = down_part.reshape((2,) * bits + rest)
    for bit in reversed(range(bits)):
        axis = bits - 1 - bit
        mine = (my_index >> bit) & 1
        keep = lax.dynamic_index_in_dim(state, mine, axis, keepdims=True)
        send = lax.dynamic_index_in_dim(state, 1 - mine, axis, keepdims=True)
        if bit > 0:
            state = keep + lax.ppermute(send, "site", xor_pairs(group_size, bit))
            continue
        own = keep.reshape(rest) + residual
        forward = [
            (section * group_size + site, ((section + 1) % section_count) * group_size + site)
            for section in range(section_count)
            for site in range(group_size)
        ]
        across = [
            (
                section * group_size + site,
                ((section + 1) % section_count) * group_size + (site ^ (1 << bit)),
            )
            for section in range(section_count)
            for site in range(group_size)
        ]
        mine_part = lax.ppermute(own, ("section", "site"), forward)
        other_part = lax.ppermute(send.reshape(rest), ("section", "site"), across)
        output_rows = (mine_part + other_part).astype(jnp.bfloat16)
    return output_rows[None]


def ffn_block(rows_ref, gate_ref, up_ref, down_ref, out_ref):
    step = pl.program_id(0)

    @pl.when(step == 0)
    def _():
        out_ref[...] = jnp.zeros_like(out_ref)

    rows = rows_ref[...]
    dims = (((1,), (1,)), ((), ()))
    gate_sum = lax.dot_general(rows, gate_ref[...], dims, preferred_element_type=jnp.float32)
    up_sum = lax.dot_general(rows, up_ref[...], dims, preferred_element_type=jnp.float32)
    hidden = (gate_sum * jax.nn.sigmoid(gate_sum) * up_sum).astype(jnp.bfloat16)
    out_ref[...] += jnp.dot(hidden, down_ref[...], preferred_element_type=jnp.float32)


def gated_ffn(rows, gate, up, down):
    units, width = gate.shape
    block = 128 if units % 128 == 0 else units
    count = rows.shape[0]
    return pl.pallas_call(
        ffn_block,
        grid=(units // block,),
        in_specs=[
            pl.BlockSpec((count, width), lambda i: (0, 0)),
            pl.BlockSpec((block, width), lambda i: (i, 0)),
            pl.BlockSpec((block, width), lambda i: (i, 0)),
            pl.BlockSpec((block, width), lambda i: (i, 0)),
        ],
        out_specs=pl.BlockSpec((count, width), lambda i: (0, 0)),
        out_shape=jax.ShapeDtypeStruct((count, width), jnp.float32),
        compiler_params=pltpu.CompilerParams(dimension_semantics=("arbitrary",)),
    )(rows, gate, up, down)


def heads_split(
    acts,
    patches,
    site_tiles,
    site_count,
    q_weight,
    q_gain,
    k_gain,
    tile_in,
    tile_out,
    out_weight,
    ffn_gain,
    gate_weight,
    up_weight,
    down_weight,
):
    group_size = lax.axis_size("site")
    section_count = lax.axis_size("section")
    my_index = lax.axis_index("site")
    sites_here = acts.shape[1]
    list_width = site_tiles.shape[1]
    tiles_here = patches.shape[1]
    head_size = q_gain.shape[1]
    heads_here = HEADS // group_size
    current = acts[0]
    model_width = current.shape[-1]
    hidden_width = tile_in.shape[-1]
    all_sites = group_size * sites_here

    act_rows = sites_here * model_width // hidden_width
    ring_in = RingGather(
        jnp.concatenate([tile_in[0], current.reshape(act_rows, hidden_width)], axis=0),
        group_size,
        my_index,
    )
    in_slots, in_sources = ring_in.finish()
    in_rows = tile_in.shape[1]
    everyone = (
        in_slots[:, in_rows:]
        .at[ring_in.slot_of_source]
        .get(mode="promise_in_bounds")
        .reshape(all_sites, model_width)
    )
    weight_in = (
        in_slots[:, :in_rows]
        .at[ring_in.slot_of_source]
        .get(mode="promise_in_bounds")
        .reshape(-1, hidden_width)
    )
    tile_hidden = jax.nn.gelu(
        jnp.dot(patches[0], weight_in, preferred_element_type=jnp.float32),
        approximate=True,
    ).astype(jnp.bfloat16)

    kv_width = tile_out.shape[-1]
    my_cols = heads_here * head_size
    col_blocks = tile_out[0].reshape(tile_out.shape[1], 2, group_size, my_cols)
    col_blocks = jnp.transpose(col_blocks, (2, 0, 1, 3)).reshape(group_size, tile_out.shape[1], 2 * my_cols)
    weight_out = lax.all_to_all(col_blocks, "site", split_axis=0, concat_axis=0, tiled=True)
    weight_out = weight_out.reshape(-1, 2 * my_cols)
    del kv_width

    q_part = by_rows(everyone, q_weight[0]).astype(jnp.bfloat16)
    queries = head_norm(q_part, q_gain[0]).astype(jnp.bfloat16)
    query_heads = queries.reshape(all_sites, heads_here, head_size)

    ring_hidden = RingGather(tile_hidden, group_size, my_index)
    hidden_slots, hidden_sources = ring_hidden.finish()
    table_hidden = hidden_slots.reshape(group_size * tiles_here, hidden_width)
    keyval = jnp.dot(table_hidden, weight_out, preferred_element_type=jnp.float32)
    normed_keys = head_norm(keyval[:, :my_cols], k_gain[0])
    table = jnp.concatenate([normed_keys, keyval[:, my_cols:]], axis=1).astype(jnp.bfloat16)
    table = table.reshape(group_size * tiles_here, 2, heads_here, head_size)

    tile_of_row = (
        hidden_sources[:, None] * tiles_here + jnp.arange(tiles_here, dtype=jnp.int32)[None, :]
    ).reshape(-1)
    slot_index = jnp.arange(list_width, dtype=jnp.int32)
    live = slot_index[None, :] < site_count[:, None]
    named = jnp.logical_and(
        site_tiles[:, :, None] == tile_of_row[None, None, :], live[:, :, None]
    )
    uses = jnp.sum(named.astype(jnp.float32), axis=1)
    scores = jnp.einsum(
        "nhd,rhd->nhr", query_heads, table[:, 0], preferred_element_type=jnp.float32
    ) / math.sqrt(head_size)
    exponents = jnp.exp(scores) * uses[:, None, :]
    weights = (exponents / jnp.sum(exponents, axis=-1, keepdims=True)).astype(jnp.bfloat16)
    combined = jnp.einsum(
        "nhr,rhd->nhd", weights, table[:, 1], preferred_element_type=jnp.float32
    )
    combined = combined.reshape(all_sites, my_cols).astype(jnp.bfloat16)
    attn_part = jnp.dot(combined, out_weight[0], preferred_element_type=jnp.float32)
    attn_all = doubling_sum(attn_part.reshape(group_size, sites_here, -1), group_size)
    residual_all = everyone.reshape(group_size, sites_here, -1).astype(jnp.float32) + attn_all
    residual = lax.dynamic_index_in_dim(residual_all, my_index, 0, keepdims=False)
    normed_rows = rms_norm(residual_all, ffn_gain[0]).astype(jnp.bfloat16).reshape(-1, model_width)
    down_part = gated_ffn(normed_rows, gate_weight[0], up_weight[0], down_weight[0])
    down_part = down_part.reshape(group_size, sites_here, -1)
    return last_round(down_part, residual, group_size, section_count, my_index)


def last_round(down_part, residual, group_size, section_count, my_index):
    bits = group_size.bit_length() - 1
    rest = down_part.shape[1:]
    state = down_part.reshape((2,) * bits + rest)
    for bit in reversed(range(bits)):
        axis = bits - 1 - bit
        mine = (my_index >> bit) & 1
        keep = lax.dynamic_index_in_dim(state, mine, axis, keepdims=True)
        send = lax.dynamic_index_in_dim(state, 1 - mine, axis, keepdims=True)
        if bit > 0:
            state = keep + lax.ppermute(send, "site", xor_pairs(group_size, bit))
            continue
        own = keep.reshape(rest) + residual
        forward = [
            (section * group_size + site, ((section + 1) % section_count) * group_size + site)
            for section in range(section_count)
            for site in range(group_size)
        ]
        across = [
            (
                section * group_size + site,
                ((section + 1) % section_count) * group_size + (site ^ (1 << bit)),
            )
            for section in range(section_count)
            for site in range(group_size)
        ]
        mine_part = lax.ppermute(own, ("section", "site"), forward)
        other_part = lax.ppermute(send.reshape(rest), ("section", "site"), across)
        return (mine_part + other_part).astype(jnp.bfloat16)[None]


def solution(mesh):
    group_size = mesh.shape["site"]
    split_heads = (
        direct_ok(group_size)
        and group_size > 1
        and HEADS % group_size == 0
        and mesh.shape["section"] > 0
    )
    return jax.shard_map(
        heads_split if split_heads else shards,
        mesh=mesh,
        in_specs=(
            P("section", "site", None),
            P("section", "site", None),
            P(),
            P(),
            P("section", "site", None),
            P("section", None),
            P("section", None),
            P("section", "site", None),
            P("section", "site", None),
            P("section", "site", None),
            P("section", None),
            P("section", "site", None),
            P("section", "site", None),
            P("section", "site", None),
        ),
        out_specs=P("section", "site", None),
        check_vma=False,
    )
```

```python
import math

import jax
import jax.numpy as jnp
from jax import lax
from jax.experimental import pallas as pl
from jax.experimental.pallas import tpu as pltpu
from jax.sharding import PartitionSpec as P

HEADS = 16


epsilon = 1e-05

DIRECT_LIMIT = 8


def shift_pairs(count, steps):
    return [(source, (source + steps) % count) for source in range(count)]


def by_rows(left, weight_rows):
    return lax.dot_general(
        left, weight_rows, (((1,), (1,)), ((), ())), preferred_element_type=jnp.float32
    )


def head_norm(values, gain_row):
    shaped = values.astype(jnp.float32).reshape(values.shape[0], -1, gain_row.shape[0])
    scaled = (
        shaped * lax.rsqrt(jnp.mean(shaped * shaped, axis=-1, keepdims=True) + epsilon) * gain_row
    )
    return scaled.reshape(values.shape[0], -1)


def rms_norm(values, gain_row):
    return (
        values * lax.rsqrt(jnp.mean(values * values, axis=-1, keepdims=True) + epsilon) * gain_row
    )


def to_source_order(slots, count, me):
    return jnp.take(slots, (me - jnp.arange(count, dtype=jnp.int32)) % count, axis=0)


def xor_pairs(count, bit):
    return [(source, source ^ (1 << bit)) for source in range(count)]


def direct_ok(count):
    return count <= DIRECT_LIMIT and count & (count - 1) == 0


def site_exchange(by_target, count, me):
    if not direct_ok(count):
        return lax.all_to_all(by_target, "site", split_axis=0, concat_axis=0, tiled=True)
    slots = [lax.dynamic_index_in_dim(by_target, me, 0, keepdims=False)]
    for steps in range(1, count):
        piece = lax.dynamic_index_in_dim(by_target, (me + steps) % count, 0, keepdims=False)
        slots.append(lax.ppermute(piece, "site", shift_pairs(count, steps)))
    return to_source_order(jnp.stack(slots), count, me)


def halving_exchange(by_target, count, me):
    if not direct_ok(count):
        return lax.all_to_all(by_target, "site", split_axis=0, concat_axis=0, tiled=True)
    bits = count.bit_length() - 1
    rest = by_target.shape[1:]
    state = by_target.reshape((2,) * bits + rest)
    for bit in range(bits):
        axis = bits - 1 - bit
        mine = (me >> bit) & 1
        keep = lax.dynamic_index_in_dim(state, mine, axis, keepdims=True)
        send = lax.dynamic_index_in_dim(state, 1 - mine, axis, keepdims=True)
        recv = lax.ppermute(send, "site", xor_pairs(count, bit))
        state = jnp.where(
            mine == 0,
            jnp.concatenate([keep, recv], axis),
            jnp.concatenate([recv, keep], axis),
        )
    return state.reshape((count,) + rest)


def doubling_gather(value, count, me):
    if not direct_ok(count):
        return lax.all_gather(value, "site", axis=0, tiled=False)
    bits = count.bit_length() - 1
    state = value[None]
    for bit in range(bits):
        recv = lax.ppermute(state, "site", xor_pairs(count, bit))
        mine = (me >> bit) & 1
        state = jnp.where(
            mine == 0, jnp.concatenate([state, recv], 0), jnp.concatenate([recv, state], 0)
        )
    return state


def halving_sum(parts, count, me):
    if not direct_ok(count):
        return lax.psum_scatter(parts, "site", scatter_dimension=0, tiled=True)[0]
    bits = count.bit_length() - 1
    rest = parts.shape[1:]
    state = parts.reshape((2,) * bits + rest)
    for bit in range(bits):
        axis = bits - 1 - bit
        mine = (me >> bit) & 1
        keep = lax.dynamic_index_in_dim(state, mine, axis, keepdims=True)
        send = lax.dynamic_index_in_dim(state, 1 - mine, axis, keepdims=True)
        state = keep + lax.ppermute(send, "site", xor_pairs(count, bit))
    return state.reshape(rest)


def doubling_sum(parts, count):
    state = parts
    for bit in range(count.bit_length() - 1):
        state = state + lax.ppermute(state, "site", xor_pairs(count, bit))
    return state


class RingGather:
    def __init__(self, value, count, me):
        self.count = count
        self.direct = direct_ok(count)
        if not self.direct:
            self.slots = lax.all_gather(value, "site", axis=0, tiled=False)
            self.sources = jnp.arange(count, dtype=jnp.int32)
            self.slot_of_source = self.sources
            return
        order = list(range(0, count, 2)) + [i for i in range(count - 1, -1, -1) if i % 2 == 1]
        place = [0] * count
        for position, device in enumerate(order):
            place[device] = position
        self.forward = [(order[p], order[(p + 1) % count]) for p in range(count)]
        self.backward = [(order[p], order[(p - 1) % count]) for p in range(count)]
        self.forward_left = count // 2
        self.backward_left = count - 1 - self.forward_left
        offsets = [0] + [count - s for s in range(1, self.forward_left + 1)]
        offsets += list(range(1, self.backward_left + 1))
        half = count // 2
        my_place = jnp.where(me % 2 == 0, me // 2, count - 1 - me // 2)
        place_of_slot = (my_place + jnp.array(offsets, dtype=jnp.int32)) % count
        self.sources = jnp.where(
            place_of_slot < half, 2 * place_of_slot, 2 * (count - 1 - place_of_slot) + 1
        )
        devices = jnp.arange(count, dtype=jnp.int32)
        their_place = jnp.where(devices % 2 == 0, devices // 2, count - 1 - devices // 2)
        delta = (their_place - my_place) % count
        forward_count = self.forward_left
        self.slot_of_source = jnp.where(
            delta == 0,
            0,
            jnp.where(delta >= count - forward_count, count - delta, forward_count + delta),
        )
        self.forward_slots = []
        self.backward_slots = []
        self.ahead = value
        self.behind = value
        self.value = value
        self._issue()

    def _issue(self):
        if self.forward_left > 0:
            self.ahead = lax.ppermute(self.ahead, "site", self.forward)
            self.forward_slots.append(self.ahead)
            self.forward_left -= 1
        if self.backward_left > 0:
            self.behind = lax.ppermute(self.behind, "site", self.backward)
            self.backward_slots.append(self.behind)
            self.backward_left -= 1

    def step(self, tied):
        if not self.direct or (self.forward_left == 0 and self.backward_left == 0):
            return tied
        self.ahead, self.behind, tied = lax.optimization_barrier((self.ahead, self.behind, tied))
        self.forward_slots[-1] = self.ahead
        if self.backward_slots:
            self.backward_slots[-1] = self.behind
        self._issue()
        return tied

    def slots_in_arrival(self):
        if not self.direct:
            return [self.slots[i] for i in range(self.count)], [self.sources[i] for i in range(self.count)]
        while self.forward_left > 0 or self.backward_left > 0:
            self._issue()
        slots = [self.value]
        positions = [0]
        forward_count = len(self.forward_slots)
        for step in range(max(forward_count, len(self.backward_slots))):
            if step < forward_count:
                slots.append(self.forward_slots[step])
                positions.append(1 + step)
            if step < len(self.backward_slots):
                slots.append(self.backward_slots[step])
                positions.append(1 + forward_count + step)
        return slots, [self.sources[p] for p in positions]

    def finish(self):
        if not self.direct:
            return self.slots, self.sources
        while self.forward_left > 0 or self.backward_left > 0:
            self._issue()
        slots = [self.value] + self.forward_slots + self.backward_slots
        return jnp.stack(slots), self.sources


def shards(
    acts,
    patches,
    site_tiles,
    site_count,
    q_weight,
    q_gain,
    k_gain,
    tile_in,
    tile_out,
    out_weight,
    ffn_gain,
    gate_weight,
    up_weight,
    down_weight,
):
    group_size = lax.axis_size("site")
    section_count = lax.axis_size("section")
    my_index = lax.axis_index("site")
    sites_here = acts.shape[1]
    list_width = site_tiles.shape[1]
    tiles_here = patches.shape[1]
    head_size = q_gain.shape[1]
    capacity = max(2, 5 * sites_here * list_width // (4 * group_size))
    entries = sites_here * list_width
    current = acts[0]
    model_width = current.shape[-1]
    row_width = patches.shape[-1]

    ring_in = RingGather(tile_in[0], group_size, my_index)
    in_slots, in_sources = ring_in.finish()
    ring_out = RingGather(tile_out[0], group_size, my_index)
    weight_in = in_slots.reshape(-1, in_slots.shape[-1])
    own_rows = jnp.take(patches[0].reshape(tiles_here, group_size, -1), in_sources, axis=1)
    tile_hidden = jax.nn.gelu(
        jnp.dot(own_rows.reshape(tiles_here, -1), weight_in, preferred_element_type=jnp.float32),
        approximate=True,
    ).astype(jnp.bfloat16)
    hidden_width = tile_hidden.shape[-1]

    slot_index = jnp.arange(list_width, dtype=jnp.int32)
    live_all = (slot_index[None, :] < site_count[:, None]).reshape(group_size, entries)
    owner_all = (site_tiles // tiles_here).reshape(group_size, entries)
    local_all = (site_tiles % tiles_here).reshape(group_size, entries)
    mine_mask = jnp.logical_and(live_all, owner_all == my_index)
    slot_rank = jnp.cumsum(mine_mask.astype(jnp.int32), axis=1) - 1
    picks = jnp.logical_and(
        mine_mask[:, :, None],
        slot_rank[:, :, None] == jnp.arange(capacity, dtype=jnp.int32)[None, None, :],
    )
    send_index = jnp.sum(jnp.where(picks, local_all[:, :, None], 0), axis=1)
    send_rows = tile_hidden[send_index.reshape(-1)].reshape(group_size, capacity, hidden_width)
    act_rows = sites_here * model_width // hidden_width
    packed = model_width % hidden_width == 0
    if packed:
        act_block = jnp.broadcast_to(
            current.reshape(1, act_rows, hidden_width), (group_size, act_rows, hidden_width)
        )
        send_rows = jnp.concatenate([send_rows, act_block], axis=1)
    send_rows = ring_out.step(send_rows)
    arrived = lax.all_to_all(send_rows, "site", split_axis=0, concat_axis=0, tiled=True)
    if packed:
        everyone = arrived[:, capacity:].reshape(-1, model_width)
        arrived = arrived[:, :capacity]
    else:
        everyone = doubling_gather(current, group_size, my_index).reshape(-1, model_width)
    q_part = by_rows(everyone, q_weight[0]).astype(jnp.bfloat16)
    q_part = ring_out.step(q_part)
    q_blocks = halving_exchange(
        q_part.reshape(group_size, sites_here, -1), group_size, my_index
    )
    q_blocks = ring_out.step(q_blocks)

    my_tiles = lax.dynamic_slice_in_dim(site_tiles, my_index * sites_here, sites_here, 0)
    my_count = lax.dynamic_slice_in_dim(site_count, my_index * sites_here, sites_here, 0)
    my_live = slot_index[None, :] < my_count[:, None]
    my_owner = (my_tiles // tiles_here).reshape(-1)
    one_hot = jnp.logical_and(
        my_owner[:, None] == jnp.arange(group_size, dtype=jnp.int32)[None, :],
        my_live.reshape(-1)[:, None],
    ).astype(jnp.int32)
    my_rank = jnp.sum(jnp.cumsum(one_hot, axis=0) * one_hot, axis=1) - 1
    fetch_index = jnp.where(my_live.reshape(-1), my_owner * capacity + my_rank, 0)
    pair_hidden = arrived.reshape(group_size * capacity, hidden_width)[fetch_index]

    shard_rows = tile_out.shape[1]
    keyval = None
    if not ring_out.direct:
        out_slots, out_sources = [ring_out.slots.reshape(-1, ring_out.slots.shape[-1])], [0]
        shard_rows = hidden_width
    else:
        out_slots, out_sources = ring_out.slots_in_arrival()
    for slot, source in zip(out_slots, out_sources):
        columns_here = lax.dynamic_slice_in_dim(pair_hidden, source * shard_rows, shard_rows, 1)
        term = jnp.dot(columns_here, slot, preferred_element_type=jnp.float32)
        keyval = term if keyval is None else keyval + term
    half_width = keyval.shape[1] // 2
    normed_keys = head_norm(keyval[:, :half_width], k_gain[0])
    pair_kv = jnp.concatenate([normed_keys, keyval[:, half_width:]], axis=1).astype(jnp.bfloat16)
    pair_kv = pair_kv.reshape(sites_here, list_width, 2, HEADS, head_size)

    my_queries = jnp.moveaxis(q_blocks, 0, 1).reshape(sites_here, -1)
    queries = head_norm(my_queries, q_gain[0]).astype(jnp.bfloat16)
    query_heads = queries.reshape(sites_here, HEADS, head_size)
    scores = jnp.einsum(
        "nhd,nlhd->nhl", query_heads, pair_kv[:, :, 0], preferred_element_type=jnp.float32
    ) / math.sqrt(head_size)
    exponents = jnp.exp(scores) * my_live.astype(jnp.float32)[:, None, :]
    weights = (exponents / jnp.sum(exponents, axis=-1, keepdims=True)).astype(jnp.bfloat16)
    combined = jnp.einsum(
        "nhl,nlhd->nhd", weights, pair_kv[:, :, 1], preferred_element_type=jnp.float32
    )
    combined = combined.reshape(sites_here, -1).astype(jnp.bfloat16)
    column_blocks = jnp.moveaxis(combined.reshape(sites_here, group_size, -1), 1, 0)
    columns = halving_exchange(column_blocks, group_size, my_index).reshape(
        group_size * sites_here, -1
    )
    attn_part = jnp.dot(columns, out_weight[0], preferred_element_type=jnp.float32)
    attn_part = attn_part.reshape(group_size, sites_here, -1)
    if direct_ok(group_size):
        attn_all = doubling_sum(attn_part, group_size)
        residual_all = everyone.reshape(group_size, sites_here, -1).astype(jnp.float32) + attn_all
        residual = lax.dynamic_index_in_dim(residual_all, my_index, 0, keepdims=False)
        normed_rows = rms_norm(residual_all, ffn_gain[0]).astype(jnp.bfloat16)
        normed_rows = normed_rows.reshape(-1, model_width)
    else:
        attn_sum = halving_sum(attn_part, group_size, my_index)
        residual = current.astype(jnp.float32) + attn_sum
        normed = rms_norm(residual, ffn_gain[0]).astype(jnp.bfloat16)
        normed_rows = doubling_gather(normed, group_size, my_index).reshape(-1, model_width)
    gate_sum = by_rows(normed_rows, gate_weight[0])
    up_sum = by_rows(normed_rows, up_weight[0])
    hidden_ffn = (jax.nn.silu(gate_sum) * up_sum).astype(jnp.bfloat16)
    down_part = jnp.dot(hidden_ffn, down_weight[0], preferred_element_type=jnp.float32)
    down_part = down_part.reshape(group_size, sites_here, -1)
    if not direct_ok(group_size) or group_size == 1:
        down_sum = halving_sum(down_part, group_size, my_index)
        output_rows = (residual + down_sum).astype(jnp.bfloat16)
        return lax.ppermute(output_rows[None], "section", shift_pairs(section_count, 1))
    bits = group_size.bit_length() - 1
    rest = down_part.shape[1:]
    state = down_part.reshape((2,) * bits + rest)
    for bit in range(bits):
        axis = bits - 1 - bit
        mine = (my_index >> bit) & 1
        keep = lax.dynamic_index_in_dim(state, mine, axis, keepdims=True)
        send = lax.dynamic_index_in_dim(state, 1 - mine, axis, keepdims=True)
        if bit < bits - 1:
            state = keep + lax.ppermute(send, "site", xor_pairs(group_size, bit))
            continue
        own = keep.reshape(rest) + residual
        forward = [
            (section * group_size + site, ((section + 1) % section_count) * group_size + site)
            for section in range(section_count)
            for site in range(group_size)
        ]
        across = [
            (
                section * group_size + site,
                ((section + 1) % section_count) * group_size + (site ^ (1 << bit)),
            )
            for section in range(section_count)
            for site in range(group_size)
        ]
        mine_part = lax.ppermute(own, ("section", "site"), forward)
        other_part = lax.ppermute(send.reshape(rest), ("section", "site"), across)
        output_rows = (mine_part + other_part).astype(jnp.bfloat16)
    return output_rows[None]


def ffn_block(rows_ref, gate_ref, up_ref, down_ref, out_ref):
    step = pl.program_id(0)

    @pl.when(step == 0)
    def _():
        out_ref[...] = jnp.zeros_like(out_ref)

    rows = rows_ref[...]
    dims = (((1,), (1,)), ((), ()))
    gate_sum = lax.dot_general(rows, gate_ref[...], dims, preferred_element_type=jnp.float32)
    up_sum = lax.dot_general(rows, up_ref[...], dims, preferred_element_type=jnp.float32)
    hidden = (gate_sum * jax.nn.sigmoid(gate_sum) * up_sum).astype(jnp.bfloat16)
    out_ref[...] += jnp.dot(hidden, down_ref[...], preferred_element_type=jnp.float32)


def gated_ffn(rows, gate, up, down):
    units, width = gate.shape
    block = 128 if units % 128 == 0 else units
    count = rows.shape[0]
    return pl.pallas_call(
        ffn_block,
        grid=(units // block,),
        in_specs=[
            pl.BlockSpec((count, width), lambda i: (0, 0)),
            pl.BlockSpec((block, width), lambda i: (i, 0)),
            pl.BlockSpec((block, width), lambda i: (i, 0)),
            pl.BlockSpec((block, width), lambda i: (i, 0)),
        ],
        out_specs=pl.BlockSpec((count, width), lambda i: (0, 0)),
        out_shape=jax.ShapeDtypeStruct((count, width), jnp.float32),
        compiler_params=pltpu.CompilerParams(dimension_semantics=("arbitrary",)),
    )(rows, gate, up, down)


def heads_split(
    acts,
    patches,
    site_tiles,
    site_count,
    q_weight,
    q_gain,
    k_gain,
    tile_in,
    tile_out,
    out_weight,
    ffn_gain,
    gate_weight,
    up_weight,
    down_weight,
):
    group_size = lax.axis_size("site")
    section_count = lax.axis_size("section")
    my_index = lax.axis_index("site")
    sites_here = acts.shape[1]
    list_width = site_tiles.shape[1]
    tiles_here = patches.shape[1]
    head_size = q_gain.shape[1]
    heads_here = HEADS // group_size
    current = acts[0]
    model_width = current.shape[-1]
    hidden_width = tile_in.shape[-1]
    all_sites = group_size * sites_here

    act_rows = sites_here * model_width // hidden_width
    ring_in = RingGather(
        jnp.concatenate([tile_in[0], current.reshape(act_rows, hidden_width)], axis=0),
        group_size,
        my_index,
    )
    in_slots, in_sources = ring_in.finish()
    in_rows = tile_in.shape[1]
    kv_width = tile_out.shape[-1]
    my_cols = heads_here * head_size
    col_blocks = tile_out[0].reshape(tile_out.shape[1], 2, group_size, my_cols)
    col_blocks = jnp.transpose(col_blocks, (2, 0, 1, 3)).reshape(group_size, tile_out.shape[1], 2 * my_cols)
    in_slots, col_blocks = lax.optimization_barrier((in_slots, col_blocks))
    weight_out = lax.all_to_all(col_blocks, "site", split_axis=0, concat_axis=0, tiled=True)
    weight_out = weight_out.reshape(-1, 2 * my_cols)
    del kv_width

    everyone = (
        in_slots[:, in_rows:]
        .at[ring_in.slot_of_source]
        .get(mode="promise_in_bounds")
        .reshape(all_sites, model_width)
    )
    weight_in = in_slots[:, :in_rows].reshape(-1, hidden_width)
    own_rows = (
        patches[0].reshape(tiles_here, group_size, -1).at[:, in_sources].get(mode="promise_in_bounds")
    )
    tile_hidden = jax.nn.gelu(
        jnp.dot(own_rows.reshape(tiles_here, -1), weight_in, preferred_element_type=jnp.float32),
        approximate=True,
    ).astype(jnp.bfloat16)

    q_part = by_rows(everyone, q_weight[0]).astype(jnp.bfloat16)
    queries = head_norm(q_part, q_gain[0]).astype(jnp.bfloat16)
    query_heads = queries.reshape(all_sites, heads_here, head_size)

    ring_hidden = RingGather(tile_hidden, group_size, my_index)
    site_tiles, site_count = ring_hidden.step((site_tiles, site_count))
    hidden_slots, hidden_sources = ring_hidden.finish()
    table_hidden = hidden_slots.reshape(group_size * tiles_here, hidden_width)
    keyval = jnp.dot(table_hidden, weight_out, preferred_element_type=jnp.float32)
    normed_keys = head_norm(keyval[:, :my_cols], k_gain[0])
    table = jnp.concatenate([normed_keys, keyval[:, my_cols:]], axis=1).astype(jnp.bfloat16)
    table = table.reshape(group_size * tiles_here, 2, heads_here, head_size)

    tile_of_row = (
        hidden_sources[:, None] * tiles_here + jnp.arange(tiles_here, dtype=jnp.int32)[None, :]
    ).reshape(-1)
    slot_index = jnp.arange(list_width, dtype=jnp.int32)
    live = slot_index[None, :] < site_count[:, None]
    named = jnp.logical_and(
        site_tiles[:, :, None] == tile_of_row[None, None, :], live[:, :, None]
    )
    uses = jnp.sum(named.astype(jnp.float32), axis=1)
    scores = jnp.einsum(
        "nhd,rhd->nhr", query_heads, table[:, 0], preferred_element_type=jnp.float32
    ) / math.sqrt(head_size)
    exponents = jnp.exp(scores) * uses[:, None, :]
    weights = (exponents / jnp.sum(exponents, axis=-1, keepdims=True)).astype(jnp.bfloat16)
    combined = jnp.einsum(
        "nhr,rhd->nhd", weights, table[:, 1], preferred_element_type=jnp.float32
    )
    combined = combined.reshape(all_sites, my_cols).astype(jnp.bfloat16)
    attn_part = jnp.dot(combined, out_weight[0], preferred_element_type=jnp.float32)
    attn_all = doubling_sum(attn_part.reshape(group_size, sites_here, -1), group_size)
    residual_all = everyone.reshape(group_size, sites_here, -1).astype(jnp.float32) + attn_all
    residual = lax.dynamic_index_in_dim(residual_all, my_index, 0, keepdims=False)
    normed_rows = rms_norm(residual_all, ffn_gain[0]).astype(jnp.bfloat16).reshape(-1, model_width)
    down_part = gated_ffn(normed_rows, gate_weight[0], up_weight[0], down_weight[0])
    down_part = down_part.reshape(group_size, sites_here, -1)
    return last_round(down_part, residual, group_size, section_count, my_index)


def last_round(down_part, residual, group_size, section_count, my_index):
    bits = group_size.bit_length() - 1
    rest = down_part.shape[1:]
    state = down_part.reshape((2,) * bits + rest)
    for bit in range(bits):
        axis = bits - 1 - bit
        mine = (my_index >> bit) & 1
        keep = lax.dynamic_index_in_dim(state, mine, axis, keepdims=True)
        send = lax.dynamic_index_in_dim(state, 1 - mine, axis, keepdims=True)
        if bit < bits - 1:
            state = keep + lax.ppermute(send, "site", xor_pairs(group_size, bit))
            continue
        own = keep.reshape(rest) + residual
        forward = [
            (section * group_size + site, ((section + 1) % section_count) * group_size + site)
            for section in range(section_count)
            for site in range(group_size)
        ]
        across = [
            (
                section * group_size + site,
                ((section + 1) % section_count) * group_size + (site ^ (1 << bit)),
            )
            for section in range(section_count)
            for site in range(group_size)
        ]
        mine_part = lax.ppermute(own, ("section", "site"), forward)
        other_part = lax.ppermute(send.reshape(rest), ("section", "site"), across)
        return (mine_part + other_part).astype(jnp.bfloat16)[None]


def solution(mesh):
    group_size = mesh.shape["site"]
    split_heads = (
        direct_ok(group_size)
        and group_size > 1
        and HEADS % group_size == 0
        and mesh.shape["section"] > 0
    )
    return jax.shard_map(
        heads_split if split_heads else shards,
        mesh=mesh,
        in_specs=(
            P("section", "site", None),
            P("section", "site", None),
            P(),
            P(),
            P("section", "site", None),
            P("section", None),
            P("section", None),
            P("section", "site", None),
            P("section", "site", None),
            P("section", "site", None),
            P("section", None),
            P("section", "site", None),
            P("section", "site", None),
            P("section", "site", None),
        ),
        out_specs=P("section", "site", None),
        check_vma=False,
    )
```

```python
import math

import jax
import jax.numpy as jnp
from jax import lax
from jax.experimental import pallas as pl
from jax.experimental.pallas import tpu as pltpu
from jax.sharding import PartitionSpec as P

HEADS = 16


epsilon = 1e-05

DIRECT_LIMIT = 8


def shift_pairs(count, steps):
    return [(source, (source + steps) % count) for source in range(count)]


def by_rows(left, weight_rows):
    return lax.dot_general(
        left, weight_rows, (((1,), (1,)), ((), ())), preferred_element_type=jnp.float32
    )


def head_norm(values, gain_row):
    shaped = values.astype(jnp.float32).reshape(values.shape[0], -1, gain_row.shape[0])
    scaled = (
        shaped * lax.rsqrt(jnp.mean(shaped * shaped, axis=-1, keepdims=True) + epsilon) * gain_row
    )
    return scaled.reshape(values.shape[0], -1)


def rms_norm(values, gain_row):
    return (
        values * lax.rsqrt(jnp.mean(values * values, axis=-1, keepdims=True) + epsilon) * gain_row
    )


def to_source_order(slots, count, me):
    return jnp.take(slots, (me - jnp.arange(count, dtype=jnp.int32)) % count, axis=0)


def xor_pairs(count, bit):
    return [(source, source ^ (1 << bit)) for source in range(count)]


def direct_ok(count):
    return count <= DIRECT_LIMIT and count & (count - 1) == 0


def site_exchange(by_target, count, me):
    if not direct_ok(count):
        return lax.all_to_all(by_target, "site", split_axis=0, concat_axis=0, tiled=True)
    slots = [lax.dynamic_index_in_dim(by_target, me, 0, keepdims=False)]
    for steps in range(1, count):
        piece = lax.dynamic_index_in_dim(by_target, (me + steps) % count, 0, keepdims=False)
        slots.append(lax.ppermute(piece, "site", shift_pairs(count, steps)))
    return to_source_order(jnp.stack(slots), count, me)


def halving_exchange(by_target, count, me):
    if not direct_ok(count):
        return lax.all_to_all(by_target, "site", split_axis=0, concat_axis=0, tiled=True)
    bits = count.bit_length() - 1
    rest = by_target.shape[1:]
    state = by_target.reshape((2,) * bits + rest)
    for bit in range(bits):
        axis = bits - 1 - bit
        mine = (me >> bit) & 1
        keep = lax.dynamic_index_in_dim(state, mine, axis, keepdims=True)
        send = lax.dynamic_index_in_dim(state, 1 - mine, axis, keepdims=True)
        recv = lax.ppermute(send, "site", xor_pairs(count, bit))
        state = jnp.where(
            mine == 0,
            jnp.concatenate([keep, recv], axis),
            jnp.concatenate([recv, keep], axis),
        )
    return state.reshape((count,) + rest)


def doubling_gather(value, count, me):
    if not direct_ok(count):
        return lax.all_gather(value, "site", axis=0, tiled=False)
    bits = count.bit_length() - 1
    state = value[None]
    for bit in range(bits):
        recv = lax.ppermute(state, "site", xor_pairs(count, bit))
        mine = (me >> bit) & 1
        state = jnp.where(
            mine == 0, jnp.concatenate([state, recv], 0), jnp.concatenate([recv, state], 0)
        )
    return state


def halving_sum(parts, count, me):
    if not direct_ok(count):
        return lax.psum_scatter(parts, "site", scatter_dimension=0, tiled=True)[0]
    bits = count.bit_length() - 1
    rest = parts.shape[1:]
    state = parts.reshape((2,) * bits + rest)
    for bit in range(bits):
        axis = bits - 1 - bit
        mine = (me >> bit) & 1
        keep = lax.dynamic_index_in_dim(state, mine, axis, keepdims=True)
        send = lax.dynamic_index_in_dim(state, 1 - mine, axis, keepdims=True)
        state = keep + lax.ppermute(send, "site", xor_pairs(count, bit))
    return state.reshape(rest)


def doubling_sum(parts, count):
    state = parts
    for bit in range(count.bit_length() - 1):
        state = state + lax.ppermute(state, "site", xor_pairs(count, bit))
    return state


class RingGather:
    def __init__(self, value, count, me):
        self.count = count
        self.direct = direct_ok(count)
        if not self.direct:
            self.slots = lax.all_gather(value, "site", axis=0, tiled=False)
            self.sources = jnp.arange(count, dtype=jnp.int32)
            self.slot_of_source = self.sources
            return
        order = list(range(0, count, 2)) + [i for i in range(count - 1, -1, -1) if i % 2 == 1]
        place = [0] * count
        for position, device in enumerate(order):
            place[device] = position
        self.forward = [(order[p], order[(p + 1) % count]) for p in range(count)]
        self.backward = [(order[p], order[(p - 1) % count]) for p in range(count)]
        self.forward_left = count // 2
        self.backward_left = count - 1 - self.forward_left
        offsets = [0] + [count - s for s in range(1, self.forward_left + 1)]
        offsets += list(range(1, self.backward_left + 1))
        half = count // 2
        my_place = jnp.where(me % 2 == 0, me // 2, count - 1 - me // 2)
        place_of_slot = (my_place + jnp.array(offsets, dtype=jnp.int32)) % count
        self.sources = jnp.where(
            place_of_slot < half, 2 * place_of_slot, 2 * (count - 1 - place_of_slot) + 1
        )
        devices = jnp.arange(count, dtype=jnp.int32)
        their_place = jnp.where(devices % 2 == 0, devices // 2, count - 1 - devices // 2)
        delta = (their_place - my_place) % count
        forward_count = self.forward_left
        self.slot_of_source = jnp.where(
            delta == 0,
            0,
            jnp.where(delta >= count - forward_count, count - delta, forward_count + delta),
        )
        self.forward_slots = []
        self.backward_slots = []
        self.ahead = value
        self.behind = value
        self.value = value
        self._issue()

    def _issue(self):
        if self.forward_left > 0:
            self.ahead = lax.ppermute(self.ahead, "site", self.forward)
            self.forward_slots.append(self.ahead)
            self.forward_left -= 1
        if self.backward_left > 0:
            self.behind = lax.ppermute(self.behind, "site", self.backward)
            self.backward_slots.append(self.behind)
            self.backward_left -= 1

    def step(self, tied):
        if not self.direct or (self.forward_left == 0 and self.backward_left == 0):
            return tied
        self.ahead, self.behind, tied = lax.optimization_barrier((self.ahead, self.behind, tied))
        self.forward_slots[-1] = self.ahead
        if self.backward_slots:
            self.backward_slots[-1] = self.behind
        self._issue()
        return tied

    def slots_in_arrival(self):
        if not self.direct:
            return [self.slots[i] for i in range(self.count)], [self.sources[i] for i in range(self.count)]
        while self.forward_left > 0 or self.backward_left > 0:
            self._issue()
        slots = [self.value]
        positions = [0]
        forward_count = len(self.forward_slots)
        for step in range(max(forward_count, len(self.backward_slots))):
            if step < forward_count:
                slots.append(self.forward_slots[step])
                positions.append(1 + step)
            if step < len(self.backward_slots):
                slots.append(self.backward_slots[step])
                positions.append(1 + forward_count + step)
        return slots, [self.sources[p] for p in positions]

    def finish(self):
        if not self.direct:
            return self.slots, self.sources
        while self.forward_left > 0 or self.backward_left > 0:
            self._issue()
        slots = [self.value] + self.forward_slots + self.backward_slots
        return jnp.stack(slots), self.sources


def shards(
    acts,
    patches,
    site_tiles,
    site_count,
    q_weight,
    q_gain,
    k_gain,
    tile_in,
    tile_out,
    out_weight,
    ffn_gain,
    gate_weight,
    up_weight,
    down_weight,
):
    group_size = lax.axis_size("site")
    section_count = lax.axis_size("section")
    my_index = lax.axis_index("site")
    sites_here = acts.shape[1]
    list_width = site_tiles.shape[1]
    tiles_here = patches.shape[1]
    head_size = q_gain.shape[1]
    capacity = max(2, 5 * sites_here * list_width // (4 * group_size))
    entries = sites_here * list_width
    current = acts[0]
    model_width = current.shape[-1]
    row_width = patches.shape[-1]

    ring_in = RingGather(tile_in[0], group_size, my_index)
    in_slots, in_sources = ring_in.finish()
    ring_out = RingGather(tile_out[0], group_size, my_index)
    weight_in = in_slots.reshape(-1, in_slots.shape[-1])
    own_rows = jnp.take(patches[0].reshape(tiles_here, group_size, -1), in_sources, axis=1)
    tile_hidden = jax.nn.gelu(
        jnp.dot(own_rows.reshape(tiles_here, -1), weight_in, preferred_element_type=jnp.float32),
        approximate=True,
    ).astype(jnp.bfloat16)
    hidden_width = tile_hidden.shape[-1]

    slot_index = jnp.arange(list_width, dtype=jnp.int32)
    live_all = (slot_index[None, :] < site_count[:, None]).reshape(group_size, entries)
    owner_all = (site_tiles // tiles_here).reshape(group_size, entries)
    local_all = (site_tiles % tiles_here).reshape(group_size, entries)
    mine_mask = jnp.logical_and(live_all, owner_all == my_index)
    slot_rank = jnp.cumsum(mine_mask.astype(jnp.int32), axis=1) - 1
    picks = jnp.logical_and(
        mine_mask[:, :, None],
        slot_rank[:, :, None] == jnp.arange(capacity, dtype=jnp.int32)[None, None, :],
    )
    send_index = jnp.sum(jnp.where(picks, local_all[:, :, None], 0), axis=1)
    send_rows = tile_hidden[send_index.reshape(-1)].reshape(group_size, capacity, hidden_width)
    act_rows = sites_here * model_width // hidden_width
    packed = model_width % hidden_width == 0
    if packed:
        act_block = jnp.broadcast_to(
            current.reshape(1, act_rows, hidden_width), (group_size, act_rows, hidden_width)
        )
        send_rows = jnp.concatenate([send_rows, act_block], axis=1)
    send_rows = ring_out.step(send_rows)
    arrived = lax.all_to_all(send_rows, "site", split_axis=0, concat_axis=0, tiled=True)
    if packed:
        everyone = arrived[:, capacity:].reshape(-1, model_width)
        arrived = arrived[:, :capacity]
    else:
        everyone = doubling_gather(current, group_size, my_index).reshape(-1, model_width)
    q_part = by_rows(everyone, q_weight[0]).astype(jnp.bfloat16)
    q_part = ring_out.step(q_part)
    q_blocks = halving_exchange(
        q_part.reshape(group_size, sites_here, -1), group_size, my_index
    )
    q_blocks = ring_out.step(q_blocks)

    my_tiles = lax.dynamic_slice_in_dim(site_tiles, my_index * sites_here, sites_here, 0)
    my_count = lax.dynamic_slice_in_dim(site_count, my_index * sites_here, sites_here, 0)
    my_live = slot_index[None, :] < my_count[:, None]
    my_owner = (my_tiles // tiles_here).reshape(-1)
    one_hot = jnp.logical_and(
        my_owner[:, None] == jnp.arange(group_size, dtype=jnp.int32)[None, :],
        my_live.reshape(-1)[:, None],
    ).astype(jnp.int32)
    my_rank = jnp.sum(jnp.cumsum(one_hot, axis=0) * one_hot, axis=1) - 1
    fetch_index = jnp.where(my_live.reshape(-1), my_owner * capacity + my_rank, 0)
    pair_hidden = arrived.reshape(group_size * capacity, hidden_width)[fetch_index]

    shard_rows = tile_out.shape[1]
    keyval = None
    if not ring_out.direct:
        out_slots, out_sources = [ring_out.slots.reshape(-1, ring_out.slots.shape[-1])], [0]
        shard_rows = hidden_width
    else:
        out_slots, out_sources = ring_out.slots_in_arrival()
    for slot, source in zip(out_slots, out_sources):
        columns_here = lax.dynamic_slice_in_dim(pair_hidden, source * shard_rows, shard_rows, 1)
        term = jnp.dot(columns_here, slot, preferred_element_type=jnp.float32)
        keyval = term if keyval is None else keyval + term
    half_width = keyval.shape[1] // 2
    normed_keys = head_norm(keyval[:, :half_width], k_gain[0])
    pair_kv = jnp.concatenate([normed_keys, keyval[:, half_width:]], axis=1).astype(jnp.bfloat16)
    pair_kv = pair_kv.reshape(sites_here, list_width, 2, HEADS, head_size)

    my_queries = jnp.moveaxis(q_blocks, 0, 1).reshape(sites_here, -1)
    queries = head_norm(my_queries, q_gain[0]).astype(jnp.bfloat16)
    query_heads = queries.reshape(sites_here, HEADS, head_size)
    scores = jnp.einsum(
        "nhd,nlhd->nhl", query_heads, pair_kv[:, :, 0], preferred_element_type=jnp.float32
    ) / math.sqrt(head_size)
    exponents = jnp.exp(scores) * my_live.astype(jnp.float32)[:, None, :]
    weights = (exponents / jnp.sum(exponents, axis=-1, keepdims=True)).astype(jnp.bfloat16)
    combined = jnp.einsum(
        "nhl,nlhd->nhd", weights, pair_kv[:, :, 1], preferred_element_type=jnp.float32
    )
    combined = combined.reshape(sites_here, -1).astype(jnp.bfloat16)
    column_blocks = jnp.moveaxis(combined.reshape(sites_here, group_size, -1), 1, 0)
    columns = halving_exchange(column_blocks, group_size, my_index).reshape(
        group_size * sites_here, -1
    )
    attn_part = jnp.dot(columns, out_weight[0], preferred_element_type=jnp.float32)
    attn_part = attn_part.reshape(group_size, sites_here, -1)
    if direct_ok(group_size):
        attn_all = doubling_sum(attn_part, group_size)
        residual_all = everyone.reshape(group_size, sites_here, -1).astype(jnp.float32) + attn_all
        residual = lax.dynamic_index_in_dim(residual_all, my_index, 0, keepdims=False)
        normed_rows = rms_norm(residual_all, ffn_gain[0]).astype(jnp.bfloat16)
        normed_rows = normed_rows.reshape(-1, model_width)
    else:
        attn_sum = halving_sum(attn_part, group_size, my_index)
        residual = current.astype(jnp.float32) + attn_sum
        normed = rms_norm(residual, ffn_gain[0]).astype(jnp.bfloat16)
        normed_rows = doubling_gather(normed, group_size, my_index).reshape(-1, model_width)
    gate_sum = by_rows(normed_rows, gate_weight[0])
    up_sum = by_rows(normed_rows, up_weight[0])
    hidden_ffn = (jax.nn.silu(gate_sum) * up_sum).astype(jnp.bfloat16)
    down_part = jnp.dot(hidden_ffn, down_weight[0], preferred_element_type=jnp.float32)
    down_part = down_part.reshape(group_size, sites_here, -1)
    if not direct_ok(group_size) or group_size == 1:
        down_sum = halving_sum(down_part, group_size, my_index)
        output_rows = (residual + down_sum).astype(jnp.bfloat16)
        return lax.ppermute(output_rows[None], "section", shift_pairs(section_count, 1))
    bits = group_size.bit_length() - 1
    rest = down_part.shape[1:]
    state = down_part.reshape((2,) * bits + rest)
    for bit in range(bits):
        axis = bits - 1 - bit
        mine = (my_index >> bit) & 1
        keep = lax.dynamic_index_in_dim(state, mine, axis, keepdims=True)
        send = lax.dynamic_index_in_dim(state, 1 - mine, axis, keepdims=True)
        if bit < bits - 1:
            state = keep + lax.ppermute(send, "site", xor_pairs(group_size, bit))
            continue
        own = keep.reshape(rest) + residual
        forward = [
            (section * group_size + site, ((section + 1) % section_count) * group_size + site)
            for section in range(section_count)
            for site in range(group_size)
        ]
        across = [
            (
                section * group_size + site,
                ((section + 1) % section_count) * group_size + (site ^ (1 << bit)),
            )
            for section in range(section_count)
            for site in range(group_size)
        ]
        mine_part = lax.ppermute(own, ("section", "site"), forward)
        other_part = lax.ppermute(send.reshape(rest), ("section", "site"), across)
        output_rows = (mine_part + other_part).astype(jnp.bfloat16)
    return output_rows[None]


def ffn_block(rows_ref, gate_a, gate_b, up_a, up_b, down_a, down_b, out_ref):
    step = pl.program_id(0)

    @pl.when(step == 0)
    def _():
        out_ref[...] = jnp.zeros_like(out_ref)

    half = gate_a.shape[1]
    rows_a = rows_ref[:, :half]
    rows_b = rows_ref[:, half:]
    dims = (((1,), (1,)), ((), ()))
    gate_sum = lax.dot_general(rows_a, gate_a[...], dims, preferred_element_type=jnp.float32)
    gate_sum += lax.dot_general(rows_b, gate_b[...], dims, preferred_element_type=jnp.float32)
    up_sum = lax.dot_general(rows_a, up_a[...], dims, preferred_element_type=jnp.float32)
    up_sum += lax.dot_general(rows_b, up_b[...], dims, preferred_element_type=jnp.float32)
    hidden = (gate_sum * jax.nn.sigmoid(gate_sum) * up_sum).astype(jnp.bfloat16)
    out_ref[:, :half] += jnp.dot(hidden, down_a[...], preferred_element_type=jnp.float32)
    out_ref[:, half:] += jnp.dot(hidden, down_b[...], preferred_element_type=jnp.float32)


def gated_ffn(rows, gate, up, down):
    units, width = gate.shape
    block = 128 if units % 128 == 0 else units
    half = width // 2
    count = rows.shape[0]
    first = pl.BlockSpec((block, half), lambda i: (i, 0))
    second = pl.BlockSpec((block, half), lambda i: (i, 1))
    return pl.pallas_call(
        ffn_block,
        grid=(units // block,),
        in_specs=[pl.BlockSpec((count, width), lambda i: (0, 0)), first, second, first, second, first, second],
        out_specs=pl.BlockSpec((count, width), lambda i: (0, 0)),
        out_shape=jax.ShapeDtypeStruct((count, width), jnp.float32),
        compiler_params=pltpu.CompilerParams(dimension_semantics=("arbitrary",)),
    )(rows, gate, gate, up, up, down, down)


def heads_split(
    acts,
    patches,
    site_tiles,
    site_count,
    q_weight,
    q_gain,
    k_gain,
    tile_in,
    tile_out,
    out_weight,
    ffn_gain,
    gate_weight,
    up_weight,
    down_weight,
):
    group_size = lax.axis_size("site")
    section_count = lax.axis_size("section")
    my_index = lax.axis_index("site")
    sites_here = acts.shape[1]
    list_width = site_tiles.shape[1]
    tiles_here = patches.shape[1]
    head_size = q_gain.shape[1]
    heads_here = HEADS // group_size
    current = acts[0]
    model_width = current.shape[-1]
    hidden_width = tile_in.shape[-1]
    all_sites = group_size * sites_here

    act_rows = sites_here * model_width // hidden_width
    ring_in = RingGather(
        jnp.concatenate([tile_in[0], current.reshape(act_rows, hidden_width)], axis=0),
        group_size,
        my_index,
    )
    in_slots, in_sources = ring_in.finish()
    in_rows = tile_in.shape[1]
    kv_width = tile_out.shape[-1]
    my_cols = heads_here * head_size
    col_blocks = tile_out[0].reshape(tile_out.shape[1], 2, group_size, my_cols)
    col_blocks = jnp.transpose(col_blocks, (2, 0, 1, 3)).reshape(group_size, tile_out.shape[1], 2 * my_cols)
    in_slots, col_blocks = lax.optimization_barrier((in_slots, col_blocks))
    weight_out = lax.all_to_all(col_blocks, "site", split_axis=0, concat_axis=0, tiled=True)
    weight_out = weight_out.reshape(-1, 2 * my_cols)
    del kv_width

    everyone = (
        in_slots[:, in_rows:]
        .at[ring_in.slot_of_source]
        .get(mode="promise_in_bounds")
        .reshape(all_sites, model_width)
    )
    weight_in = in_slots[:, :in_rows].reshape(-1, hidden_width)
    own_rows = (
        patches[0].reshape(tiles_here, group_size, -1).at[:, in_sources].get(mode="promise_in_bounds")
    )
    tile_hidden = jax.nn.gelu(
        jnp.dot(own_rows.reshape(tiles_here, -1), weight_in, preferred_element_type=jnp.float32),
        approximate=True,
    ).astype(jnp.bfloat16)

    q_part = by_rows(everyone, q_weight[0]).astype(jnp.bfloat16)
    queries = head_norm(q_part, q_gain[0]).astype(jnp.bfloat16)
    query_heads = queries.reshape(all_sites, heads_here, head_size)

    ring_hidden = RingGather(tile_hidden, group_size, my_index)
    site_tiles, site_count = ring_hidden.step((site_tiles, site_count))
    hidden_slots, hidden_sources = ring_hidden.finish()
    table_hidden = hidden_slots.reshape(group_size * tiles_here, hidden_width)
    keyval = jnp.dot(table_hidden, weight_out, preferred_element_type=jnp.float32)
    normed_keys = head_norm(keyval[:, :my_cols], k_gain[0])
    table = jnp.concatenate([normed_keys, keyval[:, my_cols:]], axis=1).astype(jnp.bfloat16)
    table = table.reshape(group_size * tiles_here, 2, heads_here, head_size)

    tile_of_row = (
        hidden_sources[:, None] * tiles_here + jnp.arange(tiles_here, dtype=jnp.int32)[None, :]
    ).reshape(-1)
    slot_index = jnp.arange(list_width, dtype=jnp.int32)
    live = slot_index[None, :] < site_count[:, None]
    named = jnp.logical_and(
        site_tiles[:, :, None] == tile_of_row[None, None, :], live[:, :, None]
    )
    uses = jnp.sum(named.astype(jnp.float32), axis=1)
    scores = jnp.einsum(
        "nhd,rhd->nhr", query_heads, table[:, 0], preferred_element_type=jnp.float32
    ) / math.sqrt(head_size)
    exponents = jnp.exp(scores) * uses[:, None, :]
    weights = (exponents / jnp.sum(exponents, axis=-1, keepdims=True)).astype(jnp.bfloat16)
    combined = jnp.einsum(
        "nhr,rhd->nhd", weights, table[:, 1], preferred_element_type=jnp.float32
    )
    combined = combined.reshape(all_sites, my_cols).astype(jnp.bfloat16)
    attn_part = jnp.dot(combined, out_weight[0], preferred_element_type=jnp.float32)
    attn_all = doubling_sum(attn_part.reshape(group_size, sites_here, -1), group_size)
    residual_all = everyone.reshape(group_size, sites_here, -1).astype(jnp.float32) + attn_all
    residual = lax.dynamic_index_in_dim(residual_all, my_index, 0, keepdims=False)
    normed_rows = rms_norm(residual_all, ffn_gain[0]).astype(jnp.bfloat16).reshape(-1, model_width)
    down_part = gated_ffn(normed_rows, gate_weight[0], up_weight[0], down_weight[0])
    down_part = down_part.reshape(group_size, sites_here, -1)
    return last_round(down_part, residual, group_size, section_count, my_index)


def last_round(down_part, residual, group_size, section_count, my_index):
    bits = group_size.bit_length() - 1
    rest = down_part.shape[1:]
    state = down_part.reshape((2,) * bits + rest)
    for bit in range(bits):
        axis = bits - 1 - bit
        mine = (my_index >> bit) & 1
        keep = lax.dynamic_index_in_dim(state, mine, axis, keepdims=True)
        send = lax.dynamic_index_in_dim(state, 1 - mine, axis, keepdims=True)
        if bit < bits - 1:
            state = keep + lax.ppermute(send, "site", xor_pairs(group_size, bit))
            continue
        own = keep.reshape(rest) + residual
        forward = [
            (section * group_size + site, ((section + 1) % section_count) * group_size + site)
            for section in range(section_count)
            for site in range(group_size)
        ]
        across = [
            (
                section * group_size + site,
                ((section + 1) % section_count) * group_size + (site ^ (1 << bit)),
            )
            for section in range(section_count)
            for site in range(group_size)
        ]
        mine_part = lax.ppermute(own, ("section", "site"), forward)
        other_part = lax.ppermute(send.reshape(rest), ("section", "site"), across)
        return (mine_part + other_part).astype(jnp.bfloat16)[None]


def solution(mesh):
    group_size = mesh.shape["site"]
    split_heads = (
        direct_ok(group_size)
        and group_size > 1
        and HEADS % group_size == 0
        and mesh.shape["section"] > 0
    )
    return jax.shard_map(
        heads_split if split_heads else shards,
        mesh=mesh,
        in_specs=(
            P("section", "site", None),
            P("section", "site", None),
            P(),
            P(),
            P("section", "site", None),
            P("section", None),
            P("section", None),
            P("section", "site", None),
            P("section", "site", None),
            P("section", "site", None),
            P("section", None),
            P("section", "site", None),
            P("section", "site", None),
            P("section", "site", None),
        ),
        out_specs=P("section", "site", None),
        check_vma=False,
    )
```

```python
import math

import jax
import jax.numpy as jnp
from jax import lax
from jax.experimental import pallas as pl
from jax.experimental.pallas import tpu as pltpu
from jax.sharding import PartitionSpec as P

HEADS = 16


epsilon = 1e-05

DIRECT_LIMIT = 8


def shift_pairs(count, steps):
    return [(source, (source + steps) % count) for source in range(count)]


def by_rows(left, weight_rows):
    return lax.dot_general(
        left, weight_rows, (((1,), (1,)), ((), ())), preferred_element_type=jnp.float32
    )


def head_norm(values, gain_row):
    shaped = values.astype(jnp.float32).reshape(values.shape[0], -1, gain_row.shape[0])
    scaled = (
        shaped * lax.rsqrt(jnp.mean(shaped * shaped, axis=-1, keepdims=True) + epsilon) * gain_row
    )
    return scaled.reshape(values.shape[0], -1)


def rms_norm(values, gain_row):
    return (
        values * lax.rsqrt(jnp.mean(values * values, axis=-1, keepdims=True) + epsilon) * gain_row
    )


def to_source_order(slots, count, me):
    return jnp.take(slots, (me - jnp.arange(count, dtype=jnp.int32)) % count, axis=0)


def xor_pairs(count, bit):
    return [(source, source ^ (1 << bit)) for source in range(count)]


def direct_ok(count):
    return count <= DIRECT_LIMIT and count & (count - 1) == 0


def site_exchange(by_target, count, me):
    if not direct_ok(count):
        return lax.all_to_all(by_target, "site", split_axis=0, concat_axis=0, tiled=True)
    slots = [lax.dynamic_index_in_dim(by_target, me, 0, keepdims=False)]
    for steps in range(1, count):
        piece = lax.dynamic_index_in_dim(by_target, (me + steps) % count, 0, keepdims=False)
        slots.append(lax.ppermute(piece, "site", shift_pairs(count, steps)))
    return to_source_order(jnp.stack(slots), count, me)


def halving_exchange(by_target, count, me):
    if not direct_ok(count):
        return lax.all_to_all(by_target, "site", split_axis=0, concat_axis=0, tiled=True)
    bits = count.bit_length() - 1
    rest = by_target.shape[1:]
    state = by_target.reshape((2,) * bits + rest)
    for bit in range(bits):
        axis = bits - 1 - bit
        mine = (me >> bit) & 1
        keep = lax.dynamic_index_in_dim(state, mine, axis, keepdims=True)
        send = lax.dynamic_index_in_dim(state, 1 - mine, axis, keepdims=True)
        recv = lax.ppermute(send, "site", xor_pairs(count, bit))
        state = jnp.where(
            mine == 0,
            jnp.concatenate([keep, recv], axis),
            jnp.concatenate([recv, keep], axis),
        )
    return state.reshape((count,) + rest)


def doubling_gather(value, count, me):
    if not direct_ok(count):
        return lax.all_gather(value, "site", axis=0, tiled=False)
    bits = count.bit_length() - 1
    state = value[None]
    for bit in range(bits):
        recv = lax.ppermute(state, "site", xor_pairs(count, bit))
        mine = (me >> bit) & 1
        state = jnp.where(
            mine == 0, jnp.concatenate([state, recv], 0), jnp.concatenate([recv, state], 0)
        )
    return state


def halving_sum(parts, count, me):
    if not direct_ok(count):
        return lax.psum_scatter(parts, "site", scatter_dimension=0, tiled=True)[0]
    bits = count.bit_length() - 1
    rest = parts.shape[1:]
    state = parts.reshape((2,) * bits + rest)
    for bit in range(bits):
        axis = bits - 1 - bit
        mine = (me >> bit) & 1
        keep = lax.dynamic_index_in_dim(state, mine, axis, keepdims=True)
        send = lax.dynamic_index_in_dim(state, 1 - mine, axis, keepdims=True)
        state = keep + lax.ppermute(send, "site", xor_pairs(count, bit))
    return state.reshape(rest)


def doubling_sum(parts, count):
    state = parts
    for bit in range(count.bit_length() - 1):
        state = state + lax.ppermute(state, "site", xor_pairs(count, bit))
    return state


class RingGather:
    def __init__(self, value, count, me):
        self.count = count
        self.direct = direct_ok(count)
        if not self.direct:
            self.slots = lax.all_gather(value, "site", axis=0, tiled=False)
            self.sources = jnp.arange(count, dtype=jnp.int32)
            self.slot_of_source = self.sources
            return
        order = list(range(0, count, 2)) + [i for i in range(count - 1, -1, -1) if i % 2 == 1]
        place = [0] * count
        for position, device in enumerate(order):
            place[device] = position
        self.forward = [(order[p], order[(p + 1) % count]) for p in range(count)]
        self.backward = [(order[p], order[(p - 1) % count]) for p in range(count)]
        self.forward_left = count // 2
        self.backward_left = count - 1 - self.forward_left
        offsets = [0] + [count - s for s in range(1, self.forward_left + 1)]
        offsets += list(range(1, self.backward_left + 1))
        half = count // 2
        my_place = jnp.where(me % 2 == 0, me // 2, count - 1 - me // 2)
        place_of_slot = (my_place + jnp.array(offsets, dtype=jnp.int32)) % count
        self.sources = jnp.where(
            place_of_slot < half, 2 * place_of_slot, 2 * (count - 1 - place_of_slot) + 1
        )
        devices = jnp.arange(count, dtype=jnp.int32)
        their_place = jnp.where(devices % 2 == 0, devices // 2, count - 1 - devices // 2)
        delta = (their_place - my_place) % count
        forward_count = self.forward_left
        self.slot_of_source = jnp.where(
            delta == 0,
            0,
            jnp.where(delta >= count - forward_count, count - delta, forward_count + delta),
        )
        self.forward_slots = []
        self.backward_slots = []
        self.ahead = value
        self.behind = value
        self.value = value
        self._issue()

    def _issue(self):
        if self.forward_left > 0:
            self.ahead = lax.ppermute(self.ahead, "site", self.forward)
            self.forward_slots.append(self.ahead)
            self.forward_left -= 1
        if self.backward_left > 0:
            self.behind = lax.ppermute(self.behind, "site", self.backward)
            self.backward_slots.append(self.behind)
            self.backward_left -= 1

    def step(self, tied):
        if not self.direct or (self.forward_left == 0 and self.backward_left == 0):
            return tied
        self.ahead, self.behind, tied = lax.optimization_barrier((self.ahead, self.behind, tied))
        self.forward_slots[-1] = self.ahead
        if self.backward_slots:
            self.backward_slots[-1] = self.behind
        self._issue()
        return tied

    def slots_in_arrival(self):
        if not self.direct:
            return [self.slots[i] for i in range(self.count)], [self.sources[i] for i in range(self.count)]
        while self.forward_left > 0 or self.backward_left > 0:
            self._issue()
        slots = [self.value]
        positions = [0]
        forward_count = len(self.forward_slots)
        for step in range(max(forward_count, len(self.backward_slots))):
            if step < forward_count:
                slots.append(self.forward_slots[step])
                positions.append(1 + step)
            if step < len(self.backward_slots):
                slots.append(self.backward_slots[step])
                positions.append(1 + forward_count + step)
        return slots, [self.sources[p] for p in positions]

    def finish(self):
        if not self.direct:
            return self.slots, self.sources
        while self.forward_left > 0 or self.backward_left > 0:
            self._issue()
        slots = [self.value] + self.forward_slots + self.backward_slots
        return jnp.stack(slots), self.sources


def shards(
    acts,
    patches,
    site_tiles,
    site_count,
    q_weight,
    q_gain,
    k_gain,
    tile_in,
    tile_out,
    out_weight,
    ffn_gain,
    gate_weight,
    up_weight,
    down_weight,
):
    group_size = lax.axis_size("site")
    section_count = lax.axis_size("section")
    my_index = lax.axis_index("site")
    sites_here = acts.shape[1]
    list_width = site_tiles.shape[1]
    tiles_here = patches.shape[1]
    head_size = q_gain.shape[1]
    capacity = max(2, 5 * sites_here * list_width // (4 * group_size))
    entries = sites_here * list_width
    current = acts[0]
    model_width = current.shape[-1]
    row_width = patches.shape[-1]

    ring_in = RingGather(tile_in[0], group_size, my_index)
    in_slots, in_sources = ring_in.finish()
    ring_out = RingGather(tile_out[0], group_size, my_index)
    weight_in = in_slots.reshape(-1, in_slots.shape[-1])
    own_rows = jnp.take(patches[0].reshape(tiles_here, group_size, -1), in_sources, axis=1)
    tile_hidden = jax.nn.gelu(
        jnp.dot(own_rows.reshape(tiles_here, -1), weight_in, preferred_element_type=jnp.float32),
        approximate=True,
    ).astype(jnp.bfloat16)
    hidden_width = tile_hidden.shape[-1]

    slot_index = jnp.arange(list_width, dtype=jnp.int32)
    live_all = (slot_index[None, :] < site_count[:, None]).reshape(group_size, entries)
    owner_all = (site_tiles // tiles_here).reshape(group_size, entries)
    local_all = (site_tiles % tiles_here).reshape(group_size, entries)
    mine_mask = jnp.logical_and(live_all, owner_all == my_index)
    slot_rank = jnp.cumsum(mine_mask.astype(jnp.int32), axis=1) - 1
    picks = jnp.logical_and(
        mine_mask[:, :, None],
        slot_rank[:, :, None] == jnp.arange(capacity, dtype=jnp.int32)[None, None, :],
    )
    send_index = jnp.sum(jnp.where(picks, local_all[:, :, None], 0), axis=1)
    send_rows = tile_hidden[send_index.reshape(-1)].reshape(group_size, capacity, hidden_width)
    act_rows = sites_here * model_width // hidden_width
    packed = model_width % hidden_width == 0
    if packed:
        act_block = jnp.broadcast_to(
            current.reshape(1, act_rows, hidden_width), (group_size, act_rows, hidden_width)
        )
        send_rows = jnp.concatenate([send_rows, act_block], axis=1)
    send_rows = ring_out.step(send_rows)
    arrived = lax.all_to_all(send_rows, "site", split_axis=0, concat_axis=0, tiled=True)
    if packed:
        everyone = arrived[:, capacity:].reshape(-1, model_width)
        arrived = arrived[:, :capacity]
    else:
        everyone = doubling_gather(current, group_size, my_index).reshape(-1, model_width)
    q_part = by_rows(everyone, q_weight[0]).astype(jnp.bfloat16)
    q_part = ring_out.step(q_part)
    q_blocks = halving_exchange(
        q_part.reshape(group_size, sites_here, -1), group_size, my_index
    )
    q_blocks = ring_out.step(q_blocks)

    my_tiles = lax.dynamic_slice_in_dim(site_tiles, my_index * sites_here, sites_here, 0)
    my_count = lax.dynamic_slice_in_dim(site_count, my_index * sites_here, sites_here, 0)
    my_live = slot_index[None, :] < my_count[:, None]
    my_owner = (my_tiles // tiles_here).reshape(-1)
    one_hot = jnp.logical_and(
        my_owner[:, None] == jnp.arange(group_size, dtype=jnp.int32)[None, :],
        my_live.reshape(-1)[:, None],
    ).astype(jnp.int32)
    my_rank = jnp.sum(jnp.cumsum(one_hot, axis=0) * one_hot, axis=1) - 1
    fetch_index = jnp.where(my_live.reshape(-1), my_owner * capacity + my_rank, 0)
    pair_hidden = arrived.reshape(group_size * capacity, hidden_width)[fetch_index]

    shard_rows = tile_out.shape[1]
    keyval = None
    if not ring_out.direct:
        out_slots, out_sources = [ring_out.slots.reshape(-1, ring_out.slots.shape[-1])], [0]
        shard_rows = hidden_width
    else:
        out_slots, out_sources = ring_out.slots_in_arrival()
    for slot, source in zip(out_slots, out_sources):
        columns_here = lax.dynamic_slice_in_dim(pair_hidden, source * shard_rows, shard_rows, 1)
        term = jnp.dot(columns_here, slot, preferred_element_type=jnp.float32)
        keyval = term if keyval is None else keyval + term
    half_width = keyval.shape[1] // 2
    normed_keys = head_norm(keyval[:, :half_width], k_gain[0])
    pair_kv = jnp.concatenate([normed_keys, keyval[:, half_width:]], axis=1).astype(jnp.bfloat16)
    pair_kv = pair_kv.reshape(sites_here, list_width, 2, HEADS, head_size)

    my_queries = jnp.moveaxis(q_blocks, 0, 1).reshape(sites_here, -1)
    queries = head_norm(my_queries, q_gain[0]).astype(jnp.bfloat16)
    query_heads = queries.reshape(sites_here, HEADS, head_size)
    scores = jnp.einsum(
        "nhd,nlhd->nhl", query_heads, pair_kv[:, :, 0], preferred_element_type=jnp.float32
    ) / math.sqrt(head_size)
    exponents = jnp.exp(scores) * my_live.astype(jnp.float32)[:, None, :]
    weights = (exponents / jnp.sum(exponents, axis=-1, keepdims=True)).astype(jnp.bfloat16)
    combined = jnp.einsum(
        "nhl,nlhd->nhd", weights, pair_kv[:, :, 1], preferred_element_type=jnp.float32
    )
    combined = combined.reshape(sites_here, -1).astype(jnp.bfloat16)
    column_blocks = jnp.moveaxis(combined.reshape(sites_here, group_size, -1), 1, 0)
    columns = halving_exchange(column_blocks, group_size, my_index).reshape(
        group_size * sites_here, -1
    )
    attn_part = jnp.dot(columns, out_weight[0], preferred_element_type=jnp.float32)
    attn_part = attn_part.reshape(group_size, sites_here, -1)
    if direct_ok(group_size):
        attn_all = doubling_sum(attn_part, group_size)
        residual_all = everyone.reshape(group_size, sites_here, -1).astype(jnp.float32) + attn_all
        residual = lax.dynamic_index_in_dim(residual_all, my_index, 0, keepdims=False)
        normed_rows = rms_norm(residual_all, ffn_gain[0]).astype(jnp.bfloat16)
        normed_rows = normed_rows.reshape(-1, model_width)
    else:
        attn_sum = halving_sum(attn_part, group_size, my_index)
        residual = current.astype(jnp.float32) + attn_sum
        normed = rms_norm(residual, ffn_gain[0]).astype(jnp.bfloat16)
        normed_rows = doubling_gather(normed, group_size, my_index).reshape(-1, model_width)
    gate_sum = by_rows(normed_rows, gate_weight[0])
    up_sum = by_rows(normed_rows, up_weight[0])
    hidden_ffn = (jax.nn.silu(gate_sum) * up_sum).astype(jnp.bfloat16)
    down_part = jnp.dot(hidden_ffn, down_weight[0], preferred_element_type=jnp.float32)
    down_part = down_part.reshape(group_size, sites_here, -1)
    if not direct_ok(group_size) or group_size == 1:
        down_sum = halving_sum(down_part, group_size, my_index)
        output_rows = (residual + down_sum).astype(jnp.bfloat16)
        return lax.ppermute(output_rows[None], "section", shift_pairs(section_count, 1))
    bits = group_size.bit_length() - 1
    rest = down_part.shape[1:]
    state = down_part.reshape((2,) * bits + rest)
    for bit in range(bits):
        axis = bits - 1 - bit
        mine = (my_index >> bit) & 1
        keep = lax.dynamic_index_in_dim(state, mine, axis, keepdims=True)
        send = lax.dynamic_index_in_dim(state, 1 - mine, axis, keepdims=True)
        if bit < bits - 1:
            state = keep + lax.ppermute(send, "site", xor_pairs(group_size, bit))
            continue
        own = keep.reshape(rest) + residual
        forward = [
            (section * group_size + site, ((section + 1) % section_count) * group_size + site)
            for section in range(section_count)
            for site in range(group_size)
        ]
        across = [
            (
                section * group_size + site,
                ((section + 1) % section_count) * group_size + (site ^ (1 << bit)),
            )
            for section in range(section_count)
            for site in range(group_size)
        ]
        mine_part = lax.ppermute(own, ("section", "site"), forward)
        other_part = lax.ppermute(send.reshape(rest), ("section", "site"), across)
        output_rows = (mine_part + other_part).astype(jnp.bfloat16)
    return output_rows[None]


def ffn_block(acts_ref, attn_ref, gain_ref, gate_a, gate_b, up_a, up_b, down_a, down_b, out_ref, rows_ref):
    step = pl.program_id(0)

    @pl.when(step == 0)
    def _():
        out_ref[...] = jnp.zeros_like(out_ref)
        residual = acts_ref[...].astype(jnp.float32) + attn_ref[...]
        rows_ref[...] = rms_norm(residual, gain_ref[...]).astype(rows_ref.dtype)

    half = gate_a.shape[1]
    rows_a = rows_ref[:, :half]
    rows_b = rows_ref[:, half:]
    dims = (((1,), (1,)), ((), ()))
    gate_sum = lax.dot_general(rows_a, gate_a[...], dims, preferred_element_type=jnp.float32)
    gate_sum += lax.dot_general(rows_b, gate_b[...], dims, preferred_element_type=jnp.float32)
    up_sum = lax.dot_general(rows_a, up_a[...], dims, preferred_element_type=jnp.float32)
    up_sum += lax.dot_general(rows_b, up_b[...], dims, preferred_element_type=jnp.float32)
    hidden = (gate_sum * jax.nn.sigmoid(gate_sum) * up_sum).astype(jnp.bfloat16)
    out_ref[:, :half] += jnp.dot(hidden, down_a[...], preferred_element_type=jnp.float32)
    out_ref[:, half:] += jnp.dot(hidden, down_b[...], preferred_element_type=jnp.float32)


def gated_ffn(acts_rows, attn_rows, gain, gate, up, down):
    units, width = gate.shape
    block = 128 if units % 128 == 0 else units
    half = width // 2
    count = acts_rows.shape[0]
    whole = pl.BlockSpec((count, width), lambda i: (0, 0))
    first = pl.BlockSpec((block, half), lambda i: (i, 0))
    second = pl.BlockSpec((block, half), lambda i: (i, 1))
    return pl.pallas_call(
        ffn_block,
        grid=(units // block,),
        in_specs=[
            whole,
            whole,
            pl.BlockSpec((1, width), lambda i: (0, 0)),
            first,
            second,
            first,
            second,
            first,
            second,
        ],
        out_specs=whole,
        out_shape=jax.ShapeDtypeStruct((count, width), jnp.float32),
        scratch_shapes=[pltpu.VMEM((count, width), jnp.bfloat16)],
        compiler_params=pltpu.CompilerParams(dimension_semantics=("arbitrary",)),
    )(acts_rows, attn_rows, gain.reshape(1, width), gate, gate, up, up, down, down)


def heads_split(
    acts,
    patches,
    site_tiles,
    site_count,
    q_weight,
    q_gain,
    k_gain,
    tile_in,
    tile_out,
    out_weight,
    ffn_gain,
    gate_weight,
    up_weight,
    down_weight,
):
    group_size = lax.axis_size("site")
    section_count = lax.axis_size("section")
    my_index = lax.axis_index("site")
    sites_here = acts.shape[1]
    list_width = site_tiles.shape[1]
    tiles_here = patches.shape[1]
    head_size = q_gain.shape[1]
    heads_here = HEADS // group_size
    current = acts[0]
    model_width = current.shape[-1]
    hidden_width = tile_in.shape[-1]
    all_sites = group_size * sites_here

    act_rows = sites_here * model_width // hidden_width
    ring_in = RingGather(
        jnp.concatenate([tile_in[0], current.reshape(act_rows, hidden_width)], axis=0),
        group_size,
        my_index,
    )
    in_slots, in_sources = ring_in.finish()
    in_rows = tile_in.shape[1]
    kv_width = tile_out.shape[-1]
    my_cols = heads_here * head_size
    col_blocks = tile_out[0].reshape(tile_out.shape[1], 2, group_size, my_cols)
    col_blocks = jnp.transpose(col_blocks, (2, 0, 1, 3)).reshape(group_size, tile_out.shape[1], 2 * my_cols)
    in_slots, col_blocks = lax.optimization_barrier((in_slots, col_blocks))
    weight_out = lax.all_to_all(col_blocks, "site", split_axis=0, concat_axis=0, tiled=True)
    weight_out = weight_out.reshape(-1, 2 * my_cols)
    del kv_width

    everyone = (
        in_slots[:, in_rows:]
        .at[ring_in.slot_of_source]
        .get(mode="promise_in_bounds")
        .reshape(all_sites, model_width)
    )
    weight_in = in_slots[:, :in_rows].reshape(-1, hidden_width)
    own_rows = (
        patches[0].reshape(tiles_here, group_size, -1).at[:, in_sources].get(mode="promise_in_bounds")
    )
    tile_hidden = jax.nn.gelu(
        jnp.dot(own_rows.reshape(tiles_here, -1), weight_in, preferred_element_type=jnp.float32),
        approximate=True,
    ).astype(jnp.bfloat16)

    q_part = by_rows(everyone, q_weight[0]).astype(jnp.bfloat16)
    queries = head_norm(q_part, q_gain[0]).astype(jnp.bfloat16)
    query_heads = queries.reshape(all_sites, heads_here, head_size)

    ring_hidden = RingGather(tile_hidden, group_size, my_index)
    site_tiles, site_count = ring_hidden.step((site_tiles, site_count))
    hidden_slots, hidden_sources = ring_hidden.finish()
    table_hidden = hidden_slots.reshape(group_size * tiles_here, hidden_width)
    keyval = jnp.dot(table_hidden, weight_out, preferred_element_type=jnp.float32)
    normed_keys = head_norm(keyval[:, :my_cols], k_gain[0])
    table = jnp.concatenate([normed_keys, keyval[:, my_cols:]], axis=1).astype(jnp.bfloat16)
    table = table.reshape(group_size * tiles_here, 2, heads_here, head_size)

    tile_of_row = (
        hidden_sources[:, None] * tiles_here + jnp.arange(tiles_here, dtype=jnp.int32)[None, :]
    ).reshape(-1)
    slot_index = jnp.arange(list_width, dtype=jnp.int32)
    live = slot_index[None, :] < site_count[:, None]
    named = jnp.logical_and(
        site_tiles[:, :, None] == tile_of_row[None, None, :], live[:, :, None]
    )
    uses = jnp.sum(named.astype(jnp.float32), axis=1)
    scores = jnp.einsum(
        "nhd,rhd->nhr", query_heads, table[:, 0], preferred_element_type=jnp.float32
    ) / math.sqrt(head_size)
    exponents = jnp.exp(scores) * uses[:, None, :]
    weights = (exponents / jnp.sum(exponents, axis=-1, keepdims=True)).astype(jnp.bfloat16)
    combined = jnp.einsum(
        "nhr,rhd->nhd", weights, table[:, 1], preferred_element_type=jnp.float32
    )
    combined = combined.reshape(all_sites, my_cols).astype(jnp.bfloat16)
    attn_part = jnp.dot(combined, out_weight[0], preferred_element_type=jnp.float32)
    attn_all = doubling_sum(attn_part.reshape(group_size, sites_here, -1), group_size)
    residual_all = everyone.reshape(group_size, sites_here, -1).astype(jnp.float32) + attn_all
    residual = lax.dynamic_index_in_dim(residual_all, my_index, 0, keepdims=False)
    down_part = gated_ffn(
        everyone,
        attn_all.reshape(-1, model_width),
        ffn_gain[0],
        gate_weight[0],
        up_weight[0],
        down_weight[0],
    )
    down_part = down_part.reshape(group_size, sites_here, -1)
    return last_round(down_part, residual, group_size, section_count, my_index)


def last_round(down_part, residual, group_size, section_count, my_index):
    bits = group_size.bit_length() - 1
    rest = down_part.shape[1:]
    state = down_part.reshape((2,) * bits + rest)
    for bit in range(bits):
        axis = bits - 1 - bit
        mine = (my_index >> bit) & 1
        keep = lax.dynamic_index_in_dim(state, mine, axis, keepdims=True)
        send = lax.dynamic_index_in_dim(state, 1 - mine, axis, keepdims=True)
        if bit < bits - 1:
            state = keep + lax.ppermute(send, "site", xor_pairs(group_size, bit))
            continue
        own = keep.reshape(rest) + residual
        forward = [
            (section * group_size + site, ((section + 1) % section_count) * group_size + site)
            for section in range(section_count)
            for site in range(group_size)
        ]
        across = [
            (
                section * group_size + site,
                ((section + 1) % section_count) * group_size + (site ^ (1 << bit)),
            )
            for section in range(section_count)
            for site in range(group_size)
        ]
        mine_part = lax.ppermute(own, ("section", "site"), forward)
        other_part = lax.ppermute(send.reshape(rest), ("section", "site"), across)
        return (mine_part + other_part).astype(jnp.bfloat16)[None]


def solution(mesh):
    group_size = mesh.shape["site"]
    split_heads = (
        direct_ok(group_size)
        and group_size > 1
        and HEADS % group_size == 0
        and mesh.shape["section"] > 0
    )
    return jax.shard_map(
        heads_split if split_heads else shards,
        mesh=mesh,
        in_specs=(
            P("section", "site", None),
            P("section", "site", None),
            P(),
            P(),
            P("section", "site", None),
            P("section", None),
            P("section", None),
            P("section", "site", None),
            P("section", "site", None),
            P("section", "site", None),
            P("section", None),
            P("section", "site", None),
            P("section", "site", None),
            P("section", "site", None),
        ),
        out_specs=P("section", "site", None),
        check_vma=False,
    )
```

```python
import math

import jax
import jax.numpy as jnp
from jax import lax
from jax.experimental import pallas as pl
from jax.experimental.pallas import tpu as pltpu
from jax.sharding import PartitionSpec as P

HEADS = 16


epsilon = 1e-05

DIRECT_LIMIT = 8


def shift_pairs(count, steps):
    return [(source, (source + steps) % count) for source in range(count)]


def by_rows(left, weight_rows):
    return lax.dot_general(
        left, weight_rows, (((1,), (1,)), ((), ())), preferred_element_type=jnp.float32
    )


def head_norm(values, gain_row):
    shaped = values.astype(jnp.float32).reshape(values.shape[0], -1, gain_row.shape[0])
    scaled = (
        shaped * lax.rsqrt(jnp.mean(shaped * shaped, axis=-1, keepdims=True) + epsilon) * gain_row
    )
    return scaled.reshape(values.shape[0], -1)


def rms_norm(values, gain_row):
    return (
        values * lax.rsqrt(jnp.mean(values * values, axis=-1, keepdims=True) + epsilon) * gain_row
    )


def to_source_order(slots, count, me):
    return jnp.take(slots, (me - jnp.arange(count, dtype=jnp.int32)) % count, axis=0)


def xor_pairs(count, bit):
    return [(source, source ^ (1 << bit)) for source in range(count)]


def direct_ok(count):
    return count <= DIRECT_LIMIT and count & (count - 1) == 0


def site_exchange(by_target, count, me):
    if not direct_ok(count):
        return lax.all_to_all(by_target, "site", split_axis=0, concat_axis=0, tiled=True)
    slots = [lax.dynamic_index_in_dim(by_target, me, 0, keepdims=False)]
    for steps in range(1, count):
        piece = lax.dynamic_index_in_dim(by_target, (me + steps) % count, 0, keepdims=False)
        slots.append(lax.ppermute(piece, "site", shift_pairs(count, steps)))
    return to_source_order(jnp.stack(slots), count, me)


def halving_exchange(by_target, count, me):
    if not direct_ok(count):
        return lax.all_to_all(by_target, "site", split_axis=0, concat_axis=0, tiled=True)
    bits = count.bit_length() - 1
    rest = by_target.shape[1:]
    state = by_target.reshape((2,) * bits + rest)
    for bit in range(bits):
        axis = bits - 1 - bit
        mine = (me >> bit) & 1
        keep = lax.dynamic_index_in_dim(state, mine, axis, keepdims=True)
        send = lax.dynamic_index_in_dim(state, 1 - mine, axis, keepdims=True)
        recv = lax.ppermute(send, "site", xor_pairs(count, bit))
        state = jnp.where(
            mine == 0,
            jnp.concatenate([keep, recv], axis),
            jnp.concatenate([recv, keep], axis),
        )
    return state.reshape((count,) + rest)


def doubling_gather(value, count, me):
    if not direct_ok(count):
        return lax.all_gather(value, "site", axis=0, tiled=False)
    bits = count.bit_length() - 1
    state = value[None]
    for bit in range(bits):
        recv = lax.ppermute(state, "site", xor_pairs(count, bit))
        mine = (me >> bit) & 1
        state = jnp.where(
            mine == 0, jnp.concatenate([state, recv], 0), jnp.concatenate([recv, state], 0)
        )
    return state


def halving_sum(parts, count, me):
    if not direct_ok(count):
        return lax.psum_scatter(parts, "site", scatter_dimension=0, tiled=True)[0]
    bits = count.bit_length() - 1
    rest = parts.shape[1:]
    state = parts.reshape((2,) * bits + rest)
    for bit in range(bits):
        axis = bits - 1 - bit
        mine = (me >> bit) & 1
        keep = lax.dynamic_index_in_dim(state, mine, axis, keepdims=True)
        send = lax.dynamic_index_in_dim(state, 1 - mine, axis, keepdims=True)
        state = keep + lax.ppermute(send, "site", xor_pairs(count, bit))
    return state.reshape(rest)


def doubling_sum(parts, count):
    state = parts
    for bit in range(count.bit_length() - 1):
        state = state + lax.ppermute(state, "site", xor_pairs(count, bit))
    return state


class RingGather:
    def __init__(self, value, count, me):
        self.count = count
        self.direct = direct_ok(count)
        if not self.direct:
            self.slots = lax.all_gather(value, "site", axis=0, tiled=False)
            self.sources = jnp.arange(count, dtype=jnp.int32)
            self.slot_of_source = self.sources
            return
        order = list(range(0, count, 2)) + [i for i in range(count - 1, -1, -1) if i % 2 == 1]
        place = [0] * count
        for position, device in enumerate(order):
            place[device] = position
        self.forward = [(order[p], order[(p + 1) % count]) for p in range(count)]
        self.backward = [(order[p], order[(p - 1) % count]) for p in range(count)]
        self.forward_left = count // 2
        self.backward_left = count - 1 - self.forward_left
        offsets = [0] + [count - s for s in range(1, self.forward_left + 1)]
        offsets += list(range(1, self.backward_left + 1))
        half = count // 2
        my_place = jnp.where(me % 2 == 0, me // 2, count - 1 - me // 2)
        place_of_slot = (my_place + jnp.array(offsets, dtype=jnp.int32)) % count
        self.sources = jnp.where(
            place_of_slot < half, 2 * place_of_slot, 2 * (count - 1 - place_of_slot) + 1
        )
        devices = jnp.arange(count, dtype=jnp.int32)
        their_place = jnp.where(devices % 2 == 0, devices // 2, count - 1 - devices // 2)
        delta = (their_place - my_place) % count
        forward_count = self.forward_left
        self.slot_of_source = jnp.where(
            delta == 0,
            0,
            jnp.where(delta >= count - forward_count, count - delta, forward_count + delta),
        )
        self.forward_slots = []
        self.backward_slots = []
        self.ahead = value
        self.behind = value
        self.value = value
        self._issue()

    def _issue(self):
        if self.forward_left > 0:
            self.ahead = lax.ppermute(self.ahead, "site", self.forward)
            self.forward_slots.append(self.ahead)
            self.forward_left -= 1
        if self.backward_left > 0:
            self.behind = lax.ppermute(self.behind, "site", self.backward)
            self.backward_slots.append(self.behind)
            self.backward_left -= 1

    def step(self, tied):
        if not self.direct or (self.forward_left == 0 and self.backward_left == 0):
            return tied
        self.ahead, self.behind, tied = lax.optimization_barrier((self.ahead, self.behind, tied))
        self.forward_slots[-1] = self.ahead
        if self.backward_slots:
            self.backward_slots[-1] = self.behind
        self._issue()
        return tied

    def slots_in_arrival(self):
        if not self.direct:
            return [self.slots[i] for i in range(self.count)], [self.sources[i] for i in range(self.count)]
        while self.forward_left > 0 or self.backward_left > 0:
            self._issue()
        slots = [self.value]
        positions = [0]
        forward_count = len(self.forward_slots)
        for step in range(max(forward_count, len(self.backward_slots))):
            if step < forward_count:
                slots.append(self.forward_slots[step])
                positions.append(1 + step)
            if step < len(self.backward_slots):
                slots.append(self.backward_slots[step])
                positions.append(1 + forward_count + step)
        return slots, [self.sources[p] for p in positions]

    def finish(self):
        if not self.direct:
            return self.slots, self.sources
        while self.forward_left > 0 or self.backward_left > 0:
            self._issue()
        slots = [self.value] + self.forward_slots + self.backward_slots
        return jnp.stack(slots), self.sources


def shards(
    acts,
    patches,
    site_tiles,
    site_count,
    q_weight,
    q_gain,
    k_gain,
    tile_in,
    tile_out,
    out_weight,
    ffn_gain,
    gate_weight,
    up_weight,
    down_weight,
):
    group_size = lax.axis_size("site")
    section_count = lax.axis_size("section")
    my_index = lax.axis_index("site")
    sites_here = acts.shape[1]
    list_width = site_tiles.shape[1]
    tiles_here = patches.shape[1]
    head_size = q_gain.shape[1]
    capacity = max(2, 5 * sites_here * list_width // (4 * group_size))
    entries = sites_here * list_width
    current = acts[0]
    model_width = current.shape[-1]
    row_width = patches.shape[-1]

    ring_in = RingGather(tile_in[0], group_size, my_index)
    in_slots, in_sources = ring_in.finish()
    ring_out = RingGather(tile_out[0], group_size, my_index)
    weight_in = in_slots.reshape(-1, in_slots.shape[-1])
    own_rows = jnp.take(patches[0].reshape(tiles_here, group_size, -1), in_sources, axis=1)
    tile_hidden = jax.nn.gelu(
        jnp.dot(own_rows.reshape(tiles_here, -1), weight_in, preferred_element_type=jnp.float32),
        approximate=True,
    ).astype(jnp.bfloat16)
    hidden_width = tile_hidden.shape[-1]

    slot_index = jnp.arange(list_width, dtype=jnp.int32)
    live_all = (slot_index[None, :] < site_count[:, None]).reshape(group_size, entries)
    owner_all = (site_tiles // tiles_here).reshape(group_size, entries)
    local_all = (site_tiles % tiles_here).reshape(group_size, entries)
    mine_mask = jnp.logical_and(live_all, owner_all == my_index)
    slot_rank = jnp.cumsum(mine_mask.astype(jnp.int32), axis=1) - 1
    picks = jnp.logical_and(
        mine_mask[:, :, None],
        slot_rank[:, :, None] == jnp.arange(capacity, dtype=jnp.int32)[None, None, :],
    )
    send_index = jnp.sum(jnp.where(picks, local_all[:, :, None], 0), axis=1)
    send_rows = tile_hidden[send_index.reshape(-1)].reshape(group_size, capacity, hidden_width)
    act_rows = sites_here * model_width // hidden_width
    packed = model_width % hidden_width == 0
    if packed:
        act_block = jnp.broadcast_to(
            current.reshape(1, act_rows, hidden_width), (group_size, act_rows, hidden_width)
        )
        send_rows = jnp.concatenate([send_rows, act_block], axis=1)
    send_rows = ring_out.step(send_rows)
    arrived = lax.all_to_all(send_rows, "site", split_axis=0, concat_axis=0, tiled=True)
    if packed:
        everyone = arrived[:, capacity:].reshape(-1, model_width)
        arrived = arrived[:, :capacity]
    else:
        everyone = doubling_gather(current, group_size, my_index).reshape(-1, model_width)
    q_part = by_rows(everyone, q_weight[0]).astype(jnp.bfloat16)
    q_part = ring_out.step(q_part)
    q_blocks = halving_exchange(
        q_part.reshape(group_size, sites_here, -1), group_size, my_index
    )
    q_blocks = ring_out.step(q_blocks)

    my_tiles = lax.dynamic_slice_in_dim(site_tiles, my_index * sites_here, sites_here, 0)
    my_count = lax.dynamic_slice_in_dim(site_count, my_index * sites_here, sites_here, 0)
    my_live = slot_index[None, :] < my_count[:, None]
    my_owner = (my_tiles // tiles_here).reshape(-1)
    one_hot = jnp.logical_and(
        my_owner[:, None] == jnp.arange(group_size, dtype=jnp.int32)[None, :],
        my_live.reshape(-1)[:, None],
    ).astype(jnp.int32)
    my_rank = jnp.sum(jnp.cumsum(one_hot, axis=0) * one_hot, axis=1) - 1
    fetch_index = jnp.where(my_live.reshape(-1), my_owner * capacity + my_rank, 0)
    pair_hidden = arrived.reshape(group_size * capacity, hidden_width)[fetch_index]

    shard_rows = tile_out.shape[1]
    keyval = None
    if not ring_out.direct:
        out_slots, out_sources = [ring_out.slots.reshape(-1, ring_out.slots.shape[-1])], [0]
        shard_rows = hidden_width
    else:
        out_slots, out_sources = ring_out.slots_in_arrival()
    for slot, source in zip(out_slots, out_sources):
        columns_here = lax.dynamic_slice_in_dim(pair_hidden, source * shard_rows, shard_rows, 1)
        term = jnp.dot(columns_here, slot, preferred_element_type=jnp.float32)
        keyval = term if keyval is None else keyval + term
    half_width = keyval.shape[1] // 2
    normed_keys = head_norm(keyval[:, :half_width], k_gain[0])
    pair_kv = jnp.concatenate([normed_keys, keyval[:, half_width:]], axis=1).astype(jnp.bfloat16)
    pair_kv = pair_kv.reshape(sites_here, list_width, 2, HEADS, head_size)

    my_queries = jnp.moveaxis(q_blocks, 0, 1).reshape(sites_here, -1)
    queries = head_norm(my_queries, q_gain[0]).astype(jnp.bfloat16)
    query_heads = queries.reshape(sites_here, HEADS, head_size)
    scores = jnp.einsum(
        "nhd,nlhd->nhl", query_heads, pair_kv[:, :, 0], preferred_element_type=jnp.float32
    ) / math.sqrt(head_size)
    exponents = jnp.exp(scores) * my_live.astype(jnp.float32)[:, None, :]
    weights = (exponents / jnp.sum(exponents, axis=-1, keepdims=True)).astype(jnp.bfloat16)
    combined = jnp.einsum(
        "nhl,nlhd->nhd", weights, pair_kv[:, :, 1], preferred_element_type=jnp.float32
    )
    combined = combined.reshape(sites_here, -1).astype(jnp.bfloat16)
    column_blocks = jnp.moveaxis(combined.reshape(sites_here, group_size, -1), 1, 0)
    columns = halving_exchange(column_blocks, group_size, my_index).reshape(
        group_size * sites_here, -1
    )
    attn_part = jnp.dot(columns, out_weight[0], preferred_element_type=jnp.float32)
    attn_part = attn_part.reshape(group_size, sites_here, -1)
    if direct_ok(group_size):
        attn_all = doubling_sum(attn_part, group_size)
        residual_all = everyone.reshape(group_size, sites_here, -1).astype(jnp.float32) + attn_all
        residual = lax.dynamic_index_in_dim(residual_all, my_index, 0, keepdims=False)
        normed_rows = rms_norm(residual_all, ffn_gain[0]).astype(jnp.bfloat16)
        normed_rows = normed_rows.reshape(-1, model_width)
    else:
        attn_sum = halving_sum(attn_part, group_size, my_index)
        residual = current.astype(jnp.float32) + attn_sum
        normed = rms_norm(residual, ffn_gain[0]).astype(jnp.bfloat16)
        normed_rows = doubling_gather(normed, group_size, my_index).reshape(-1, model_width)
    gate_sum = by_rows(normed_rows, gate_weight[0])
    up_sum = by_rows(normed_rows, up_weight[0])
    hidden_ffn = (jax.nn.silu(gate_sum) * up_sum).astype(jnp.bfloat16)
    down_part = jnp.dot(hidden_ffn, down_weight[0], preferred_element_type=jnp.float32)
    down_part = down_part.reshape(group_size, sites_here, -1)
    if not direct_ok(group_size) or group_size == 1:
        down_sum = halving_sum(down_part, group_size, my_index)
        output_rows = (residual + down_sum).astype(jnp.bfloat16)
        return lax.ppermute(output_rows[None], "section", shift_pairs(section_count, 1))
    bits = group_size.bit_length() - 1
    rest = down_part.shape[1:]
    state = down_part.reshape((2,) * bits + rest)
    for bit in range(bits):
        axis = bits - 1 - bit
        mine = (my_index >> bit) & 1
        keep = lax.dynamic_index_in_dim(state, mine, axis, keepdims=True)
        send = lax.dynamic_index_in_dim(state, 1 - mine, axis, keepdims=True)
        if bit < bits - 1:
            state = keep + lax.ppermute(send, "site", xor_pairs(group_size, bit))
            continue
        own = keep.reshape(rest) + residual
        forward = [
            (section * group_size + site, ((section + 1) % section_count) * group_size + site)
            for section in range(section_count)
            for site in range(group_size)
        ]
        across = [
            (
                section * group_size + site,
                ((section + 1) % section_count) * group_size + (site ^ (1 << bit)),
            )
            for section in range(section_count)
            for site in range(group_size)
        ]
        mine_part = lax.ppermute(own, ("section", "site"), forward)
        other_part = lax.ppermute(send.reshape(rest), ("section", "site"), across)
        output_rows = (mine_part + other_part).astype(jnp.bfloat16)
    return output_rows[None]


def ffn_block(acts_ref, attn_ref, gain_ref, gate_a, gate_b, up_a, up_b, down_a, down_b, out_ref, rows_ref):
    step = pl.program_id(0)

    @pl.when(step == 0)
    def _():
        out_ref[...] = jnp.zeros_like(out_ref)
        residual = acts_ref[...].astype(jnp.float32) + attn_ref[...]
        rows_ref[...] = rms_norm(residual, gain_ref[...]).astype(rows_ref.dtype)

    half = gate_a.shape[1]
    rows_a = rows_ref[:, :half]
    rows_b = rows_ref[:, half:]
    dims = (((1,), (1,)), ((), ()))
    gate_sum = lax.dot_general(rows_a, gate_a[...], dims, preferred_element_type=jnp.float32)
    gate_sum += lax.dot_general(rows_b, gate_b[...], dims, preferred_element_type=jnp.float32)
    up_sum = lax.dot_general(rows_a, up_a[...], dims, preferred_element_type=jnp.float32)
    up_sum += lax.dot_general(rows_b, up_b[...], dims, preferred_element_type=jnp.float32)
    hidden = (gate_sum * jax.nn.sigmoid(gate_sum) * up_sum).astype(jnp.bfloat16)
    out_ref[:, :half] += jnp.dot(hidden, down_a[...], preferred_element_type=jnp.float32)
    out_ref[:, half:] += jnp.dot(hidden, down_b[...], preferred_element_type=jnp.float32)


def gated_ffn(acts_rows, attn_rows, gain, gate, up, down):
    units, width = gate.shape
    block = 128 if units % 128 == 0 else units
    half = width // 2
    count = acts_rows.shape[0]
    whole = pl.BlockSpec((count, width), lambda i: (0, 0))
    first = pl.BlockSpec((block, half), lambda i: (i, 0))
    second = pl.BlockSpec((block, half), lambda i: (i, 1))
    return pl.pallas_call(
        ffn_block,
        grid=(units // block,),
        in_specs=[
            whole,
            whole,
            pl.BlockSpec((1, width), lambda i: (0, 0)),
            first,
            second,
            first,
            second,
            first,
            second,
        ],
        out_specs=whole,
        out_shape=jax.ShapeDtypeStruct((count, width), jnp.float32),
        scratch_shapes=[pltpu.VMEM((count, width), jnp.bfloat16)],
        compiler_params=pltpu.CompilerParams(dimension_semantics=("arbitrary",)),
    )(acts_rows, attn_rows, gain.reshape(1, width), gate, gate, up, up, down, down)


def heads_split(
    acts,
    patches,
    site_tiles,
    site_count,
    q_weight,
    q_gain,
    k_gain,
    tile_in,
    tile_out,
    out_weight,
    ffn_gain,
    gate_weight,
    up_weight,
    down_weight,
):
    group_size = lax.axis_size("site")
    section_count = lax.axis_size("section")
    my_index = lax.axis_index("site")
    sites_here = acts.shape[1]
    list_width = site_tiles.shape[1]
    tiles_here = patches.shape[1]
    head_size = q_gain.shape[1]
    heads_here = HEADS // group_size
    current = acts[0]
    model_width = current.shape[-1]
    hidden_width = tile_in.shape[-1]
    all_sites = group_size * sites_here

    act_rows = sites_here * model_width // hidden_width
    ring_in = RingGather(
        jnp.concatenate([tile_in[0], current.reshape(act_rows, hidden_width)], axis=0),
        group_size,
        my_index,
    )
    in_slots, in_sources = ring_in.finish()
    in_rows = tile_in.shape[1]
    kv_width = tile_out.shape[-1]
    my_cols = heads_here * head_size
    col_blocks = tile_out[0].reshape(tile_out.shape[1], 2, group_size, my_cols)
    col_blocks = jnp.transpose(col_blocks, (2, 0, 1, 3)).reshape(group_size, tile_out.shape[1], 2 * my_cols)
    in_slots, col_blocks = lax.optimization_barrier((in_slots, col_blocks))
    weight_out = lax.all_to_all(col_blocks, "site", split_axis=0, concat_axis=0, tiled=True)
    weight_out = weight_out.reshape(-1, 2 * my_cols)
    del kv_width

    everyone = (
        in_slots[:, in_rows:]
        .at[ring_in.slot_of_source]
        .get(mode="promise_in_bounds")
        .reshape(all_sites, model_width)
    )
    weight_in = in_slots[:, :in_rows].reshape(-1, hidden_width)
    own_rows = (
        patches[0].reshape(tiles_here, group_size, -1).at[:, in_sources].get(mode="promise_in_bounds")
    )
    tile_hidden = jax.nn.gelu(
        jnp.dot(own_rows.reshape(tiles_here, -1), weight_in, preferred_element_type=jnp.float32),
        approximate=True,
    ).astype(jnp.bfloat16)

    q_part = by_rows(everyone, q_weight[0]).astype(jnp.bfloat16)
    queries = head_norm(q_part, q_gain[0]).astype(jnp.bfloat16)
    query_heads = queries.reshape(all_sites, heads_here, head_size)

    ring_hidden = RingGather(tile_hidden, group_size, my_index)
    site_tiles, site_count = ring_hidden.step((site_tiles, site_count))
    hidden_slots, hidden_sources = ring_hidden.finish()
    if ring_hidden.direct and ring_hidden.forward_slots:
        last = len(ring_hidden.forward_slots)
        early = [ring_hidden.value] + ring_hidden.forward_slots[:-1] + ring_hidden.backward_slots
        parts = [jnp.stack(early), ring_hidden.forward_slots[-1][None]]
        order = [i for i in range(group_size) if i != last] + [last]
        hidden_sources = jnp.stack([hidden_sources[i] for i in order])
    else:
        parts = [hidden_slots]
    tables = []
    for part in parts:
        keyval = jnp.dot(
            part.reshape(-1, hidden_width), weight_out, preferred_element_type=jnp.float32
        )
        normed_keys = head_norm(keyval[:, :my_cols], k_gain[0])
        tables.append(
            jnp.concatenate([normed_keys, keyval[:, my_cols:]], axis=1)
            .astype(jnp.bfloat16)
            .reshape(-1, 2, heads_here, head_size)
        )

    tile_of_row = (
        hidden_sources[:, None] * tiles_here + jnp.arange(tiles_here, dtype=jnp.int32)[None, :]
    ).reshape(-1)
    slot_index = jnp.arange(list_width, dtype=jnp.int32)
    live = slot_index[None, :] < site_count[:, None]
    named = jnp.logical_and(
        site_tiles[:, :, None] == tile_of_row[None, None, :], live[:, :, None]
    )
    uses = jnp.sum(named.astype(jnp.float32), axis=1)
    scores = jnp.concatenate(
        [
            jnp.einsum("nhd,rhd->nhr", query_heads, table[:, 0], preferred_element_type=jnp.float32)
            for table in tables
        ],
        axis=-1,
    ) / math.sqrt(head_size)
    exponents = jnp.exp(scores) * uses[:, None, :]
    weights = (exponents / jnp.sum(exponents, axis=-1, keepdims=True)).astype(jnp.bfloat16)
    combined = None
    start = 0
    for table in tables:
        rows_here = table.shape[0]
        term = jnp.einsum(
            "nhr,rhd->nhd",
            weights[:, :, start : start + rows_here],
            table[:, 1],
            preferred_element_type=jnp.float32,
        )
        combined = term if combined is None else combined + term
        start += rows_here
    combined = combined.reshape(all_sites, my_cols).astype(jnp.bfloat16)
    attn_part = jnp.dot(combined, out_weight[0], preferred_element_type=jnp.float32)
    attn_all = doubling_sum(attn_part.reshape(group_size, sites_here, -1), group_size)
    residual_all = everyone.reshape(group_size, sites_here, -1).astype(jnp.float32) + attn_all
    residual = lax.dynamic_index_in_dim(residual_all, my_index, 0, keepdims=False)
    down_part = gated_ffn(
        everyone,
        attn_all.reshape(-1, model_width),
        ffn_gain[0],
        gate_weight[0],
        up_weight[0],
        down_weight[0],
    )
    down_part = down_part.reshape(group_size, sites_here, -1)
    return last_round(down_part, residual, group_size, section_count, my_index)


def last_round(down_part, residual, group_size, section_count, my_index):
    bits = group_size.bit_length() - 1
    rest = down_part.shape[1:]
    state = down_part.reshape((2,) * bits + rest)
    for bit in range(bits):
        axis = bits - 1 - bit
        mine = (my_index >> bit) & 1
        keep = lax.dynamic_index_in_dim(state, mine, axis, keepdims=True)
        send = lax.dynamic_index_in_dim(state, 1 - mine, axis, keepdims=True)
        if bit < bits - 1:
            state = keep + lax.ppermute(send, "site", xor_pairs(group_size, bit))
            continue
        own = keep.reshape(rest) + residual
        forward = [
            (section * group_size + site, ((section + 1) % section_count) * group_size + site)
            for section in range(section_count)
            for site in range(group_size)
        ]
        across = [
            (
                section * group_size + site,
                ((section + 1) % section_count) * group_size + (site ^ (1 << bit)),
            )
            for section in range(section_count)
            for site in range(group_size)
        ]
        mine_part = lax.ppermute(own, ("section", "site"), forward)
        other_part = lax.ppermute(send.reshape(rest), ("section", "site"), across)
        return (mine_part + other_part).astype(jnp.bfloat16)[None]


def solution(mesh):
    group_size = mesh.shape["site"]
    split_heads = (
        direct_ok(group_size)
        and group_size > 1
        and HEADS % group_size == 0
        and mesh.shape["section"] > 0
    )
    return jax.shard_map(
        heads_split if split_heads else shards,
        mesh=mesh,
        in_specs=(
            P("section", "site", None),
            P("section", "site", None),
            P(),
            P(),
            P("section", "site", None),
            P("section", None),
            P("section", None),
            P("section", "site", None),
            P("section", "site", None),
            P("section", "site", None),
            P("section", None),
            P("section", "site", None),
            P("section", "site", None),
            P("section", "site", None),
        ),
        out_specs=P("section", "site", None),
        check_vma=False,
    )
```

```python
import math

import jax
import jax.numpy as jnp
from jax import lax
from jax.experimental import pallas as pl
from jax.experimental.pallas import tpu as pltpu
from jax.sharding import PartitionSpec as P

HEADS = 16


epsilon = 1e-05

DIRECT_LIMIT = 8


def shift_pairs(count, steps):
    return [(source, (source + steps) % count) for source in range(count)]


def by_rows(left, weight_rows):
    return lax.dot_general(
        left, weight_rows, (((1,), (1,)), ((), ())), preferred_element_type=jnp.float32
    )


def head_norm(values, gain_row):
    shaped = values.astype(jnp.float32).reshape(values.shape[0], -1, gain_row.shape[0])
    scaled = (
        shaped * lax.rsqrt(jnp.mean(shaped * shaped, axis=-1, keepdims=True) + epsilon) * gain_row
    )
    return scaled.reshape(values.shape[0], -1)


def rms_norm(values, gain_row):
    return (
        values * lax.rsqrt(jnp.mean(values * values, axis=-1, keepdims=True) + epsilon) * gain_row
    )


def to_source_order(slots, count, me):
    return jnp.take(slots, (me - jnp.arange(count, dtype=jnp.int32)) % count, axis=0)


def xor_pairs(count, bit):
    return [(source, source ^ (1 << bit)) for source in range(count)]


def direct_ok(count):
    return count <= DIRECT_LIMIT and count & (count - 1) == 0


def site_exchange(by_target, count, me):
    if not direct_ok(count):
        return lax.all_to_all(by_target, "site", split_axis=0, concat_axis=0, tiled=True)
    slots = [lax.dynamic_index_in_dim(by_target, me, 0, keepdims=False)]
    for steps in range(1, count):
        piece = lax.dynamic_index_in_dim(by_target, (me + steps) % count, 0, keepdims=False)
        slots.append(lax.ppermute(piece, "site", shift_pairs(count, steps)))
    return to_source_order(jnp.stack(slots), count, me)


def halving_exchange(by_target, count, me):
    if not direct_ok(count):
        return lax.all_to_all(by_target, "site", split_axis=0, concat_axis=0, tiled=True)
    bits = count.bit_length() - 1
    rest = by_target.shape[1:]
    state = by_target.reshape((2,) * bits + rest)
    for bit in range(bits):
        axis = bits - 1 - bit
        mine = (me >> bit) & 1
        keep = lax.dynamic_index_in_dim(state, mine, axis, keepdims=True)
        send = lax.dynamic_index_in_dim(state, 1 - mine, axis, keepdims=True)
        recv = lax.ppermute(send, "site", xor_pairs(count, bit))
        state = jnp.where(
            mine == 0,
            jnp.concatenate([keep, recv], axis),
            jnp.concatenate([recv, keep], axis),
        )
    return state.reshape((count,) + rest)


def doubling_gather(value, count, me):
    if not direct_ok(count):
        return lax.all_gather(value, "site", axis=0, tiled=False)
    bits = count.bit_length() - 1
    state = value[None]
    for bit in range(bits):
        recv = lax.ppermute(state, "site", xor_pairs(count, bit))
        mine = (me >> bit) & 1
        state = jnp.where(
            mine == 0, jnp.concatenate([state, recv], 0), jnp.concatenate([recv, state], 0)
        )
    return state


def halving_sum(parts, count, me):
    if not direct_ok(count):
        return lax.psum_scatter(parts, "site", scatter_dimension=0, tiled=True)[0]
    bits = count.bit_length() - 1
    rest = parts.shape[1:]
    state = parts.reshape((2,) * bits + rest)
    for bit in range(bits):
        axis = bits - 1 - bit
        mine = (me >> bit) & 1
        keep = lax.dynamic_index_in_dim(state, mine, axis, keepdims=True)
        send = lax.dynamic_index_in_dim(state, 1 - mine, axis, keepdims=True)
        state = keep + lax.ppermute(send, "site", xor_pairs(count, bit))
    return state.reshape(rest)


def doubling_sum(parts, count):
    state = parts
    for bit in range(count.bit_length() - 1):
        state = state + lax.ppermute(state, "site", xor_pairs(count, bit))
    return state


class RingGather:
    def __init__(self, value, count, me):
        self.count = count
        self.direct = direct_ok(count)
        if not self.direct:
            self.slots = lax.all_gather(value, "site", axis=0, tiled=False)
            self.sources = jnp.arange(count, dtype=jnp.int32)
            self.slot_of_source = self.sources
            return
        order = list(range(0, count, 2)) + [i for i in range(count - 1, -1, -1) if i % 2 == 1]
        place = [0] * count
        for position, device in enumerate(order):
            place[device] = position
        self.forward = [(order[p], order[(p + 1) % count]) for p in range(count)]
        self.backward = [(order[p], order[(p - 1) % count]) for p in range(count)]
        self.forward_left = count // 2
        self.backward_left = count - 1 - self.forward_left
        offsets = [0] + [count - s for s in range(1, self.forward_left + 1)]
        offsets += list(range(1, self.backward_left + 1))
        half = count // 2
        my_place = jnp.where(me % 2 == 0, me // 2, count - 1 - me // 2)
        place_of_slot = (my_place + jnp.array(offsets, dtype=jnp.int32)) % count
        self.sources = jnp.where(
            place_of_slot < half, 2 * place_of_slot, 2 * (count - 1 - place_of_slot) + 1
        )
        devices = jnp.arange(count, dtype=jnp.int32)
        their_place = jnp.where(devices % 2 == 0, devices // 2, count - 1 - devices // 2)
        delta = (their_place - my_place) % count
        forward_count = self.forward_left
        self.slot_of_source = jnp.where(
            delta == 0,
            0,
            jnp.where(delta >= count - forward_count, count - delta, forward_count + delta),
        )
        self.forward_slots = []
        self.backward_slots = []
        self.ahead = value
        self.behind = value
        self.value = value
        self._issue()

    def _issue(self):
        if self.forward_left > 0:
            self.ahead = lax.ppermute(self.ahead, "site", self.forward)
            self.forward_slots.append(self.ahead)
            self.forward_left -= 1
        if self.backward_left > 0:
            self.behind = lax.ppermute(self.behind, "site", self.backward)
            self.backward_slots.append(self.behind)
            self.backward_left -= 1

    def step(self, tied):
        if not self.direct or (self.forward_left == 0 and self.backward_left == 0):
            return tied
        self.ahead, self.behind, tied = lax.optimization_barrier((self.ahead, self.behind, tied))
        self.forward_slots[-1] = self.ahead
        if self.backward_slots:
            self.backward_slots[-1] = self.behind
        self._issue()
        return tied

    def slots_in_arrival(self):
        if not self.direct:
            return [self.slots[i] for i in range(self.count)], [self.sources[i] for i in range(self.count)]
        while self.forward_left > 0 or self.backward_left > 0:
            self._issue()
        slots = [self.value]
        positions = [0]
        forward_count = len(self.forward_slots)
        for step in range(max(forward_count, len(self.backward_slots))):
            if step < forward_count:
                slots.append(self.forward_slots[step])
                positions.append(1 + step)
            if step < len(self.backward_slots):
                slots.append(self.backward_slots[step])
                positions.append(1 + forward_count + step)
        return slots, [self.sources[p] for p in positions]

    def finish(self):
        if not self.direct:
            return self.slots, self.sources
        while self.forward_left > 0 or self.backward_left > 0:
            self._issue()
        slots = [self.value] + self.forward_slots + self.backward_slots
        return jnp.stack(slots), self.sources


def shards(
    acts,
    patches,
    site_tiles,
    site_count,
    q_weight,
    q_gain,
    k_gain,
    tile_in,
    tile_out,
    out_weight,
    ffn_gain,
    gate_weight,
    up_weight,
    down_weight,
):
    group_size = lax.axis_size("site")
    section_count = lax.axis_size("section")
    my_index = lax.axis_index("site")
    sites_here = acts.shape[1]
    list_width = site_tiles.shape[1]
    tiles_here = patches.shape[1]
    head_size = q_gain.shape[1]
    capacity = max(2, 5 * sites_here * list_width // (4 * group_size))
    entries = sites_here * list_width
    current = acts[0]
    model_width = current.shape[-1]
    row_width = patches.shape[-1]

    ring_in = RingGather(tile_in[0], group_size, my_index)
    in_slots, in_sources = ring_in.finish()
    ring_out = RingGather(tile_out[0], group_size, my_index)
    weight_in = in_slots.reshape(-1, in_slots.shape[-1])
    own_rows = jnp.take(patches[0].reshape(tiles_here, group_size, -1), in_sources, axis=1)
    tile_hidden = jax.nn.gelu(
        jnp.dot(own_rows.reshape(tiles_here, -1), weight_in, preferred_element_type=jnp.float32),
        approximate=True,
    ).astype(jnp.bfloat16)
    hidden_width = tile_hidden.shape[-1]

    slot_index = jnp.arange(list_width, dtype=jnp.int32)
    live_all = (slot_index[None, :] < site_count[:, None]).reshape(group_size, entries)
    owner_all = (site_tiles // tiles_here).reshape(group_size, entries)
    local_all = (site_tiles % tiles_here).reshape(group_size, entries)
    mine_mask = jnp.logical_and(live_all, owner_all == my_index)
    slot_rank = jnp.cumsum(mine_mask.astype(jnp.int32), axis=1) - 1
    picks = jnp.logical_and(
        mine_mask[:, :, None],
        slot_rank[:, :, None] == jnp.arange(capacity, dtype=jnp.int32)[None, None, :],
    )
    send_index = jnp.sum(jnp.where(picks, local_all[:, :, None], 0), axis=1)
    send_rows = tile_hidden[send_index.reshape(-1)].reshape(group_size, capacity, hidden_width)
    act_rows = sites_here * model_width // hidden_width
    packed = model_width % hidden_width == 0
    if packed:
        act_block = jnp.broadcast_to(
            current.reshape(1, act_rows, hidden_width), (group_size, act_rows, hidden_width)
        )
        send_rows = jnp.concatenate([send_rows, act_block], axis=1)
    send_rows = ring_out.step(send_rows)
    arrived = lax.all_to_all(send_rows, "site", split_axis=0, concat_axis=0, tiled=True)
    if packed:
        everyone = arrived[:, capacity:].reshape(-1, model_width)
        arrived = arrived[:, :capacity]
    else:
        everyone = doubling_gather(current, group_size, my_index).reshape(-1, model_width)
    q_part = by_rows(everyone, q_weight[0]).astype(jnp.bfloat16)
    q_part = ring_out.step(q_part)
    q_blocks = halving_exchange(
        q_part.reshape(group_size, sites_here, -1), group_size, my_index
    )
    q_blocks = ring_out.step(q_blocks)

    my_tiles = lax.dynamic_slice_in_dim(site_tiles, my_index * sites_here, sites_here, 0)
    my_count = lax.dynamic_slice_in_dim(site_count, my_index * sites_here, sites_here, 0)
    my_live = slot_index[None, :] < my_count[:, None]
    my_owner = (my_tiles // tiles_here).reshape(-1)
    one_hot = jnp.logical_and(
        my_owner[:, None] == jnp.arange(group_size, dtype=jnp.int32)[None, :],
        my_live.reshape(-1)[:, None],
    ).astype(jnp.int32)
    my_rank = jnp.sum(jnp.cumsum(one_hot, axis=0) * one_hot, axis=1) - 1
    fetch_index = jnp.where(my_live.reshape(-1), my_owner * capacity + my_rank, 0)
    pair_hidden = arrived.reshape(group_size * capacity, hidden_width)[fetch_index]

    shard_rows = tile_out.shape[1]
    keyval = None
    if not ring_out.direct:
        out_slots, out_sources = [ring_out.slots.reshape(-1, ring_out.slots.shape[-1])], [0]
        shard_rows = hidden_width
    else:
        out_slots, out_sources = ring_out.slots_in_arrival()
    for slot, source in zip(out_slots, out_sources):
        columns_here = lax.dynamic_slice_in_dim(pair_hidden, source * shard_rows, shard_rows, 1)
        term = jnp.dot(columns_here, slot, preferred_element_type=jnp.float32)
        keyval = term if keyval is None else keyval + term
    half_width = keyval.shape[1] // 2
    normed_keys = head_norm(keyval[:, :half_width], k_gain[0])
    pair_kv = jnp.concatenate([normed_keys, keyval[:, half_width:]], axis=1).astype(jnp.bfloat16)
    pair_kv = pair_kv.reshape(sites_here, list_width, 2, HEADS, head_size)

    my_queries = jnp.moveaxis(q_blocks, 0, 1).reshape(sites_here, -1)
    queries = head_norm(my_queries, q_gain[0]).astype(jnp.bfloat16)
    query_heads = queries.reshape(sites_here, HEADS, head_size)
    scores = jnp.einsum(
        "nhd,nlhd->nhl", query_heads, pair_kv[:, :, 0], preferred_element_type=jnp.float32
    ) / math.sqrt(head_size)
    exponents = jnp.exp(scores) * my_live.astype(jnp.float32)[:, None, :]
    weights = (exponents / jnp.sum(exponents, axis=-1, keepdims=True)).astype(jnp.bfloat16)
    combined = jnp.einsum(
        "nhl,nlhd->nhd", weights, pair_kv[:, :, 1], preferred_element_type=jnp.float32
    )
    combined = combined.reshape(sites_here, -1).astype(jnp.bfloat16)
    column_blocks = jnp.moveaxis(combined.reshape(sites_here, group_size, -1), 1, 0)
    columns = halving_exchange(column_blocks, group_size, my_index).reshape(
        group_size * sites_here, -1
    )
    attn_part = jnp.dot(columns, out_weight[0], preferred_element_type=jnp.float32)
    attn_part = attn_part.reshape(group_size, sites_here, -1)
    if direct_ok(group_size):
        attn_all = doubling_sum(attn_part, group_size)
        residual_all = everyone.reshape(group_size, sites_here, -1).astype(jnp.float32) + attn_all
        residual = lax.dynamic_index_in_dim(residual_all, my_index, 0, keepdims=False)
        normed_rows = rms_norm(residual_all, ffn_gain[0]).astype(jnp.bfloat16)
        normed_rows = normed_rows.reshape(-1, model_width)
    else:
        attn_sum = halving_sum(attn_part, group_size, my_index)
        residual = current.astype(jnp.float32) + attn_sum
        normed = rms_norm(residual, ffn_gain[0]).astype(jnp.bfloat16)
        normed_rows = doubling_gather(normed, group_size, my_index).reshape(-1, model_width)
    gate_sum = by_rows(normed_rows, gate_weight[0])
    up_sum = by_rows(normed_rows, up_weight[0])
    hidden_ffn = (jax.nn.silu(gate_sum) * up_sum).astype(jnp.bfloat16)
    down_part = jnp.dot(hidden_ffn, down_weight[0], preferred_element_type=jnp.float32)
    down_part = down_part.reshape(group_size, sites_here, -1)
    if not direct_ok(group_size) or group_size == 1:
        down_sum = halving_sum(down_part, group_size, my_index)
        output_rows = (residual + down_sum).astype(jnp.bfloat16)
        return lax.ppermute(output_rows[None], "section", shift_pairs(section_count, 1))
    bits = group_size.bit_length() - 1
    rest = down_part.shape[1:]
    state = down_part.reshape((2,) * bits + rest)
    for bit in range(bits):
        axis = bits - 1 - bit
        mine = (my_index >> bit) & 1
        keep = lax.dynamic_index_in_dim(state, mine, axis, keepdims=True)
        send = lax.dynamic_index_in_dim(state, 1 - mine, axis, keepdims=True)
        if bit < bits - 1:
            state = keep + lax.ppermute(send, "site", xor_pairs(group_size, bit))
            continue
        own = keep.reshape(rest) + residual
        forward = [
            (section * group_size + site, ((section + 1) % section_count) * group_size + site)
            for section in range(section_count)
            for site in range(group_size)
        ]
        across = [
            (
                section * group_size + site,
                ((section + 1) % section_count) * group_size + (site ^ (1 << bit)),
            )
            for section in range(section_count)
            for site in range(group_size)
        ]
        mine_part = lax.ppermute(own, ("section", "site"), forward)
        other_part = lax.ppermute(send.reshape(rest), ("section", "site"), across)
        output_rows = (mine_part + other_part).astype(jnp.bfloat16)
    return output_rows[None]


def ffn_block(acts_ref, attn_ref, gain_ref, gate_a, gate_b, up_a, up_b, down_a, down_b, out_ref, rows_ref):
    step = pl.program_id(0)

    @pl.when(step == 0)
    def _():
        out_ref[...] = jnp.zeros_like(out_ref)
        residual = acts_ref[...].astype(jnp.float32) + attn_ref[...]
        rows_ref[...] = rms_norm(residual, gain_ref[...]).astype(rows_ref.dtype)

    half = gate_a.shape[1]
    rows_a = rows_ref[:, :half]
    rows_b = rows_ref[:, half:]
    dims = (((1,), (1,)), ((), ()))
    gate_sum = lax.dot_general(rows_a, gate_a[...], dims, preferred_element_type=jnp.float32)
    gate_sum += lax.dot_general(rows_b, gate_b[...], dims, preferred_element_type=jnp.float32)
    up_sum = lax.dot_general(rows_a, up_a[...], dims, preferred_element_type=jnp.float32)
    up_sum += lax.dot_general(rows_b, up_b[...], dims, preferred_element_type=jnp.float32)
    hidden = (gate_sum * jax.nn.sigmoid(gate_sum) * up_sum).astype(jnp.bfloat16)
    out_ref[:, :half] += jnp.dot(hidden, down_a[...], preferred_element_type=jnp.float32)
    out_ref[:, half:] += jnp.dot(hidden, down_b[...], preferred_element_type=jnp.float32)


def gated_ffn(acts_rows, attn_rows, gain, gate, up, down):
    units, width = gate.shape
    block = 128 if units % 128 == 0 else units
    half = width // 2
    count = acts_rows.shape[0]
    whole = pl.BlockSpec((count, width), lambda i: (0, 0))
    first = pl.BlockSpec((block, half), lambda i: (i, 0))
    second = pl.BlockSpec((block, half), lambda i: (i, 1))
    return pl.pallas_call(
        ffn_block,
        grid=(units // block,),
        in_specs=[
            whole,
            whole,
            pl.BlockSpec((1, width), lambda i: (0, 0)),
            first,
            second,
            first,
            second,
            first,
            second,
        ],
        out_specs=whole,
        out_shape=jax.ShapeDtypeStruct((count, width), jnp.float32),
        scratch_shapes=[pltpu.VMEM((count, width), jnp.bfloat16)],
        compiler_params=pltpu.CompilerParams(dimension_semantics=("arbitrary",)),
    )(acts_rows, attn_rows, gain.reshape(1, width), gate, gate, up, up, down, down)


def heads_split(
    acts,
    patches,
    site_tiles,
    site_count,
    q_weight,
    q_gain,
    k_gain,
    tile_in,
    tile_out,
    out_weight,
    ffn_gain,
    gate_weight,
    up_weight,
    down_weight,
):
    group_size = lax.axis_size("site")
    section_count = lax.axis_size("section")
    my_index = lax.axis_index("site")
    sites_here = acts.shape[1]
    list_width = site_tiles.shape[1]
    tiles_here = patches.shape[1]
    head_size = q_gain.shape[1]
    heads_here = HEADS // group_size
    current = acts[0]
    model_width = current.shape[-1]
    hidden_width = tile_in.shape[-1]
    all_sites = group_size * sites_here

    act_rows = sites_here * model_width // hidden_width
    ring_in = RingGather(
        jnp.concatenate([tile_in[0], current.reshape(act_rows, hidden_width)], axis=0),
        group_size,
        my_index,
    )
    in_slots, in_sources = ring_in.finish()
    in_rows = tile_in.shape[1]
    kv_width = tile_out.shape[-1]
    my_cols = heads_here * head_size
    col_blocks = tile_out[0].reshape(tile_out.shape[1], 2, group_size, my_cols)
    col_blocks = jnp.transpose(col_blocks, (2, 0, 1, 3)).reshape(group_size, tile_out.shape[1], 2 * my_cols)
    del kv_width

    everyone = (
        in_slots[:, in_rows:]
        .at[ring_in.slot_of_source]
        .get(mode="promise_in_bounds")
        .reshape(all_sites, model_width)
    )
    weight_in = in_slots[:, :in_rows].reshape(-1, hidden_width)
    own_rows = (
        patches[0].reshape(tiles_here, group_size, -1).at[:, in_sources].get(mode="promise_in_bounds")
    )
    tile_hidden = jax.nn.gelu(
        jnp.dot(own_rows.reshape(tiles_here, -1), weight_in, preferred_element_type=jnp.float32),
        approximate=True,
    ).astype(jnp.bfloat16)

    q_part = by_rows(everyone, q_weight[0]).astype(jnp.bfloat16)
    queries = head_norm(q_part, q_gain[0]).astype(jnp.bfloat16)
    query_heads = queries.reshape(all_sites, heads_here, head_size)

    ring_hidden = RingGather(tile_hidden, group_size, my_index)
    site_tiles, site_count = ring_hidden.step((site_tiles, site_count))
    col_blocks = ring_hidden.step(col_blocks)
    weight_out = lax.all_to_all(col_blocks, "site", split_axis=0, concat_axis=0, tiled=True)
    weight_out = weight_out.reshape(-1, 2 * my_cols)
    hidden_slots, hidden_sources = ring_hidden.finish()
    table_hidden = hidden_slots.reshape(group_size * tiles_here, hidden_width)
    keyval = jnp.dot(table_hidden, weight_out, preferred_element_type=jnp.float32)
    normed_keys = head_norm(keyval[:, :my_cols], k_gain[0])
    table = jnp.concatenate([normed_keys, keyval[:, my_cols:]], axis=1).astype(jnp.bfloat16)
    table = table.reshape(group_size * tiles_here, 2, heads_here, head_size)

    tile_of_row = (
        hidden_sources[:, None] * tiles_here + jnp.arange(tiles_here, dtype=jnp.int32)[None, :]
    ).reshape(-1)
    slot_index = jnp.arange(list_width, dtype=jnp.int32)
    live = slot_index[None, :] < site_count[:, None]
    named = jnp.logical_and(
        site_tiles[:, :, None] == tile_of_row[None, None, :], live[:, :, None]
    )
    uses = jnp.sum(named.astype(jnp.float32), axis=1)
    scores = jnp.einsum(
        "nhd,rhd->nhr", query_heads, table[:, 0], preferred_element_type=jnp.float32
    ) / math.sqrt(head_size)
    exponents = jnp.exp(scores) * uses[:, None, :]
    weights = (exponents / jnp.sum(exponents, axis=-1, keepdims=True)).astype(jnp.bfloat16)
    combined = jnp.einsum(
        "nhr,rhd->nhd", weights, table[:, 1], preferred_element_type=jnp.float32
    )
    combined = combined.reshape(all_sites, my_cols).astype(jnp.bfloat16)
    attn_part = jnp.dot(combined, out_weight[0], preferred_element_type=jnp.float32)
    attn_all = doubling_sum(attn_part.reshape(group_size, sites_here, -1), group_size)
    residual_all = everyone.reshape(group_size, sites_here, -1).astype(jnp.float32) + attn_all
    residual = lax.dynamic_index_in_dim(residual_all, my_index, 0, keepdims=False)
    down_part = gated_ffn(
        everyone,
        attn_all.reshape(-1, model_width),
        ffn_gain[0],
        gate_weight[0],
        up_weight[0],
        down_weight[0],
    )
    down_part = down_part.reshape(group_size, sites_here, -1)
    return last_round(down_part, residual, group_size, section_count, my_index)


def last_round(down_part, residual, group_size, section_count, my_index):
    bits = group_size.bit_length() - 1
    rest = down_part.shape[1:]
    state = down_part.reshape((2,) * bits + rest)
    for bit in range(bits):
        axis = bits - 1 - bit
        mine = (my_index >> bit) & 1
        keep = lax.dynamic_index_in_dim(state, mine, axis, keepdims=True)
        send = lax.dynamic_index_in_dim(state, 1 - mine, axis, keepdims=True)
        if bit < bits - 1:
            state = keep + lax.ppermute(send, "site", xor_pairs(group_size, bit))
            continue
        own = keep.reshape(rest) + residual
        forward = [
            (section * group_size + site, ((section + 1) % section_count) * group_size + site)
            for section in range(section_count)
            for site in range(group_size)
        ]
        across = [
            (
                section * group_size + site,
                ((section + 1) % section_count) * group_size + (site ^ (1 << bit)),
            )
            for section in range(section_count)
            for site in range(group_size)
        ]
        mine_part = lax.ppermute(own, ("section", "site"), forward)
        other_part = lax.ppermute(send.reshape(rest), ("section", "site"), across)
        return (mine_part + other_part).astype(jnp.bfloat16)[None]


def solution(mesh):
    group_size = mesh.shape["site"]
    split_heads = (
        direct_ok(group_size)
        and group_size > 1
        and HEADS % group_size == 0
        and mesh.shape["section"] > 0
    )
    return jax.shard_map(
        heads_split if split_heads else shards,
        mesh=mesh,
        in_specs=(
            P("section", "site", None),
            P("section", "site", None),
            P(),
            P(),
            P("section", "site", None),
            P("section", None),
            P("section", None),
            P("section", "site", None),
            P("section", "site", None),
            P("section", "site", None),
            P("section", None),
            P("section", "site", None),
            P("section", "site", None),
            P("section", "site", None),
        ),
        out_specs=P("section", "site", None),
        check_vma=False,
    )
```
